128 devices in a mesh: valve: 8 (over y, core), bulk: 16 (over z, x).
Axes of the slice: x: 4, y: 4, z: 4, core: 2. Of those that a mesh axis runs over, the one named last changes fastest.
Arguments:
- solution: float32 [5, 64, 131072], P(None, None, ('valve', 'bulk')), may hold values from -6 to 6
- velocity: float32 [3, 131072], P(None, ('valve', 'bulk')), may hold values from -1 to 1
- inv_jacobian: float32 [64, 131072], P(None, ('valve', 'bulk')), may hold values from 0.5 to 3
- face_speed: float32 [96, 131072], P(None, ('valve', 'bulk')), may hold values from -6 to 6
- face_link: int32 [6, 131072], P(None, ('valve', 'bulk')), may hold values from 0 to 6271, as said below
- donor_elem: int32 [1048576], P(('valve', 'bulk')), may hold values from 0 to 1023
- ref_coords: float32 [3, 1048576], P(None, ('valve', 'bulk')), may hold values from -1 to 1
- owner_list: int32 [1048576, 1], P(('valve', 'bulk')), may hold values from 0 to 15; in each aligned block of 8192 rows (0 to 8191, 8192 to 16383, ...) at most 1024 rows name the same one
Outputs:
- section_rate: float32 [5, 64, 131072], P(None, None, ('valve', 'bulk'))
- fringe_values: float32 [5, 2097152], P(None, ('valve', 'bulk'))
The draws below stay inside these ranges and needn't reach their ends.
Inputs may be any that keep to these rules, and one draw needn't show every extreme that they name: `face_link`: on each device, the values 6 * 1024 to 6271 appear exactly once each; every other face slot links to another slot of the same device that links back to it. `owner_list`: among the receptors of one device no owner is named more than 1024 times; in every draw some device names some owner exactly 1024 times.
All inputs are finite; a program needn't handle non-finite values.
Results may differ from the reference program's by a relative error of at most 0.0003.
Values sent between devices are 32-bit elements; how exact they have to be, the bound alone decides.
No kernel may reach another device: no remote copies, remote signals or barrier semaphores. Data moves between devices by JAX's collectives and lax.ppermute only.
A program may use at most 192 MiB of HBM per device.

```python
import math
import jax
import jax.numpy as jnp
import numpy as np
from jax import lax

NVAR = 5
SOLPTS = 64
FLXPTS = 96
E_DEV = 1024
IFACE = 64
REC_DEV = 8192
CAP = 1024
NEL = 131072
NREC = 1048576
SLOTS = 2097152
N_VALVE = 8
N_BULK = 16
DEVICES = 128


def draw_face_link(key, part):
    faces_total = 6 * E_DEV

    def one_device(device):
        order = jax.random.permutation(jax.random.fold_in(key, device), faces_total).astype(jnp.int32)
        places = jnp.arange(faces_total, dtype=jnp.int32)
        paired = 2 * IFACE + jnp.bitwise_xor(places - 2 * IFACE, 1)
        partner = jnp.take(order, jnp.clip(paired, 0, faces_total - 1))
        values = jnp.where(places < 2 * IFACE, faces_total + places, partner)
        return jnp.zeros((faces_total,), jnp.int32).at[order].set(values).reshape(6, E_DEV)
    stacked = jax.vmap(one_device)(jnp.arange(DEVICES, dtype=jnp.int32))
    return jnp.transpose(stacked, (1, 0, 2)).reshape(6, DEVICES * E_DEV)


def touch_ends(values, rng, low, largest):
    spot = [jax.random.randint(jax.random.fold_in(rng, axis), (), 0, length) for axis, length in enumerate(values.shape)]
    widest = values.shape.index(max(values.shape))
    beside = spot[:widest] + [(spot[widest] + 1) % values.shape[widest]] + spot[widest + 1:]
    return values.at[tuple(spot)].set(low).at[tuple(beside)].set(largest)


def level_of(rng, shape, shards, low, largest):
    gain = 1.0
    for dim, blocks in shards:
        steps = jax.random.uniform(jax.random.fold_in(jax.random.fold_in(rng, 6), dim), (blocks,), jnp.float32, low / len(shards), largest / len(shards))
        gain = gain * jnp.repeat(jnp.exp(steps), shape[dim] // blocks).reshape((-1,) + (1,) * (len(shape) - 1 - dim))
    return gain


def deal_out(own_key, own, number, rows, count, top, reach, skew):
    sequence = jax.random.permutation(own_key, count)
    heavy_load, ordinary = portions_of(count, rows * top, reach, skew, True), portions_of(count, rows * top, reach, skew, False)
    places = jnp.arange(count)

    def named(lengths, rotation):
        used = int((lengths > 0).sum())
        fixed = max(1, used // 4)
        shifted = fixed + (places - fixed + rotation * (used - fixed)) % max(1, count - fixed)
        return jnp.zeros((count,), jnp.int32).at[sequence[jnp.where(places < fixed, places, shifted)]].set(jnp.asarray(lengths, jnp.int32))

    lengths = jnp.where(number % 4 == 0, named(heavy_load, number // 4), named(ordinary, number - number // 4 - 1))
    mixed = jax.random.permutation(jax.random.fold_in(own, 3), count)
    donor, receiver = mixed[0:count // 2 * 2:2], mixed[1:count // 2 * 2:2]
    margin = jnp.minimum(lengths[donor] - 1, reach - lengths[receiver]) // 2
    margin = jnp.where((donor == sequence[0]) | (receiver == sequence[0]) | (lengths[receiver] == 0), 0, jnp.maximum(margin, 0))
    shifted = jax.random.randint(jax.random.fold_in(own, 4), (count // 2,), 0, 1 << 20) % (margin + 1)
    lengths = lengths.at[donor].add(-shifted).at[receiver].add(shifted)
    items = jnp.searchsorted(jnp.cumsum(lengths), jnp.arange(rows * top), side="right").astype(jnp.int32)
    grid = items.reshape(top, rows).T
    grid = grid[jax.random.permutation(jax.random.fold_in(own, 1), rows)]
    rotation = jax.random.randint(jax.random.fold_in(own, 2), (rows, 1), 0, top)
    return jnp.take_along_axis(grid, (jnp.arange(top)[None, :] + rotation) % top, axis=1)


def portions_of(amount, total, bound, lean, full):
    portions = [(1 << 20) // math.isqrt(standing ** lean) + 1 for standing in range(1, amount + 1)]
    largest = bound if full else min(bound, max(-(-total // amount), total * portions[0] // sum(portions)))
    least = 1 if total - largest >= amount - 1 else 0
    given, surplus = [largest] + [least] * (amount - 1), total - largest - least * (amount - 1)
    while surplus > 0:
        movable = [i for i in range(1, amount) if given[i] < largest] or [i for i in range(1, amount) if given[i] < bound]
        pool, budget = sum([portions[i] for i in movable]), surplus
        for i in movable:
            addition = min(bound - given[i], max(1, budget * portions[i] // pool), surplus)
            given[i] = given[i] + addition
            surplus = surplus - addition
    return np.array(given)


def scatter_about(key, dims, deviation, reach, shards=(), held_as=jnp.bfloat16):
    entries = deviation * jax.random.normal(key, dims, jnp.float32)
    if shards:
        entries = entries * level_of(key, dims, shards, -0.22, 0.18)
    return jnp.clip(entries, -reach, reach).astype(held_as)


def setup_inputs(seed: int = 0) -> dict:
    key_list = jax.random.split(jax.random.key(seed), 9)
    solution = scatter_about(key_list[0], (NVAR, SOLPTS, NEL), 1.0, 6.0, ((2, 128),), jnp.float32)
    velocity = jnp.clip(jax.random.uniform(key_list[1], (3, NEL), jnp.float32, -1.0, 1.0) * level_of(key_list[1], (3, NEL), ((1, 128),), -0.4, 0.0), -1.0, 1.0)
    inv_jacobian = jnp.clip(jnp.exp(math.log(3.0) - 1.7917595 * jax.random.uniform(key_list[2], (SOLPTS, NEL), jnp.float32) ** level_of(key_list[2], (SOLPTS, NEL), ((1, 128),), -0.2, 0.2)), 0.5, 3.0)
    face_speed = scatter_about(key_list[3], (FLXPTS, NEL), 1.0, 6.0, ((1, 128),), jnp.float32)
    face_link = draw_face_link(jax.random.fold_in(key_list[8], 71), 0)
    donor_elem = touch_ends(jax.random.randint(key_list[5], (NREC,), 0, E_DEV), jax.random.fold_in(key_list[5], 1), 0, E_DEV - 1).astype(jnp.int32)
    ref_coords = jnp.clip(jax.random.uniform(key_list[6], (3, NREC), jnp.float32, -1.0, 1.0) * level_of(key_list[6], (3, NREC), ((1, 128),), -0.4, 0.0), -1.0, 1.0)
    owner_list_keys = jax.random.split(jax.random.fold_in(key_list[7], 1), NREC // REC_DEV)
    owner_list_turns = jax.random.permutation(jax.random.fold_in(key_list[7], 3), NREC // REC_DEV)
    owner_list = jax.vmap(lambda own, number: deal_out(jax.random.fold_in(key_list[7], 2), own, number, REC_DEV, N_BULK, 1, CAP, 2))(owner_list_keys, owner_list_turns).reshape((NREC, 1))
    return dict(solution=solution, velocity=velocity, inv_jacobian=inv_jacobian, face_speed=face_speed, face_link=face_link, donor_elem=donor_elem, ref_coords=ref_coords, owner_list=owner_list)


gauss_nodes = (-0.8611363115940526, -0.3399810435848563, 0.3399810435848563, 0.8611363115940526)
quad_weights = (0.3478548451374538, 0.6521451548625461, 0.6521451548625461, 0.3478548451374538)
section_step = 0.2


def lagrange_at(x):
    values = []
    for j in range(4):
        factor = 1.0
        for m in range(4):
            if m != j:
                factor = factor * (x - gauss_nodes[m]) / (gauss_nodes[j] - gauss_nodes[m])
        values.append(factor)
    return values


def tables():
    slopes = np.zeros((4, 4))
    for i in range(4):
        for j in range(4):
            summed = 0.0
            for m in range(4):
                if m != j:
                    product = 1.0 / (gauss_nodes[j] - gauss_nodes[m])
                    for n in range(4):
                        if n != j and n != m:
                            product = product * (gauss_nodes[i] - gauss_nodes[n]) / (gauss_nodes[j] - gauss_nodes[n])
                    summed = summed + product
            slopes[i, j] = summed
    end_values = [lagrange_at(-1.0), lagrange_at(1.0)]
    extrapolate = np.zeros((96, 64))
    lifting = np.zeros((64, 96))
    derivative = np.zeros((3, 64, 64))
    for p in range(64):
        point_idx = (p // 16, (p // 4) % 4, p % 4)
        for f in range(6):
            normal_dir = f // 2
            across = [t for t in range(3) if t != normal_dir]
            q = point_idx[across[0]] * 4 + point_idx[across[1]]
            flux_row = q * 6 + f
            extrapolate[flux_row, p] = end_values[f % 2][point_idx[normal_dir]]
            lifting[p, flux_row] = end_values[f % 2][point_idx[normal_dir]] / quad_weights[point_idx[normal_dir]]
        for s in range(64):
            other_idx = (s // 16, (s // 4) % 4, s % 4)
            for normal_dir in range(3):
                if all(point_idx[t] == other_idx[t] for t in range(3) if t != normal_dir):
                    derivative[normal_dir, p, s] = slopes[point_idx[normal_dir], other_idx[normal_dir]]
    return (jnp.asarray(extrapolate, dtype=jnp.float32), jnp.asarray(derivative, dtype=jnp.float32),
            jnp.asarray(lifting, dtype=jnp.float32))


def face_values(solution, extrapolate):
    values = jnp.einsum('kp,vpe->vke', extrapolate, solution, precision=lax.Precision.HIGHEST)
    return values.reshape(values.shape[0], 16, 6 * values.shape[2])


def rim_buffer(surface_vals, speeds, links, faces_total, rim_count):
    slots = jnp.where(links >= faces_total, links - faces_total, 2 * rim_count)
    senders = jnp.zeros((2 * rim_count,), jnp.int32).at[slots].set(
        jnp.arange(faces_total, dtype=jnp.int32), mode="drop")
    return jnp.concatenate([jnp.take(surface_vals, senders, axis=2),
                            jnp.take(speeds, senders, axis=1)[None]], axis=0)


def surface_term(surface_vals, speeds, links, received, lifting, elems):
    table_vals = jnp.concatenate([surface_vals, received[:-1]], axis=2)
    table_speed = jnp.concatenate([speeds, received[-1]], axis=1)
    outer_vals = jnp.take(table_vals, links, axis=2)
    outer_speed = jnp.take(table_speed, links, axis=1)
    normal = 0.5 * (speeds - outer_speed)
    common = 0.5 * normal * (surface_vals + outer_vals) + 0.5 * jnp.abs(normal) * (surface_vals - outer_vals)
    jump_term = (common - speeds * surface_vals).reshape(surface_vals.shape[0], 96, elems)
    return jnp.einsum('pk,vke->vpe', lifting, jump_term, precision=lax.Precision.HIGHEST)


def volume_term(solution, velocity, derivative):
    slopes = jnp.einsum('dpq,vqe->dvpe', derivative, solution, precision=lax.Precision.HIGHEST)
    return jnp.sum(velocity[:, None, None, :] * slopes, axis=0)


def receptor_values(advanced, donors, coords):
    basis_x = jnp.stack(lagrange_at(coords[0]))
    basis_y = jnp.stack(lagrange_at(coords[1]))
    basis_z = jnp.stack(lagrange_at(coords[2]))
    weights = (basis_x[:, None, None, :] * basis_y[None, :, None, :] * basis_z[None, None, :, :]).reshape(64, -1)
    picked = jnp.take(advanced, donors, axis=2)
    return jnp.einsum('vpr,pr->vr', picked, weights, precision=lax.Precision.HIGHEST)


def owner_ranks(owners, buckets):
    onehot = (owners[:, None] == jnp.arange(buckets, dtype=jnp.int32)[None, :]).astype(jnp.int32)
    before = jnp.cumsum(onehot, axis=0) - onehot
    return jnp.sum(before * onehot, axis=1)


def reference(solution, velocity, inv_jacobian, face_speed, face_link, donor_elem, ref_coords, owner_list):
    extrapolate, derivative, lifting = tables()
    faces_total = 6 * E_DEV

    def device_slice(array, device):
        return lax.dynamic_slice_in_dim(array, device * E_DEV, E_DEV, array.ndim - 1)

    def outgoing_of(device):
        surface_vals = face_values(device_slice(solution, device), extrapolate)
        speeds = device_slice(face_speed, device).reshape(16, faces_total)
        links = device_slice(face_link, device).reshape(faces_total)
        return rim_buffer(surface_vals, speeds, links, faces_total, IFACE)

    devices_all = jnp.arange(DEVICES, dtype=jnp.int32)
    outgoing = lax.map(outgoing_of, devices_all)
    by_valve = outgoing.reshape(N_VALVE, N_BULK, 6, 16, 2 * IFACE)
    from_prev = jnp.roll(by_valve[..., IFACE:], 1, axis=0)
    from_next = jnp.roll(by_valve[..., :IFACE], -1, axis=0)
    incoming = jnp.concatenate([from_prev, from_next], axis=-1).reshape(DEVICES, 6, 16, 2 * IFACE)

    def section_of(packed):
        device, received = packed
        local_sol = device_slice(solution, device)
        surface_vals = face_values(local_sol, extrapolate)
        speeds = device_slice(face_speed, device).reshape(16, faces_total)
        links = device_slice(face_link, device).reshape(faces_total)
        surface = surface_term(surface_vals, speeds, links, received, lifting, E_DEV)
        volume = volume_term(local_sol, device_slice(velocity, device), derivative)
        rate = -device_slice(inv_jacobian, device)[None] * (volume + surface)
        advanced = local_sol + section_step * rate
        donors = lax.dynamic_slice_in_dim(donor_elem, device * REC_DEV, REC_DEV, 0)
        coords = lax.dynamic_slice_in_dim(ref_coords, device * REC_DEV, REC_DEV, 1)
        return rate, receptor_values(advanced, donors, coords)

    rates, receptor_vals = lax.map(section_of, (devices_all, incoming))
    section_rate = jnp.transpose(rates, (1, 2, 0, 3)).reshape(NVAR, SOLPTS, NEL)
    owners = owner_list[:, 0].reshape(N_VALVE * N_BULK, REC_DEV)
    ranks = jax.vmap(lambda row: owner_ranks(row, N_BULK))(owners).reshape(N_VALVE, N_BULK, REC_DEV)
    owners = owners.reshape(N_VALVE, N_BULK, REC_DEV)
    values = jnp.transpose(receptor_vals.reshape(N_VALVE, N_BULK, NVAR, REC_DEV), (2, 0, 1, 3))
    valve_idx = jnp.broadcast_to(jnp.arange(N_VALVE, dtype=jnp.int32)[:, None, None], owners.shape)
    places = jnp.arange(N_BULK, dtype=jnp.int32)[None, :, None] * CAP + ranks
    fringe = jnp.zeros((NVAR, N_VALVE, N_BULK, N_BULK * CAP), jnp.float32)
    fringe = fringe.at[:, valve_idx, owners, places].set(values)
    return section_rate, fringe.reshape(NVAR, SLOTS)
```

```python
import jax
import jax.numpy as jnp
import numpy as np
from jax import lax
from jax.sharding import PartitionSpec as P

gauss_nodes = (-0.8611363115940526, -0.3399810435848563, 0.3399810435848563, 0.8611363115940526)
quad_weights = (0.3478548451374538, 0.6521451548625461, 0.6521451548625461, 0.3478548451374538)
section_step = 0.2


def padded(shard, sides, width):
    for axis, dim in sides:
        size, length = (lax.axis_size(axis), shard.shape[dim])
        up = [(i, (i + 1) % size) for i in range(size)]
        down = [(j, i) for i, j in up]
        last = lax.slice_in_dim(shard, length - width, length, axis=dim)
        initial = lax.slice_in_dim(shard, 0, width, axis=dim)
        before = lax.ppermute(last, axis, up)
        after = lax.ppermute(initial, axis, down)
        shard = jnp.concatenate([before, shard, after], axis=dim)
    return shard


def lagrange_at(x):
    values = []
    for j in range(4):
        factor = 1.0
        for m in range(4):
            if m != j:
                factor = factor * (x - gauss_nodes[m]) / (gauss_nodes[j] - gauss_nodes[m])
        values.append(factor)
    return values


def tables():
    slopes = np.zeros((4, 4))
    for i in range(4):
        for j in range(4):
            summed = 0.0
            for m in range(4):
                if m != j:
                    product = 1.0 / (gauss_nodes[j] - gauss_nodes[m])
                    for n in range(4):
                        if n != j and n != m:
                            product = (
                                product
                                * (gauss_nodes[i] - gauss_nodes[n])
                                / (gauss_nodes[j] - gauss_nodes[n])
                            )
                    summed = summed + product
            slopes[i, j] = summed
    end_values = [lagrange_at(-1.0), lagrange_at(1.0)]
    extrapolate = np.zeros((96, 64))
    lifting = np.zeros((64, 96))
    derivative = np.zeros((3, 64, 64))
    for p in range(64):
        point_idx = (p // 16, p // 4 % 4, p % 4)
        for f in range(6):
            normal_dir = f // 2
            across = [t for t in range(3) if t != normal_dir]
            q = point_idx[across[0]] * 4 + point_idx[across[1]]
            flux_row = q * 6 + f
            extrapolate[flux_row, p] = end_values[f % 2][point_idx[normal_dir]]
            lifting[p, flux_row] = (
                end_values[f % 2][point_idx[normal_dir]] / quad_weights[point_idx[normal_dir]]
            )
        for s in range(64):
            other_idx = (s // 16, s // 4 % 4, s % 4)
            for normal_dir in range(3):
                if all((point_idx[t] == other_idx[t] for t in range(3) if t != normal_dir)):
                    derivative[normal_dir, p, s] = slopes[
                        point_idx[normal_dir], other_idx[normal_dir]
                    ]
    return (
        jnp.asarray(extrapolate, dtype=jnp.float32),
        jnp.asarray(derivative, dtype=jnp.float32),
        jnp.asarray(lifting, dtype=jnp.float32),
    )


def face_rows(solution, face_speed, extrapolate):
    nvars = solution.shape[0]
    elems = solution.shape[2]
    ext_faces = extrapolate.reshape(16, 6, 64)
    values = jnp.einsum("qfp,vpe->feqv", ext_faces, solution, precision=lax.Precision.HIGHEST)
    values = values.reshape(6 * elems, 16, nvars)
    speeds = jnp.transpose(face_speed.reshape(16, 6, elems), (1, 2, 0)).reshape(6 * elems, 16)
    return (values, speeds)


def rim_rows(table_own, links, faces_total, rim_count):
    slots = jnp.where(links >= faces_total, links - faces_total, 2 * rim_count)
    senders = (
        jnp.zeros((2 * rim_count,), jnp.int32)
        .at[slots]
        .set(jnp.arange(faces_total, dtype=jnp.int32), mode="drop")
    )
    return jnp.take(table_own, senders, axis=0)


def surface_term(values, speeds, table_own, links, received, lifting, elems):
    nvars = values.shape[2]
    full_table = jnp.concatenate([table_own, received], axis=0)
    outer = jnp.take(full_table, links, axis=0)
    outer_vals = outer[:, : 16 * nvars].reshape(6 * elems, 16, nvars)
    outer_speed = outer[:, 16 * nvars :][:, :, None]
    own_speed = speeds[:, :, None]
    normal = 0.5 * (own_speed - outer_speed)
    common = 0.5 * normal * (values + outer_vals) + 0.5 * jnp.abs(normal) * (values - outer_vals)
    jump_term = (common - own_speed * values).reshape(6, elems, 16, nvars)
    lift_faces = lifting.reshape(64, 16, 6)
    return jnp.einsum("pqf,feqv->vpe", lift_faces, jump_term, precision=lax.Precision.HIGHEST)


def volume_term(solution, velocity, derivative):
    slopes = jnp.einsum("dpq,vqe->dvpe", derivative, solution, precision=lax.Precision.HIGHEST)
    return jnp.sum(velocity[:, None, None, :] * slopes, axis=0)


def receptor_rows(advanced, donors, coords):
    nvars = advanced.shape[0]
    elems = advanced.shape[2]
    basis_x = jnp.stack(lagrange_at(coords[0]))
    basis_y = jnp.stack(lagrange_at(coords[1]))
    basis_z = jnp.stack(lagrange_at(coords[2]))
    weights = (
        basis_x[:, None, None, :] * basis_y[None, :, None, :] * basis_z[None, None, :, :]
    ).reshape(64, -1)
    element_rows = jnp.transpose(advanced, (2, 0, 1)).reshape(elems, nvars * 64)
    picked = jnp.take(element_rows, donors, axis=0).reshape(donors.shape[0], nvars, 64)
    return jnp.einsum("rvp,pr->rv", picked, weights, precision=lax.Precision.HIGHEST)


def on_device(
    solution, velocity, inv_jacobian, face_speed, face_link, donor_elem, ref_coords, owner_list
):
    extrapolate, derivative, lifting = tables()
    nvars = solution.shape[0]
    elems = solution.shape[2]
    rim_count = elems // 16
    faces_total = 6 * elems
    links = face_link.reshape(faces_total)
    values, speeds = face_rows(solution, face_speed, extrapolate)
    table_own = jnp.concatenate([values.reshape(faces_total, 16 * nvars), speeds], axis=1)
    outgoing = rim_rows(table_own, links, faces_total, rim_count)
    extended = padded(outgoing, (("valve", 0),), rim_count)
    received = jnp.concatenate([extended[:rim_count], extended[3 * rim_count :]], axis=0)
    surface = surface_term(values, speeds, table_own, links, received, lifting, elems)
    volume = volume_term(solution, velocity, derivative)
    section_rate = -inv_jacobian[None] * (volume + surface)
    advanced = solution + section_step * section_rate
    receptor_vals = receptor_rows(advanced, donor_elem, ref_coords)
    buckets = lax.axis_size("bulk")
    receptors = receptor_vals.shape[0]
    capacity = 2 * receptors // buckets
    owners = owner_list[:, 0]
    onehot = (owners[:, None] == jnp.arange(buckets, dtype=jnp.int32)[None, :]).astype(jnp.int32)
    before = jnp.cumsum(onehot, axis=0) - onehot
    ranks = jnp.sum(before * onehot, axis=1)
    places = owners * capacity + ranks
    send = jnp.zeros((buckets * capacity, nvars), jnp.float32)
    send = send.at[places].set(receptor_vals, mode="drop", unique_indices=True)
    send = jnp.transpose(send.reshape(buckets, capacity, nvars), (0, 2, 1))
    got = lax.all_to_all(send, "bulk", 0, 0, tiled=True)
    fringe = jnp.transpose(got, (1, 0, 2)).reshape(nvars, buckets * capacity)
    return (section_rate, fringe)


def solution(mesh):
    placed = (
        P(None, None, ("valve", "bulk")),
        P(None, ("valve", "bulk")),
        P(None, ("valve", "bulk")),
        P(None, ("valve", "bulk")),
        P(None, ("valve", "bulk")),
        P(("valve", "bulk")),
        P(None, ("valve", "bulk")),
        P(("valve", "bulk"), None),
    )
    return jax.shard_map(
        on_device,
        mesh=mesh,
        in_specs=placed,
        out_specs=(P(None, None, ("valve", "bulk")), P(None, ("valve", "bulk"))),
        check_vma=False,
    )
```

```python
import jax
import jax.numpy as jnp
import numpy as np
from jax import lax
from jax.sharding import PartitionSpec as P

gauss_nodes = (-0.8611363115940526, -0.3399810435848563, 0.3399810435848563, 0.8611363115940526)
quad_weights = (0.3478548451374538, 0.6521451548625461, 0.6521451548625461, 0.3478548451374538)
section_step = 0.2


def padded(shard, sides, width):
    for axis, dim in sides:
        size, length = (lax.axis_size(axis), shard.shape[dim])
        up = [(i, (i + 1) % size) for i in range(size)]
        down = [(j, i) for i, j in up]
        last = lax.slice_in_dim(shard, length - width, length, axis=dim)
        initial = lax.slice_in_dim(shard, 0, width, axis=dim)
        before = lax.ppermute(last, axis, up)
        after = lax.ppermute(initial, axis, down)
        shard = jnp.concatenate([before, shard, after], axis=dim)
    return shard


def lagrange_at(x):
    values = []
    for j in range(4):
        factor = 1.0
        for m in range(4):
            if m != j:
                factor = factor * (x - gauss_nodes[m]) / (gauss_nodes[j] - gauss_nodes[m])
        values.append(factor)
    return values


def tables():
    slopes = np.zeros((4, 4))
    for i in range(4):
        for j in range(4):
            summed = 0.0
            for m in range(4):
                if m != j:
                    product = 1.0 / (gauss_nodes[j] - gauss_nodes[m])
                    for n in range(4):
                        if n != j and n != m:
                            product = (
                                product
                                * (gauss_nodes[i] - gauss_nodes[n])
                                / (gauss_nodes[j] - gauss_nodes[n])
                            )
                    summed = summed + product
            slopes[i, j] = summed
    end_values = [lagrange_at(-1.0), lagrange_at(1.0)]
    extrapolate = np.zeros((96, 64))
    lifting = np.zeros((64, 96))
    derivative = np.zeros((3, 64, 64))
    for p in range(64):
        point_idx = (p // 16, p // 4 % 4, p % 4)
        for f in range(6):
            normal_dir = f // 2
            across = [t for t in range(3) if t != normal_dir]
            q = point_idx[across[0]] * 4 + point_idx[across[1]]
            flux_row = q * 6 + f
            extrapolate[flux_row, p] = end_values[f % 2][point_idx[normal_dir]]
            lifting[p, flux_row] = (
                end_values[f % 2][point_idx[normal_dir]] / quad_weights[point_idx[normal_dir]]
            )
        for s in range(64):
            other_idx = (s // 16, s // 4 % 4, s % 4)
            for normal_dir in range(3):
                if all((point_idx[t] == other_idx[t] for t in range(3) if t != normal_dir)):
                    derivative[normal_dir, p, s] = slopes[
                        point_idx[normal_dir], other_idx[normal_dir]
                    ]
    return (
        jnp.asarray(extrapolate, dtype=jnp.float32),
        jnp.asarray(derivative, dtype=jnp.float32),
        jnp.asarray(lifting, dtype=jnp.float32),
    )


def face_rows(solution, face_speed, extrapolate):
    nvars = solution.shape[0]
    elems = solution.shape[2]
    ext_faces = extrapolate.reshape(16, 6, 64)
    values = jnp.einsum("qfp,vpe->feqv", ext_faces, solution, precision=lax.Precision.HIGHEST)
    values = values.reshape(6 * elems, 16, nvars)
    speeds = jnp.transpose(face_speed.reshape(16, 6, elems), (1, 2, 0)).reshape(6 * elems, 16)
    return (values, speeds)


def rim_rows(table_own, links, faces_total, rim_count):
    wanted = faces_total + jnp.arange(2 * rim_count, dtype=jnp.int32)
    hits = links[None, :] == wanted[:, None]
    faces = jnp.arange(faces_total, dtype=jnp.int32)[None, :]
    senders = jnp.sum(jnp.where(hits, faces, 0), axis=1)
    return jnp.take(table_own, senders, axis=0)


def split_bf16(x):
    hi = lax.reduce_precision(x, exponent_bits=8, mantissa_bits=7)
    return hi.astype(jnp.bfloat16), (x - hi).astype(jnp.bfloat16)


def pick_dot(rows, onehot):
    hi, lo = split_bf16(rows)
    out = jnp.dot(hi, onehot, preferred_element_type=jnp.float32)
    return out + jnp.dot(lo, onehot, preferred_element_type=jnp.float32)


def surface_term(values, speeds, table_own, links, received, lifting, elems):
    nvars = values.shape[2]
    full_table = jnp.concatenate([table_own, received], axis=0)
    outer = jnp.take(full_table, links, axis=0)
    outer_vals = outer[:, : 16 * nvars].reshape(6 * elems, 16, nvars)
    outer_speed = outer[:, 16 * nvars :][:, :, None]
    own_speed = speeds[:, :, None]
    normal = 0.5 * (own_speed - outer_speed)
    common = 0.5 * normal * (values + outer_vals) + 0.5 * jnp.abs(normal) * (values - outer_vals)
    jump_term = (common - own_speed * values).reshape(6, elems, 16, nvars)
    lift_faces = lifting.reshape(64, 16, 6)
    return jnp.einsum("pqf,feqv->vpe", lift_faces, jump_term, precision=lax.Precision.HIGHEST)


def volume_term(solution, velocity, derivative):
    slopes = jnp.einsum("dpq,vqe->dvpe", derivative, solution, precision=lax.Precision.HIGHEST)
    return jnp.sum(velocity[:, None, None, :] * slopes, axis=0)


def receptor_rows(advanced, donors, coords):
    nvars = advanced.shape[0]
    elems = advanced.shape[2]
    basis_x = jnp.stack(lagrange_at(coords[0]))
    basis_y = jnp.stack(lagrange_at(coords[1]))
    basis_z = jnp.stack(lagrange_at(coords[2]))
    weights = (
        basis_x[:, None, None, :] * basis_y[None, :, None, :] * basis_z[None, None, :, :]
    ).reshape(64, -1)
    onehot = (jnp.arange(elems, dtype=jnp.int32)[:, None] == donors[None, :]).astype(jnp.bfloat16)
    picked = pick_dot(advanced.reshape(nvars * 64, elems), onehot).reshape(nvars, 64, -1)
    return jnp.sum(picked * weights[None], axis=1)


def on_device(
    solution, velocity, inv_jacobian, face_speed, face_link, donor_elem, ref_coords, owner_list
):
    extrapolate, derivative, lifting = tables()
    nvars = solution.shape[0]
    elems = solution.shape[2]
    rim_count = elems // 16
    faces_total = 6 * elems
    links = face_link.reshape(faces_total)
    values, speeds = face_rows(solution, face_speed, extrapolate)
    table_own = jnp.concatenate([values.reshape(faces_total, 16 * nvars), speeds], axis=1)
    outgoing = rim_rows(table_own, links, faces_total, rim_count)
    extended = padded(outgoing, (("valve", 0),), rim_count)
    received = jnp.concatenate([extended[:rim_count], extended[3 * rim_count :]], axis=0)
    surface = surface_term(values, speeds, table_own, links, received, lifting, elems)
    volume = volume_term(solution, velocity, derivative)
    section_rate = -inv_jacobian[None] * (volume + surface)
    advanced = solution + section_step * section_rate
    receptor_vals = receptor_rows(advanced, donor_elem, ref_coords)
    buckets = lax.axis_size("bulk")
    receptors = receptor_vals.shape[1]
    capacity = 2 * receptors // buckets
    owners = owner_list[:, 0]
    onehot = (owners[:, None] == jnp.arange(buckets, dtype=jnp.int32)[None, :]).astype(jnp.int32)
    before = jnp.cumsum(onehot, axis=0) - onehot
    ranks = jnp.sum(before * onehot, axis=1)
    chosen = owners[None, :] == jnp.arange(buckets, dtype=jnp.int32)[:, None]
    masked = jnp.where(chosen[:, None, :], receptor_vals[None, :, :], 0.0)
    masked = masked.reshape(buckets * nvars, receptors)
    by_rank = (ranks[:, None] == jnp.arange(capacity, dtype=jnp.int32)[None, :]).astype(jnp.bfloat16)
    send = pick_dot(masked, by_rank).reshape(buckets, nvars, capacity)
    got = lax.all_to_all(send, "bulk", 0, 0, tiled=True)
    fringe = jnp.transpose(got, (1, 0, 2)).reshape(nvars, buckets * capacity)
    return (section_rate, fringe)


def solution(mesh):
    placed = (
        P(None, None, ("valve", "bulk")),
        P(None, ("valve", "bulk")),
        P(None, ("valve", "bulk")),
        P(None, ("valve", "bulk")),
        P(None, ("valve", "bulk")),
        P(("valve", "bulk")),
        P(None, ("valve", "bulk")),
        P(("valve", "bulk"), None),
    )
    return jax.shard_map(
        on_device,
        mesh=mesh,
        in_specs=placed,
        out_specs=(P(None, None, ("valve", "bulk")), P(None, ("valve", "bulk"))),
        check_vma=False,
    )
```

```python
import jax
import jax.numpy as jnp
import numpy as np
from jax import lax
from jax.sharding import PartitionSpec as P

gauss_nodes = (-0.8611363115940526, -0.3399810435848563, 0.3399810435848563, 0.8611363115940526)
quad_weights = (0.3478548451374538, 0.6521451548625461, 0.6521451548625461, 0.3478548451374538)
section_step = 0.2


def padded(shard, sides, width):
    for axis, dim in sides:
        size, length = (lax.axis_size(axis), shard.shape[dim])
        up = [(i, (i + 1) % size) for i in range(size)]
        down = [(j, i) for i, j in up]
        last = lax.slice_in_dim(shard, length - width, length, axis=dim)
        initial = lax.slice_in_dim(shard, 0, width, axis=dim)
        before = lax.ppermute(last, axis, up)
        after = lax.ppermute(initial, axis, down)
        shard = jnp.concatenate([before, shard, after], axis=dim)
    return shard


def lagrange_at(x):
    values = []
    for j in range(4):
        factor = 1.0
        for m in range(4):
            if m != j:
                factor = factor * (x - gauss_nodes[m]) / (gauss_nodes[j] - gauss_nodes[m])
        values.append(factor)
    return values


def tables():
    slopes = np.zeros((4, 4))
    for i in range(4):
        for j in range(4):
            summed = 0.0
            for m in range(4):
                if m != j:
                    product = 1.0 / (gauss_nodes[j] - gauss_nodes[m])
                    for n in range(4):
                        if n != j and n != m:
                            product = (
                                product
                                * (gauss_nodes[i] - gauss_nodes[n])
                                / (gauss_nodes[j] - gauss_nodes[n])
                            )
                    summed = summed + product
            slopes[i, j] = summed
    end_values = [lagrange_at(-1.0), lagrange_at(1.0)]
    extrapolate = np.zeros((96, 64))
    lifting = np.zeros((64, 96))
    derivative = np.zeros((3, 64, 64))
    for p in range(64):
        point_idx = (p // 16, p // 4 % 4, p % 4)
        for f in range(6):
            normal_dir = f // 2
            across = [t for t in range(3) if t != normal_dir]
            q = point_idx[across[0]] * 4 + point_idx[across[1]]
            flux_row = q * 6 + f
            extrapolate[flux_row, p] = end_values[f % 2][point_idx[normal_dir]]
            lifting[p, flux_row] = (
                end_values[f % 2][point_idx[normal_dir]] / quad_weights[point_idx[normal_dir]]
            )
        for s in range(64):
            other_idx = (s // 16, s // 4 % 4, s % 4)
            for normal_dir in range(3):
                if all((point_idx[t] == other_idx[t] for t in range(3) if t != normal_dir)):
                    derivative[normal_dir, p, s] = slopes[
                        point_idx[normal_dir], other_idx[normal_dir]
                    ]
    return (
        jnp.asarray(extrapolate, dtype=jnp.float32),
        jnp.asarray(derivative, dtype=jnp.float32),
        jnp.asarray(lifting, dtype=jnp.float32),
    )


def face_rows(solution, face_speed, extrapolate):
    nvars = solution.shape[0]
    elems = solution.shape[2]
    ext_faces = extrapolate.reshape(16, 6, 64)
    values = jnp.einsum("qfp,vpe->feqv", ext_faces, solution, precision=lax.Precision.HIGHEST)
    values = values.reshape(6 * elems, 16, nvars)
    speeds = jnp.transpose(face_speed.reshape(16, 6, elems), (1, 2, 0)).reshape(6 * elems, 16)
    return (values, speeds)


def rim_rows(table_own, links, faces_total, rim_count):
    wanted = faces_total + jnp.arange(2 * rim_count, dtype=jnp.int32)
    hits = links[None, :] == wanted[:, None]
    faces = jnp.arange(faces_total, dtype=jnp.int32)[None, :]
    senders = jnp.sum(jnp.where(hits, faces, 0), axis=1)
    return jnp.take(table_own, senders, axis=0)


def split_bf16(x):
    hi = lax.reduce_precision(x, exponent_bits=8, mantissa_bits=7)
    return hi.astype(jnp.bfloat16), (x - hi).astype(jnp.bfloat16)


def pick_dot(rows, onehot):
    hi, lo = split_bf16(rows)
    out = jnp.dot(hi, onehot, preferred_element_type=jnp.float32)
    return out + jnp.dot(lo, onehot, preferred_element_type=jnp.float32)


def surface_term(values, speeds, table_own, links, received, lifting, elems):
    nvars = values.shape[2]
    full_table = jnp.concatenate([table_own, received], axis=0)
    outer = jnp.take(full_table, links, axis=0)
    outer_vals = outer[:, : 16 * nvars].reshape(6 * elems, 16, nvars)
    outer_speed = outer[:, 16 * nvars :][:, :, None]
    own_speed = speeds[:, :, None]
    normal = 0.5 * (own_speed - outer_speed)
    common = 0.5 * normal * (values + outer_vals) + 0.5 * jnp.abs(normal) * (values - outer_vals)
    jump_term = (common - own_speed * values).reshape(6, elems, 16, nvars)
    lift_faces = lifting.reshape(64, 16, 6)
    return jnp.einsum("pqf,feqv->vpe", lift_faces, jump_term, precision=lax.Precision.HIGHEST)


def volume_term(solution, velocity, derivative):
    slopes = jnp.einsum("dpq,vqe->dvpe", derivative, solution, precision=lax.Precision.HIGHEST)
    return jnp.sum(velocity[:, None, None, :] * slopes, axis=0)


def receptor_rows(advanced, donors, coords):
    nvars = advanced.shape[0]
    elems = advanced.shape[2]
    basis_x = jnp.stack(lagrange_at(coords[0]))
    basis_y = jnp.stack(lagrange_at(coords[1]))
    basis_z = jnp.stack(lagrange_at(coords[2]))
    weights = (
        basis_x[:, None, None, :] * basis_y[None, :, None, :] * basis_z[None, None, :, :]
    ).reshape(64, -1)
    onehot = (jnp.arange(elems, dtype=jnp.int32)[:, None] == donors[None, :]).astype(jnp.bfloat16)
    picked = pick_dot(advanced.reshape(nvars * 64, elems), onehot).reshape(nvars, 64, -1)
    return jnp.sum(picked * weights[None], axis=1)


def on_device(
    solution, velocity, inv_jacobian, face_speed, face_link, donor_elem, ref_coords, owner_list
):
    extrapolate, derivative, lifting = tables()
    nvars = solution.shape[0]
    elems = solution.shape[2]
    rim_count = elems // 16
    faces_total = 6 * elems
    links = face_link.reshape(faces_total)
    values, speeds = face_rows(solution, face_speed, extrapolate)
    table_own = jnp.concatenate([values.reshape(faces_total, 16 * nvars), speeds], axis=1)
    outgoing = rim_rows(table_own, links, faces_total, rim_count)
    extended = padded(outgoing, (("valve", 0),), rim_count)
    received = jnp.concatenate([extended[:rim_count], extended[3 * rim_count :]], axis=0)
    surface = surface_term(values, speeds, table_own, links, received, lifting, elems)
    volume = volume_term(solution, velocity, derivative)
    section_rate = -inv_jacobian[None] * (volume + surface)
    advanced = solution + section_step * section_rate
    receptor_vals = receptor_rows(advanced, donor_elem, ref_coords)
    buckets = lax.axis_size("bulk")
    receptors = receptor_vals.shape[1]
    capacity = 2 * receptors // buckets
    owners = owner_list[:, 0]
    onehot = (owners[:, None] == jnp.arange(buckets, dtype=jnp.int32)[None, :]).astype(jnp.int32)
    before = jnp.cumsum(onehot, axis=0) - onehot
    ranks = jnp.sum(before * onehot, axis=1)
    chosen = owners[:, None] == jnp.arange(buckets, dtype=jnp.int32)[None, :]
    masked = jnp.where(chosen[:, :, None], jnp.transpose(receptor_vals)[:, None, :], 0.0)
    hi, lo = split_bf16(masked.reshape(receptors, buckets * nvars))
    by_rank = (jnp.arange(capacity, dtype=jnp.int32)[:, None] == ranks[None, :]).astype(jnp.bfloat16)
    both = jnp.dot(by_rank, jnp.concatenate([hi, lo], axis=1), preferred_element_type=jnp.float32)
    placed = both[:, : buckets * nvars] + both[:, buckets * nvars :]
    send = jnp.transpose(placed.reshape(capacity, buckets, nvars), (1, 2, 0))
    me = lax.axis_index("bulk")
    ahead = jnp.roll(send, -me, axis=0)
    blocks = [ahead[0]]
    for k in range(1, buckets):
        pairs = [(i, (i + k) % buckets) for i in range(buckets)]
        blocks.append(lax.ppermute(ahead[k], "bulk", pairs))
    behind = jnp.stack([blocks[0]] + blocks[:0:-1], axis=0)
    got = jnp.roll(behind, me, axis=0)
    fringe = jnp.transpose(got, (1, 0, 2)).reshape(nvars, buckets * capacity)
    return (section_rate, fringe)


def solution(mesh):
    placed = (
        P(None, None, ("valve", "bulk")),
        P(None, ("valve", "bulk")),
        P(None, ("valve", "bulk")),
        P(None, ("valve", "bulk")),
        P(None, ("valve", "bulk")),
        P(("valve", "bulk")),
        P(None, ("valve", "bulk")),
        P(("valve", "bulk"), None),
    )
    return jax.shard_map(
        on_device,
        mesh=mesh,
        in_specs=placed,
        out_specs=(P(None, None, ("valve", "bulk")), P(None, ("valve", "bulk"))),
        check_vma=False,
    )
```

```python
import jax
import jax.numpy as jnp
import numpy as np
from jax import lax
from jax.sharding import PartitionSpec as P
from jax.experimental import pallas as pl
from jax.experimental.pallas import tpu as pltpu

gauss_nodes = (-0.8611363115940526, -0.3399810435848563, 0.3399810435848563, 0.8611363115940526)
quad_weights = (0.3478548451374538, 0.6521451548625461, 0.6521451548625461, 0.3478548451374538)
section_step = 0.2


def padded(shard, sides, width):
    for axis, dim in sides:
        size, length = (lax.axis_size(axis), shard.shape[dim])
        up = [(i, (i + 1) % size) for i in range(size)]
        down = [(j, i) for i, j in up]
        last = lax.slice_in_dim(shard, length - width, length, axis=dim)
        initial = lax.slice_in_dim(shard, 0, width, axis=dim)
        before = lax.ppermute(last, axis, up)
        after = lax.ppermute(initial, axis, down)
        shard = jnp.concatenate([before, shard, after], axis=dim)
    return shard


def lagrange_at(x):
    values = []
    for j in range(4):
        factor = 1.0
        for m in range(4):
            if m != j:
                factor = factor * (x - gauss_nodes[m]) / (gauss_nodes[j] - gauss_nodes[m])
        values.append(factor)
    return values


def tables():
    slopes = np.zeros((4, 4))
    for i in range(4):
        for j in range(4):
            summed = 0.0
            for m in range(4):
                if m != j:
                    product = 1.0 / (gauss_nodes[j] - gauss_nodes[m])
                    for n in range(4):
                        if n != j and n != m:
                            product = (
                                product
                                * (gauss_nodes[i] - gauss_nodes[n])
                                / (gauss_nodes[j] - gauss_nodes[n])
                            )
                    summed = summed + product
            slopes[i, j] = summed
    end_values = [lagrange_at(-1.0), lagrange_at(1.0)]
    extrapolate = np.zeros((96, 64))
    lifting = np.zeros((64, 96))
    derivative = np.zeros((3, 64, 64))
    for p in range(64):
        point_idx = (p // 16, p // 4 % 4, p % 4)
        for f in range(6):
            normal_dir = f // 2
            across = [t for t in range(3) if t != normal_dir]
            q = point_idx[across[0]] * 4 + point_idx[across[1]]
            flux_row = q * 6 + f
            extrapolate[flux_row, p] = end_values[f % 2][point_idx[normal_dir]]
            lifting[p, flux_row] = (
                end_values[f % 2][point_idx[normal_dir]] / quad_weights[point_idx[normal_dir]]
            )
        for s in range(64):
            other_idx = (s // 16, s // 4 % 4, s % 4)
            for normal_dir in range(3):
                if all((point_idx[t] == other_idx[t] for t in range(3) if t != normal_dir)):
                    derivative[normal_dir, p, s] = slopes[
                        point_idx[normal_dir], other_idx[normal_dir]
                    ]
    return (
        jnp.asarray(extrapolate, dtype=jnp.float32),
        jnp.asarray(derivative, dtype=jnp.float32),
        jnp.asarray(lifting, dtype=jnp.float32),
    )


def face_rows(solution, face_speed, extrapolate):
    nvars = solution.shape[0]
    elems = solution.shape[2]
    ext_faces = extrapolate.reshape(16, 6, 64)
    values = jnp.einsum("qfp,vpe->feqv", ext_faces, solution, precision=lax.Precision.HIGHEST)
    values = values.reshape(6 * elems, 16, nvars)
    speeds = jnp.transpose(face_speed.reshape(16, 6, elems), (1, 2, 0)).reshape(6 * elems, 16)
    return (values, speeds)


def rim_rows(table_own, links, faces_total, rim_count):
    wanted = faces_total + jnp.arange(2 * rim_count, dtype=jnp.int32)
    hits = links[None, :] == wanted[:, None]
    faces = jnp.arange(faces_total, dtype=jnp.int32)[None, :]
    senders = jnp.sum(jnp.where(hits, faces, 0), axis=1)
    return jnp.take(table_own, senders, axis=0)


def split_bf16(x):
    hi = lax.reduce_precision(x, exponent_bits=8, mantissa_bits=7)
    return hi.astype(jnp.bfloat16), (x - hi).astype(jnp.bfloat16)


def pick_dot(rows, onehot):
    hi, lo = split_bf16(rows)
    out = jnp.dot(hi, onehot, preferred_element_type=jnp.float32)
    return out + jnp.dot(lo, onehot, preferred_element_type=jnp.float32)


def _rows_kernel(idx_ref, table_ref, out_ref):
    def body(i, carry):
        base = pl.multiple_of(i * 8, 8)
        for j in range(8):
            row = idx_ref[base + j]
            out_ref[pl.ds(base + j, 1), :] = table_ref[pl.ds(row, 1), :]
        return carry

    lax.fori_loop(0, out_ref.shape[0] // 8, body, 0)


def take_rows(table, idx):
    return pl.pallas_call(
        _rows_kernel,
        out_shape=jax.ShapeDtypeStruct((idx.shape[0], table.shape[1]), table.dtype),
        in_specs=[
            pl.BlockSpec(memory_space=pltpu.SMEM),
            pl.BlockSpec(memory_space=pltpu.VMEM),
        ],
        out_specs=pl.BlockSpec(memory_space=pltpu.VMEM),
        cost_estimate=pl.CostEstimate(
            flops=0, transcendentals=0, bytes_accessed=2 * idx.shape[0] * table.shape[1] * 4
        ),
    )(idx, table)


def surface_term(values, speeds, table_own, links, received, lifting, elems):
    nvars = values.shape[2]
    full_table = jnp.concatenate([table_own, received], axis=0)
    outer = take_rows(full_table, links)
    outer_vals = outer[:, : 16 * nvars].reshape(6 * elems, 16, nvars)
    outer_speed = outer[:, 16 * nvars :][:, :, None]
    own_speed = speeds[:, :, None]
    normal = 0.5 * (own_speed - outer_speed)
    common = 0.5 * normal * (values + outer_vals) + 0.5 * jnp.abs(normal) * (values - outer_vals)
    jump_term = (common - own_speed * values).reshape(6, elems, 16, nvars)
    lift_faces = lifting.reshape(64, 16, 6)
    return jnp.einsum("pqf,feqv->vpe", lift_faces, jump_term, precision=lax.Precision.HIGHEST)


def volume_term(solution, velocity, derivative):
    slopes = jnp.einsum("dpq,vqe->dvpe", derivative, solution, precision=lax.Precision.HIGHEST)
    return jnp.sum(velocity[:, None, None, :] * slopes, axis=0)


def receptor_rows(advanced, donors, coords):
    nvars = advanced.shape[0]
    elems = advanced.shape[2]
    basis_x = jnp.stack(lagrange_at(coords[0]))
    basis_y = jnp.stack(lagrange_at(coords[1]))
    basis_z = jnp.stack(lagrange_at(coords[2]))
    weights = (
        basis_x[:, None, None, :] * basis_y[None, :, None, :] * basis_z[None, None, :, :]
    ).reshape(64, -1)
    onehot = (jnp.arange(elems, dtype=jnp.int32)[:, None] == donors[None, :]).astype(jnp.bfloat16)
    picked = pick_dot(advanced.reshape(nvars * 64, elems), onehot).reshape(nvars, 64, -1)
    return jnp.sum(picked * weights[None], axis=1)


def on_device(
    solution, velocity, inv_jacobian, face_speed, face_link, donor_elem, ref_coords, owner_list
):
    extrapolate, derivative, lifting = tables()
    nvars = solution.shape[0]
    elems = solution.shape[2]
    rim_count = elems // 16
    faces_total = 6 * elems
    links = face_link.reshape(faces_total)
    values, speeds = face_rows(solution, face_speed, extrapolate)
    table_own = jnp.concatenate([values.reshape(faces_total, 16 * nvars), speeds], axis=1)
    outgoing = rim_rows(table_own, links, faces_total, rim_count)
    extended = padded(outgoing, (("valve", 0),), rim_count)
    received = jnp.concatenate([extended[:rim_count], extended[3 * rim_count :]], axis=0)
    surface = surface_term(values, speeds, table_own, links, received, lifting, elems)
    volume = volume_term(solution, velocity, derivative)
    section_rate = -inv_jacobian[None] * (volume + surface)
    advanced = solution + section_step * section_rate
    receptor_vals = receptor_rows(advanced, donor_elem, ref_coords)
    buckets = lax.axis_size("bulk")
    receptors = receptor_vals.shape[1]
    capacity = 2 * receptors // buckets
    owners = owner_list[:, 0]
    onehot = (owners[:, None] == jnp.arange(buckets, dtype=jnp.int32)[None, :]).astype(jnp.int32)
    before = jnp.cumsum(onehot, axis=0) - onehot
    ranks = jnp.sum(before * onehot, axis=1)
    chosen = owners[:, None] == jnp.arange(buckets, dtype=jnp.int32)[None, :]
    masked = jnp.where(chosen[:, :, None], jnp.transpose(receptor_vals)[:, None, :], 0.0)
    hi, lo = split_bf16(masked.reshape(receptors, buckets * nvars))
    by_rank = (jnp.arange(capacity, dtype=jnp.int32)[:, None] == ranks[None, :]).astype(jnp.bfloat16)
    both = jnp.dot(by_rank, jnp.concatenate([hi, lo], axis=1), preferred_element_type=jnp.float32)
    placed = both[:, : buckets * nvars] + both[:, buckets * nvars :]
    send = jnp.transpose(placed.reshape(capacity, buckets, nvars), (1, 2, 0))
    got = lax.all_to_all(send, "bulk", 0, 0, tiled=True)
    fringe = jnp.transpose(got, (1, 0, 2)).reshape(nvars, buckets * capacity)
    return (section_rate, fringe)


def solution(mesh):
    placed = (
        P(None, None, ("valve", "bulk")),
        P(None, ("valve", "bulk")),
        P(None, ("valve", "bulk")),
        P(None, ("valve", "bulk")),
        P(None, ("valve", "bulk")),
        P(("valve", "bulk")),
        P(None, ("valve", "bulk")),
        P(("valve", "bulk"), None),
    )
    return jax.shard_map(
        on_device,
        mesh=mesh,
        in_specs=placed,
        out_specs=(P(None, None, ("valve", "bulk")), P(None, ("valve", "bulk"))),
        check_vma=False,
    )
```

```python
import jax
import jax.numpy as jnp
import numpy as np
from jax import lax
from jax.sharding import PartitionSpec as P
from jax.experimental import pallas as pl
from jax.experimental.pallas import tpu as pltpu

gauss_nodes = (-0.8611363115940526, -0.3399810435848563, 0.3399810435848563, 0.8611363115940526)
quad_weights = (0.3478548451374538, 0.6521451548625461, 0.6521451548625461, 0.3478548451374538)
section_step = 0.2


def padded(shard, sides, width):
    for axis, dim in sides:
        size, length = (lax.axis_size(axis), shard.shape[dim])
        up = [(i, (i + 1) % size) for i in range(size)]
        down = [(j, i) for i, j in up]
        last = lax.slice_in_dim(shard, length - width, length, axis=dim)
        initial = lax.slice_in_dim(shard, 0, width, axis=dim)
        before = lax.ppermute(last, axis, up)
        after = lax.ppermute(initial, axis, down)
        shard = jnp.concatenate([before, shard, after], axis=dim)
    return shard


def lagrange_at(x):
    values = []
    for j in range(4):
        factor = 1.0
        for m in range(4):
            if m != j:
                factor = factor * (x - gauss_nodes[m]) / (gauss_nodes[j] - gauss_nodes[m])
        values.append(factor)
    return values


def tables():
    slopes = np.zeros((4, 4))
    for i in range(4):
        for j in range(4):
            summed = 0.0
            for m in range(4):
                if m != j:
                    product = 1.0 / (gauss_nodes[j] - gauss_nodes[m])
                    for n in range(4):
                        if n != j and n != m:
                            product = (
                                product
                                * (gauss_nodes[i] - gauss_nodes[n])
                                / (gauss_nodes[j] - gauss_nodes[n])
                            )
                    summed = summed + product
            slopes[i, j] = summed
    end_values = [lagrange_at(-1.0), lagrange_at(1.0)]
    extrapolate = np.zeros((96, 64))
    lifting = np.zeros((64, 96))
    derivative = np.zeros((3, 64, 64))
    for p in range(64):
        point_idx = (p // 16, p // 4 % 4, p % 4)
        for f in range(6):
            normal_dir = f // 2
            across = [t for t in range(3) if t != normal_dir]
            q = point_idx[across[0]] * 4 + point_idx[across[1]]
            flux_row = q * 6 + f
            extrapolate[flux_row, p] = end_values[f % 2][point_idx[normal_dir]]
            lifting[p, flux_row] = (
                end_values[f % 2][point_idx[normal_dir]] / quad_weights[point_idx[normal_dir]]
            )
        for s in range(64):
            other_idx = (s // 16, s // 4 % 4, s % 4)
            for normal_dir in range(3):
                if all((point_idx[t] == other_idx[t] for t in range(3) if t != normal_dir)):
                    derivative[normal_dir, p, s] = slopes[
                        point_idx[normal_dir], other_idx[normal_dir]
                    ]
    return (
        jnp.asarray(extrapolate, dtype=jnp.float32),
        jnp.asarray(derivative, dtype=jnp.float32),
        jnp.asarray(lifting, dtype=jnp.float32),
    )


def face_rows(solution, face_speed, extrapolate):
    nvars = solution.shape[0]
    elems = solution.shape[2]
    ext_faces = extrapolate.reshape(16, 6, 64)
    values = jnp.einsum("qfp,vpe->feqv", ext_faces, solution, precision=lax.Precision.HIGHEST)
    values = values.reshape(6 * elems, 16, nvars)
    speeds = jnp.transpose(face_speed.reshape(16, 6, elems), (1, 2, 0)).reshape(6 * elems, 16)
    return (values, speeds)


def rim_rows(table_own, links, faces_total, rim_count):
    wanted = faces_total + jnp.arange(2 * rim_count, dtype=jnp.int32)
    hits = links[None, :] == wanted[:, None]
    faces = jnp.arange(faces_total, dtype=jnp.int32)[None, :]
    senders = jnp.sum(jnp.where(hits, faces, 0), axis=1)
    return jnp.take(table_own, senders, axis=0)


def split_bf16(x):
    hi = lax.reduce_precision(x, exponent_bits=8, mantissa_bits=7)
    return hi.astype(jnp.bfloat16), (x - hi).astype(jnp.bfloat16)


def pick_dot(rows, onehot):
    hi, lo = split_bf16(rows)
    out = jnp.dot(hi, onehot, preferred_element_type=jnp.float32)
    return out + jnp.dot(lo, onehot, preferred_element_type=jnp.float32)


def _rows_kernel(idx_ref, own_ref, recv_ref, out_ref, table_ref):
    own_rows = own_ref.shape[0]
    table_ref[pl.ds(0, own_rows), :] = own_ref[...]
    table_ref[pl.ds(own_rows, recv_ref.shape[0]), :] = recv_ref[...]

    def body(i, carry):
        base = pl.multiple_of(i * 16, 16)
        for j in range(16):
            row = idx_ref[base + j]
            out_ref[pl.ds(base + j, 1), :] = table_ref[pl.ds(row, 1), :]
        return carry

    lax.fori_loop(0, out_ref.shape[0] // 16, body, 0)


def take_rows(own, received, idx):
    rows = own.shape[0] + received.shape[0]
    return pl.pallas_call(
        _rows_kernel,
        out_shape=jax.ShapeDtypeStruct((idx.shape[0], own.shape[1]), own.dtype),
        in_specs=[
            pl.BlockSpec(memory_space=pltpu.SMEM),
            pl.BlockSpec(memory_space=pltpu.VMEM),
            pl.BlockSpec(memory_space=pltpu.VMEM),
        ],
        out_specs=pl.BlockSpec(memory_space=pltpu.VMEM),
        scratch_shapes=[pltpu.VMEM((rows, own.shape[1]), own.dtype)],
        cost_estimate=pl.CostEstimate(
            flops=0, transcendentals=0, bytes_accessed=(2 * idx.shape[0] + rows) * own.shape[1] * 4
        ),
    )(idx, own, received)


def owner_ranks(owners, buckets):
    receptors = owners.shape[0]
    width = 128
    blocks = receptors // width
    member = owners[None, :] == jnp.arange(buckets, dtype=jnp.int32)[:, None]
    member = member.astype(jnp.bfloat16).reshape(buckets * blocks, width)
    upper = jnp.asarray(np.triu(np.ones((width, width))), jnp.bfloat16)
    inside = jnp.dot(member, upper, preferred_element_type=jnp.float32)
    inside = inside.reshape(buckets, blocks, width)
    totals = inside[:, :, width - 1].astype(jnp.bfloat16)
    strict = jnp.asarray(np.triu(np.ones((blocks, blocks)), 1), jnp.bfloat16)
    offsets = jnp.dot(totals, strict, preferred_element_type=jnp.float32)
    counts = (inside + offsets[:, :, None]).reshape(buckets, receptors)
    picked = jnp.sum(jnp.where(member.reshape(buckets, receptors) > 0, counts, 0.0), axis=0)
    return picked.astype(jnp.int32) - 1


def surface_term(values, speeds, table_own, links, received, lifting, elems):
    nvars = values.shape[2]
    outer = take_rows(table_own, received, links)
    outer_vals = outer[:, : 16 * nvars].reshape(6 * elems, 16, nvars)
    outer_speed = outer[:, 16 * nvars :][:, :, None]
    own_speed = speeds[:, :, None]
    normal = 0.5 * (own_speed - outer_speed)
    common = 0.5 * normal * (values + outer_vals) + 0.5 * jnp.abs(normal) * (values - outer_vals)
    jump_term = (common - own_speed * values).reshape(6, elems, 16, nvars)
    lift_faces = lifting.reshape(64, 16, 6)
    return jnp.einsum("pqf,feqv->vpe", lift_faces, jump_term, precision=lax.Precision.HIGHEST)


def volume_term(solution, velocity, derivative):
    slopes = jnp.einsum("dpq,vqe->dvpe", derivative, solution, precision=lax.Precision.HIGHEST)
    return jnp.sum(velocity[:, None, None, :] * slopes, axis=0)


def receptor_rows(advanced, donors, coords):
    nvars = advanced.shape[0]
    elems = advanced.shape[2]
    basis_x = jnp.stack(lagrange_at(coords[0]))
    basis_y = jnp.stack(lagrange_at(coords[1]))
    basis_z = jnp.stack(lagrange_at(coords[2]))
    weights = (
        basis_x[:, None, None, :] * basis_y[None, :, None, :] * basis_z[None, None, :, :]
    ).reshape(64, -1)
    onehot = (jnp.arange(elems, dtype=jnp.int32)[:, None] == donors[None, :]).astype(jnp.bfloat16)
    picked = pick_dot(advanced.reshape(nvars * 64, elems), onehot).reshape(nvars, 64, -1)
    return jnp.sum(picked * weights[None], axis=1)


def on_device(
    solution, velocity, inv_jacobian, face_speed, face_link, donor_elem, ref_coords, owner_list
):
    extrapolate, derivative, lifting = tables()
    nvars = solution.shape[0]
    elems = solution.shape[2]
    rim_count = elems // 16
    faces_total = 6 * elems
    links = face_link.reshape(faces_total)
    values, speeds = face_rows(solution, face_speed, extrapolate)
    table_own = jnp.concatenate([values.reshape(faces_total, 16 * nvars), speeds], axis=1)
    outgoing = rim_rows(table_own, links, faces_total, rim_count)
    extended = padded(outgoing, (("valve", 0),), rim_count)
    received = jnp.concatenate([extended[:rim_count], extended[3 * rim_count :]], axis=0)
    surface = surface_term(values, speeds, table_own, links, received, lifting, elems)
    volume = volume_term(solution, velocity, derivative)
    section_rate = -inv_jacobian[None] * (volume + surface)
    advanced = solution + section_step * section_rate
    receptor_vals = receptor_rows(advanced, donor_elem, ref_coords)
    buckets = lax.axis_size("bulk")
    receptors = receptor_vals.shape[1]
    capacity = 2 * receptors // buckets
    owners = owner_list[:, 0]
    ranks = owner_ranks(owners, buckets)
    chosen = owners[:, None] == jnp.arange(buckets, dtype=jnp.int32)[None, :]
    masked = jnp.where(chosen[:, :, None], jnp.transpose(receptor_vals)[:, None, :], 0.0)
    hi, lo = split_bf16(masked.reshape(receptors, buckets * nvars))
    by_rank = (jnp.arange(capacity, dtype=jnp.int32)[:, None] == ranks[None, :]).astype(jnp.bfloat16)
    both = jnp.dot(by_rank, jnp.concatenate([hi, lo], axis=1), preferred_element_type=jnp.float32)
    placed = both[:, : buckets * nvars] + both[:, buckets * nvars :]
    send = jnp.transpose(placed.reshape(capacity, buckets, nvars), (1, 2, 0))
    side = 4
    across = [[z * side + x for x in range(side)] for z in range(buckets // side)]
    along = [[z * side + x for z in range(buckets // side)] for x in range(side)]
    stage = send.reshape(buckets // side, side, nvars, capacity)
    stage = lax.all_to_all(stage, "bulk", 1, 1, axis_index_groups=across, tiled=True)
    stage = lax.all_to_all(stage, "bulk", 0, 0, axis_index_groups=along, tiled=True)
    got = stage.reshape(buckets, nvars, capacity)
    fringe = jnp.transpose(got, (1, 0, 2)).reshape(nvars, buckets * capacity)
    return (section_rate, fringe)


def solution(mesh):
    placed = (
        P(None, None, ("valve", "bulk")),
        P(None, ("valve", "bulk")),
        P(None, ("valve", "bulk")),
        P(None, ("valve", "bulk")),
        P(None, ("valve", "bulk")),
        P(("valve", "bulk")),
        P(None, ("valve", "bulk")),
        P(("valve", "bulk"), None),
    )
    return jax.shard_map(
        on_device,
        mesh=mesh,
        in_specs=placed,
        out_specs=(P(None, None, ("valve", "bulk")), P(None, ("valve", "bulk"))),
        check_vma=False,
    )
```

```python
import jax
import jax.numpy as jnp
import numpy as np
from jax import lax
from jax.sharding import PartitionSpec as P
from jax.experimental import pallas as pl
from jax.experimental.pallas import tpu as pltpu

gauss_nodes = (-0.8611363115940526, -0.3399810435848563, 0.3399810435848563, 0.8611363115940526)
quad_weights = (0.3478548451374538, 0.6521451548625461, 0.6521451548625461, 0.3478548451374538)
section_step = 0.2


def padded(shard, sides, width):
    for axis, dim in sides:
        size, length = (lax.axis_size(axis), shard.shape[dim])
        up = [(i, (i + 1) % size) for i in range(size)]
        down = [(j, i) for i, j in up]
        last = lax.slice_in_dim(shard, length - width, length, axis=dim)
        initial = lax.slice_in_dim(shard, 0, width, axis=dim)
        before = lax.ppermute(last, axis, up)
        after = lax.ppermute(initial, axis, down)
        shard = jnp.concatenate([before, shard, after], axis=dim)
    return shard


def lagrange_at(x):
    values = []
    for j in range(4):
        factor = 1.0
        for m in range(4):
            if m != j:
                factor = factor * (x - gauss_nodes[m]) / (gauss_nodes[j] - gauss_nodes[m])
        values.append(factor)
    return values


def tables():
    slopes = np.zeros((4, 4))
    for i in range(4):
        for j in range(4):
            summed = 0.0
            for m in range(4):
                if m != j:
                    product = 1.0 / (gauss_nodes[j] - gauss_nodes[m])
                    for n in range(4):
                        if n != j and n != m:
                            product = (
                                product
                                * (gauss_nodes[i] - gauss_nodes[n])
                                / (gauss_nodes[j] - gauss_nodes[n])
                            )
                    summed = summed + product
            slopes[i, j] = summed
    end_values = [lagrange_at(-1.0), lagrange_at(1.0)]
    extrapolate = np.zeros((96, 64))
    lifting = np.zeros((64, 96))
    derivative = np.zeros((3, 64, 64))
    for p in range(64):
        point_idx = (p // 16, p // 4 % 4, p % 4)
        for f in range(6):
            normal_dir = f // 2
            across = [t for t in range(3) if t != normal_dir]
            q = point_idx[across[0]] * 4 + point_idx[across[1]]
            flux_row = q * 6 + f
            extrapolate[flux_row, p] = end_values[f % 2][point_idx[normal_dir]]
            lifting[p, flux_row] = (
                end_values[f % 2][point_idx[normal_dir]] / quad_weights[point_idx[normal_dir]]
            )
        for s in range(64):
            other_idx = (s // 16, s // 4 % 4, s % 4)
            for normal_dir in range(3):
                if all((point_idx[t] == other_idx[t] for t in range(3) if t != normal_dir)):
                    derivative[normal_dir, p, s] = slopes[
                        point_idx[normal_dir], other_idx[normal_dir]
                    ]
    return (
        jnp.asarray(extrapolate, dtype=jnp.float32),
        jnp.asarray(derivative, dtype=jnp.float32),
        jnp.asarray(lifting, dtype=jnp.float32),
    )


def face_rows(solution, face_speed, extrapolate):
    nvars = solution.shape[0]
    elems = solution.shape[2]
    ext_faces = extrapolate.reshape(16, 6, 64)
    values = jnp.einsum("qfp,vpe->feqv", ext_faces, solution, precision=lax.Precision.HIGHEST)
    values = values.reshape(6 * elems, 16, nvars)
    speeds = jnp.transpose(face_speed.reshape(16, 6, elems), (1, 2, 0)).reshape(6 * elems, 16)
    return (values, speeds)


def rim_rows(table_own, links, faces_total, rim_count):
    wanted = faces_total + jnp.arange(2 * rim_count, dtype=jnp.int32)
    hits = links[None, :] == wanted[:, None]
    faces = jnp.arange(faces_total, dtype=jnp.int32)[None, :]
    senders = jnp.sum(jnp.where(hits, faces, 0), axis=1)
    return jnp.take(table_own, senders, axis=0)


def split_bf16(x):
    hi = lax.reduce_precision(x, exponent_bits=8, mantissa_bits=7)
    return hi.astype(jnp.bfloat16), (x - hi).astype(jnp.bfloat16)


def pick_dot(rows, onehot):
    hi, lo = split_bf16(rows)
    out = jnp.dot(hi, onehot, preferred_element_type=jnp.float32)
    return out + jnp.dot(lo, onehot, preferred_element_type=jnp.float32)


def _rows_kernel(idx_ref, own_ref, recv_ref, out_ref, table_ref):
    own_rows = own_ref.shape[0]
    table_ref[pl.ds(0, own_rows), :] = own_ref[...]
    table_ref[pl.ds(own_rows, recv_ref.shape[0]), :] = recv_ref[...]

    def body(i, carry):
        base = pl.multiple_of(i * 16, 16)
        for j in range(16):
            row = idx_ref[base + j]
            out_ref[pl.ds(base + j, 1), :] = table_ref[pl.ds(row, 1), :]
        return carry

    lax.fori_loop(0, out_ref.shape[0] // 16, body, 0)


def take_rows(own, received, idx):
    rows = own.shape[0] + received.shape[0]
    return pl.pallas_call(
        _rows_kernel,
        out_shape=jax.ShapeDtypeStruct((idx.shape[0], own.shape[1]), own.dtype),
        in_specs=[
            pl.BlockSpec(memory_space=pltpu.SMEM),
            pl.BlockSpec(memory_space=pltpu.VMEM),
            pl.BlockSpec(memory_space=pltpu.VMEM),
        ],
        out_specs=pl.BlockSpec(memory_space=pltpu.VMEM),
        scratch_shapes=[pltpu.VMEM((rows, own.shape[1]), own.dtype)],
        cost_estimate=pl.CostEstimate(
            flops=0, transcendentals=0, bytes_accessed=(2 * idx.shape[0] + rows) * own.shape[1] * 4
        ),
    )(idx, own, received)


def owner_ranks(owners, buckets):
    receptors = owners.shape[0]
    width = 128
    blocks = receptors // width
    member = owners[None, :] == jnp.arange(buckets, dtype=jnp.int32)[:, None]
    member = member.astype(jnp.bfloat16).reshape(buckets * blocks, width)
    upper = jnp.asarray(np.triu(np.ones((width, width))), jnp.bfloat16)
    inside = jnp.dot(member, upper, preferred_element_type=jnp.float32)
    inside = inside.reshape(buckets, blocks, width)
    totals = inside[:, :, width - 1].astype(jnp.bfloat16)
    strict = jnp.asarray(np.triu(np.ones((blocks, blocks)), 1), jnp.bfloat16)
    offsets = jnp.dot(totals, strict, preferred_element_type=jnp.float32)
    counts = (inside + offsets[:, :, None]).reshape(buckets, receptors)
    picked = jnp.sum(jnp.where(member.reshape(buckets, receptors) > 0, counts, 0.0), axis=0)
    return picked.astype(jnp.int32) - 1


def surface_term(values, speeds, table_own, links, received, lifting, elems):
    nvars = values.shape[2]
    outer = take_rows(table_own, received, links)
    outer_vals = outer[:, : 16 * nvars].reshape(6 * elems, 16, nvars)
    outer_speed = outer[:, 16 * nvars :][:, :, None]
    own_speed = speeds[:, :, None]
    normal = 0.5 * (own_speed - outer_speed)
    common = 0.5 * normal * (values + outer_vals) + 0.5 * jnp.abs(normal) * (values - outer_vals)
    jump_term = (common - own_speed * values).reshape(6, elems, 16, nvars)
    lift_faces = lifting.reshape(64, 16, 6)
    return jnp.einsum("pqf,feqv->vpe", lift_faces, jump_term, precision=lax.Precision.HIGHEST)


def volume_term(solution, velocity, derivative):
    slopes = jnp.einsum("dpq,vqe->dvpe", derivative, solution, precision=lax.Precision.HIGHEST)
    return jnp.sum(velocity[:, None, None, :] * slopes, axis=0)


def receptor_rows(advanced, donors, coords):
    nvars = advanced.shape[0]
    elems = advanced.shape[2]
    basis_x = jnp.stack(lagrange_at(coords[0]))
    basis_y = jnp.stack(lagrange_at(coords[1]))
    basis_z = jnp.stack(lagrange_at(coords[2]))
    weights = (
        jnp.repeat(basis_x, 16, axis=0)
        * jnp.tile(jnp.repeat(basis_y, 4, axis=0), (4, 1))
        * jnp.tile(basis_z, (16, 1))
    )
    onehot = (jnp.arange(elems, dtype=jnp.int32)[:, None] == donors[None, :]).astype(jnp.bfloat16)
    picked = pick_dot(advanced.reshape(nvars * 64, elems), onehot).reshape(nvars, 64, -1)
    return jnp.sum(picked * weights[None], axis=1)


def on_device(
    solution, velocity, inv_jacobian, face_speed, face_link, donor_elem, ref_coords, owner_list
):
    extrapolate, derivative, lifting = tables()
    nvars = solution.shape[0]
    elems = solution.shape[2]
    rim_count = elems // 16
    faces_total = 6 * elems
    links = face_link.reshape(faces_total)
    values, speeds = face_rows(solution, face_speed, extrapolate)
    table_own = jnp.concatenate([values.reshape(faces_total, 16 * nvars), speeds], axis=1)
    outgoing = rim_rows(table_own, links, faces_total, rim_count)
    extended = padded(outgoing, (("valve", 0),), rim_count)
    received = jnp.concatenate([extended[:rim_count], extended[3 * rim_count :]], axis=0)
    surface = surface_term(values, speeds, table_own, links, received, lifting, elems)
    volume = volume_term(solution, velocity, derivative)
    section_rate = -inv_jacobian[None] * (volume + surface)
    advanced = solution + section_step * section_rate
    receptor_vals = receptor_rows(advanced, donor_elem, ref_coords)
    buckets = lax.axis_size("bulk")
    receptors = receptor_vals.shape[1]
    capacity = 2 * receptors // buckets
    owners = owner_list[:, 0]
    ranks = owner_ranks(owners, buckets)
    chosen = owners[:, None] == jnp.arange(buckets, dtype=jnp.int32)[None, :]
    masked = jnp.where(chosen[:, :, None], jnp.transpose(receptor_vals)[:, None, :], 0.0)
    hi, lo = split_bf16(masked.reshape(receptors, buckets * nvars))
    by_rank = (jnp.arange(capacity, dtype=jnp.int32)[:, None] == ranks[None, :]).astype(jnp.bfloat16)
    both = jnp.dot(by_rank, jnp.concatenate([hi, lo], axis=1), preferred_element_type=jnp.float32)
    placed = both[:, : buckets * nvars] + both[:, buckets * nvars :]
    send = jnp.transpose(placed.reshape(capacity, buckets, nvars), (1, 2, 0))
    got = lax.all_to_all(send, "bulk", 0, 0, tiled=True)
    fringe = jnp.transpose(got, (1, 0, 2)).reshape(nvars, buckets * capacity)
    return (section_rate, fringe)


def solution(mesh):
    placed = (
        P(None, None, ("valve", "bulk")),
        P(None, ("valve", "bulk")),
        P(None, ("valve", "bulk")),
        P(None, ("valve", "bulk")),
        P(None, ("valve", "bulk")),
        P(("valve", "bulk")),
        P(None, ("valve", "bulk")),
        P(("valve", "bulk"), None),
    )
    return jax.shard_map(
        on_device,
        mesh=mesh,
        in_specs=placed,
        out_specs=(P(None, None, ("valve", "bulk")), P(None, ("valve", "bulk"))),
        check_vma=False,
    )
```

```python
import jax
import jax.numpy as jnp
import numpy as np
from jax import lax
from jax.sharding import PartitionSpec as P
from jax.experimental import pallas as pl
from jax.experimental.pallas import tpu as pltpu

gauss_nodes = (-0.8611363115940526, -0.3399810435848563, 0.3399810435848563, 0.8611363115940526)
quad_weights = (0.3478548451374538, 0.6521451548625461, 0.6521451548625461, 0.3478548451374538)
section_step = 0.2


def padded(shard, sides, width):
    for axis, dim in sides:
        size, length = (lax.axis_size(axis), shard.shape[dim])
        up = [(i, (i + 1) % size) for i in range(size)]
        down = [(j, i) for i, j in up]
        last = lax.slice_in_dim(shard, length - width, length, axis=dim)
        initial = lax.slice_in_dim(shard, 0, width, axis=dim)
        before = lax.ppermute(last, axis, up)
        after = lax.ppermute(initial, axis, down)
        shard = jnp.concatenate([before, shard, after], axis=dim)
    return shard


def lagrange_at(x):
    values = []
    for j in range(4):
        factor = 1.0
        for m in range(4):
            if m != j:
                factor = factor * (x - gauss_nodes[m]) / (gauss_nodes[j] - gauss_nodes[m])
        values.append(factor)
    return values


def tables_np():
    slopes = np.zeros((4, 4))
    for i in range(4):
        for j in range(4):
            summed = 0.0
            for m in range(4):
                if m != j:
                    product = 1.0 / (gauss_nodes[j] - gauss_nodes[m])
                    for n in range(4):
                        if n != j and n != m:
                            product = (
                                product
                                * (gauss_nodes[i] - gauss_nodes[n])
                                / (gauss_nodes[j] - gauss_nodes[n])
                            )
                    summed = summed + product
            slopes[i, j] = summed
    end_values = [lagrange_at(-1.0), lagrange_at(1.0)]
    extrapolate = np.zeros((96, 64))
    lifting = np.zeros((64, 96))
    derivative = np.zeros((3, 64, 64))
    for p in range(64):
        point_idx = (p // 16, p // 4 % 4, p % 4)
        for f in range(6):
            normal_dir = f // 2
            across = [t for t in range(3) if t != normal_dir]
            q = point_idx[across[0]] * 4 + point_idx[across[1]]
            flux_row = q * 6 + f
            extrapolate[flux_row, p] = end_values[f % 2][point_idx[normal_dir]]
            lifting[p, flux_row] = (
                end_values[f % 2][point_idx[normal_dir]] / quad_weights[point_idx[normal_dir]]
            )
        for s in range(64):
            other_idx = (s // 16, s // 4 % 4, s % 4)
            for normal_dir in range(3):
                if all((point_idx[t] == other_idx[t] for t in range(3) if t != normal_dir)):
                    derivative[normal_dir, p, s] = slopes[
                        point_idx[normal_dir], other_idx[normal_dir]
                    ]
    return (extrapolate, derivative, lifting)


def tables():
    extrapolate, derivative, lifting = tables_np()
    return (
        jnp.asarray(extrapolate, dtype=jnp.float32),
        jnp.asarray(derivative, dtype=jnp.float32),
        jnp.asarray(lifting, dtype=jnp.float32),
    )


def face_mats(nvars):
    extrapolate, _, lifting = tables_np()
    ext = np.transpose(extrapolate.reshape(16, 6, 64), (1, 2, 0))
    lift = np.transpose(lifting.reshape(64, 16, 6), (2, 0, 1))
    ext, lift = lax.optimization_barrier(
        (jnp.asarray(ext, jnp.float32), jnp.asarray(lift, jnp.float32))
    )
    eye = jnp.eye(nvars, dtype=jnp.float32)
    pad = ((0, 0), (0, 0), (0, 128 - 16 * nvars))
    values = (ext[:, None, :, :, None] * eye[None, :, None, None, :]).reshape(6, nvars * 64, 16 * nvars)
    lifts = (lift[:, None, :, :, None] * eye[None, :, None, None, :]).reshape(6, nvars * 64, 16 * nvars)
    rows = jnp.arange(96, dtype=jnp.int32)
    cols = jnp.arange(16 * nvars, dtype=jnp.int32)
    faces = jnp.arange(6, dtype=jnp.int32)
    speeds = rows[None, :, None] == 6 * (cols[None, None, :] // nvars) + faces[:, None, None]
    speeds = speeds.astype(jnp.float32)
    return tuple(jnp.pad(m, pad) for m in (values, speeds, lifts))


def face_rows(solution, face_speed, value_mat, speed_mat):
    nvars, _, elems = solution.shape
    flat = solution.reshape(nvars * 64, elems)
    values = jnp.einsum("ie,fij->fej", flat, value_mat, precision=lax.Precision.HIGHEST)
    speeds = jnp.einsum("ie,fij->fej", face_speed, speed_mat, precision=lax.Precision.HIGHEST)
    return values.reshape(6 * elems, 128), speeds.reshape(6 * elems, 128)


def rim_rows(values, speeds, links, faces_total, rim_count):
    wanted = faces_total + jnp.arange(2 * rim_count, dtype=jnp.int32)
    hits = links[None, :] == wanted[:, None]
    faces = jnp.arange(faces_total, dtype=jnp.int32)[None, :]
    senders = jnp.sum(jnp.where(hits, faces, 0), axis=1)
    return jnp.concatenate(
        [jnp.take(values, senders, axis=0), jnp.take(speeds, senders, axis=0)], axis=1
    )


def split_bf16(x):
    hi = lax.reduce_precision(x, exponent_bits=8, mantissa_bits=7)
    return hi.astype(jnp.bfloat16), (x - hi).astype(jnp.bfloat16)


def pick_dot(rows, onehot):
    hi, lo = split_bf16(rows)
    out = jnp.dot(hi, onehot, preferred_element_type=jnp.float32)
    return out + jnp.dot(lo, onehot, preferred_element_type=jnp.float32)


def _rows_kernel(idx_ref, values_ref, speeds_ref, recv_ref, out_ref, table_ref):
    own_rows, width = values_ref.shape
    table_ref[pl.ds(0, own_rows), pl.ds(0, width)] = values_ref[...]
    table_ref[pl.ds(0, own_rows), pl.ds(width, width)] = speeds_ref[...]
    table_ref[pl.ds(own_rows, recv_ref.shape[0]), :] = recv_ref[...]

    def body(i, carry):
        base = pl.multiple_of(i * 16, 16)
        for j in range(16):
            row = idx_ref[base + j]
            out_ref[pl.ds(base + j, 1), :] = table_ref[pl.ds(row, 1), :]
        return carry

    lax.fori_loop(0, out_ref.shape[0] // 16, body, 0)


def take_rows(values, speeds, received, idx):
    rows = values.shape[0] + received.shape[0]
    width = received.shape[1]
    return pl.pallas_call(
        _rows_kernel,
        out_shape=jax.ShapeDtypeStruct((idx.shape[0], width), values.dtype),
        in_specs=[
            pl.BlockSpec(memory_space=pltpu.SMEM),
            pl.BlockSpec(memory_space=pltpu.VMEM),
            pl.BlockSpec(memory_space=pltpu.VMEM),
            pl.BlockSpec(memory_space=pltpu.VMEM),
        ],
        out_specs=pl.BlockSpec(memory_space=pltpu.VMEM),
        scratch_shapes=[pltpu.VMEM((rows, width), values.dtype)],
        cost_estimate=pl.CostEstimate(
            flops=0, transcendentals=0, bytes_accessed=(2 * idx.shape[0] + rows) * width * 4
        ),
    )(idx, values, speeds, received)


def owner_ranks(owners, buckets):
    receptors = owners.shape[0]
    width = 128
    blocks = receptors // width
    member = owners[None, :] == jnp.arange(buckets, dtype=jnp.int32)[:, None]
    member = member.astype(jnp.bfloat16).reshape(buckets * blocks, width)
    upper = jnp.asarray(np.triu(np.ones((width, width))), jnp.bfloat16)
    inside = jnp.dot(member, upper, preferred_element_type=jnp.float32)
    inside = inside.reshape(buckets, blocks, width)
    totals = inside[:, :, width - 1].astype(jnp.bfloat16)
    strict = jnp.asarray(np.triu(np.ones((blocks, blocks)), 1), jnp.bfloat16)
    offsets = jnp.dot(totals, strict, preferred_element_type=jnp.float32)
    counts = (inside + offsets[:, :, None]).reshape(buckets, receptors)
    picked = jnp.sum(jnp.where(member.reshape(buckets, receptors) > 0, counts, 0.0), axis=0)
    return picked.astype(jnp.int32) - 1


def surface_term(values, speeds, links, received, lift_mat, nvars, elems):
    outer = take_rows(values, speeds, received, links)
    outer_vals = outer[:, :128]
    outer_speed = outer[:, 128:]
    normal = 0.5 * (speeds - outer_speed)
    common = 0.5 * normal * (values + outer_vals) + 0.5 * jnp.abs(normal) * (values - outer_vals)
    jump_term = (common - speeds * values).reshape(6, elems, 128)
    lifted = jnp.einsum("fel,fil->ie", jump_term, lift_mat, precision=lax.Precision.HIGHEST)
    return lifted.reshape(nvars, 64, elems)


def volume_term(solution, velocity, derivative):
    slopes = jnp.einsum("dpq,vqe->dvpe", derivative, solution, precision=lax.Precision.HIGHEST)
    return jnp.sum(velocity[:, None, None, :] * slopes, axis=0)


def receptor_rows(advanced, donors, coords):
    nvars = advanced.shape[0]
    elems = advanced.shape[2]
    basis_x = jnp.stack(lagrange_at(coords[0]))
    basis_y = jnp.stack(lagrange_at(coords[1]))
    basis_z = jnp.stack(lagrange_at(coords[2]))
    weights = (
        jnp.repeat(basis_x, 16, axis=0)
        * jnp.tile(jnp.repeat(basis_y, 4, axis=0), (4, 1))
        * jnp.tile(basis_z, (16, 1))
    )
    onehot = (jnp.arange(elems, dtype=jnp.int32)[:, None] == donors[None, :]).astype(jnp.bfloat16)
    picked = pick_dot(advanced.reshape(nvars * 64, elems), onehot).reshape(nvars, 64, -1)
    return jnp.sum(picked * weights[None], axis=1)


def on_device(
    solution, velocity, inv_jacobian, face_speed, face_link, donor_elem, ref_coords, owner_list
):
    extrapolate, derivative, lifting = tables()
    nvars = solution.shape[0]
    elems = solution.shape[2]
    rim_count = elems // 16
    faces_total = 6 * elems
    links = face_link.reshape(faces_total)
    value_mat, speed_mat, lift_mat = face_mats(nvars)
    values, speeds = face_rows(solution, face_speed, value_mat, speed_mat)
    outgoing = rim_rows(values, speeds, links, faces_total, rim_count)
    extended = padded(outgoing, (("valve", 0),), rim_count)
    received = jnp.concatenate([extended[:rim_count], extended[3 * rim_count :]], axis=0)
    surface = surface_term(values, speeds, links, received, lift_mat, nvars, elems)
    volume = volume_term(solution, velocity, derivative)
    section_rate = -inv_jacobian[None] * (volume + surface)
    advanced = solution + section_step * section_rate
    receptor_vals = receptor_rows(advanced, donor_elem, ref_coords)
    buckets = lax.axis_size("bulk")
    receptors = receptor_vals.shape[1]
    capacity = 2 * receptors // buckets
    owners = owner_list[:, 0]
    ranks = owner_ranks(owners, buckets)
    chosen = owners[:, None] == jnp.arange(buckets, dtype=jnp.int32)[None, :]
    masked = jnp.where(chosen[:, :, None], jnp.transpose(receptor_vals)[:, None, :], 0.0)
    hi, lo = split_bf16(masked.reshape(receptors, buckets * nvars))
    by_rank = (jnp.arange(capacity, dtype=jnp.int32)[:, None] == ranks[None, :]).astype(jnp.bfloat16)
    both = jnp.dot(by_rank, jnp.concatenate([hi, lo], axis=1), preferred_element_type=jnp.float32)
    placed = both[:, : buckets * nvars] + both[:, buckets * nvars :]
    send = jnp.transpose(placed.reshape(capacity, buckets, nvars), (1, 2, 0))
    got = lax.all_to_all(send, "bulk", 0, 0, tiled=True)
    fringe = jnp.transpose(got, (1, 0, 2)).reshape(nvars, buckets * capacity)
    return (section_rate, fringe)


def solution(mesh):
    placed = (
        P(None, None, ("valve", "bulk")),
        P(None, ("valve", "bulk")),
        P(None, ("valve", "bulk")),
        P(None, ("valve", "bulk")),
        P(None, ("valve", "bulk")),
        P(("valve", "bulk")),
        P(None, ("valve", "bulk")),
        P(("valve", "bulk"), None),
    )
    return jax.shard_map(
        on_device,
        mesh=mesh,
        in_specs=placed,
        out_specs=(P(None, None, ("valve", "bulk")), P(None, ("valve", "bulk"))),
        check_vma=False,
    )
```

```python
import jax
import jax.numpy as jnp
import numpy as np
from jax import lax
from jax.sharding import PartitionSpec as P
from jax.experimental import pallas as pl
from jax.experimental.pallas import tpu as pltpu

gauss_nodes = (-0.8611363115940526, -0.3399810435848563, 0.3399810435848563, 0.8611363115940526)
quad_weights = (0.3478548451374538, 0.6521451548625461, 0.6521451548625461, 0.3478548451374538)
section_step = 0.2


def padded(shard, sides, width):
    for axis, dim in sides:
        size, length = (lax.axis_size(axis), shard.shape[dim])
        up = [(i, (i + 1) % size) for i in range(size)]
        down = [(j, i) for i, j in up]
        last = lax.slice_in_dim(shard, length - width, length, axis=dim)
        initial = lax.slice_in_dim(shard, 0, width, axis=dim)
        before = lax.ppermute(last, axis, up)
        after = lax.ppermute(initial, axis, down)
        shard = jnp.concatenate([before, shard, after], axis=dim)
    return shard


def lagrange_at(x):
    values = []
    for j in range(4):
        factor = 1.0
        for m in range(4):
            if m != j:
                factor = factor * (x - gauss_nodes[m]) / (gauss_nodes[j] - gauss_nodes[m])
        values.append(factor)
    return values


def tables_np():
    slopes = np.zeros((4, 4))
    for i in range(4):
        for j in range(4):
            summed = 0.0
            for m in range(4):
                if m != j:
                    product = 1.0 / (gauss_nodes[j] - gauss_nodes[m])
                    for n in range(4):
                        if n != j and n != m:
                            product = (
                                product
                                * (gauss_nodes[i] - gauss_nodes[n])
                                / (gauss_nodes[j] - gauss_nodes[n])
                            )
                    summed = summed + product
            slopes[i, j] = summed
    end_values = [lagrange_at(-1.0), lagrange_at(1.0)]
    extrapolate = np.zeros((96, 64))
    lifting = np.zeros((64, 96))
    derivative = np.zeros((3, 64, 64))
    for p in range(64):
        point_idx = (p // 16, p // 4 % 4, p % 4)
        for f in range(6):
            normal_dir = f // 2
            across = [t for t in range(3) if t != normal_dir]
            q = point_idx[across[0]] * 4 + point_idx[across[1]]
            flux_row = q * 6 + f
            extrapolate[flux_row, p] = end_values[f % 2][point_idx[normal_dir]]
            lifting[p, flux_row] = (
                end_values[f % 2][point_idx[normal_dir]] / quad_weights[point_idx[normal_dir]]
            )
        for s in range(64):
            other_idx = (s // 16, s // 4 % 4, s % 4)
            for normal_dir in range(3):
                if all((point_idx[t] == other_idx[t] for t in range(3) if t != normal_dir)):
                    derivative[normal_dir, p, s] = slopes[
                        point_idx[normal_dir], other_idx[normal_dir]
                    ]
    return (extrapolate, derivative, lifting)


def tables():
    extrapolate, derivative, lifting = tables_np()
    return (
        jnp.asarray(extrapolate, dtype=jnp.float32),
        jnp.asarray(derivative, dtype=jnp.float32),
        jnp.asarray(lifting, dtype=jnp.float32),
    )


def lift_mats(nvars):
    _, _, lifting = tables_np()
    spread = np.zeros((16 * (nvars + 1), 16 * nvars))
    for q in range(16):
        spread[16 * nvars + q, q * nvars : (q + 1) * nvars] = 1.0
    lift = np.transpose(lifting.reshape(64, 16, 6), (2, 0, 1))
    lift = lax.optimization_barrier(jnp.asarray(lift, jnp.float32))
    eye = jnp.eye(nvars, dtype=jnp.float32)
    lifts = (lift[:, None, :, :, None] * eye[None, :, None, None, :]).reshape(6, nvars * 64, 16 * nvars)
    return jnp.asarray(spread, jnp.float32), lifts


def face_rows(solution, face_speed, extrapolate):
    nvars = solution.shape[0]
    elems = solution.shape[2]
    ext_faces = extrapolate.reshape(16, 6, 64)
    values = jnp.einsum("qfp,vpe->feqv", ext_faces, solution, precision=lax.Precision.HIGHEST)
    values = values.reshape(6 * elems, 16, nvars)
    speeds = jnp.transpose(face_speed.reshape(16, 6, elems), (1, 2, 0)).reshape(6 * elems, 16)
    return (values, speeds)


def rim_rows(table_own, links, faces_total, rim_count):
    wanted = faces_total + jnp.arange(2 * rim_count, dtype=jnp.int32)
    hits = links[None, :] == wanted[:, None]
    faces = jnp.arange(faces_total, dtype=jnp.int32)[None, :]
    senders = jnp.sum(jnp.where(hits, faces, 0), axis=1)
    return jnp.take(table_own, senders, axis=0)


def split_bf16(x):
    hi = lax.reduce_precision(x, exponent_bits=8, mantissa_bits=7)
    return hi.astype(jnp.bfloat16), (x - hi).astype(jnp.bfloat16)


def pick_dot(rows, onehot):
    hi, lo = split_bf16(rows)
    out = jnp.dot(hi, onehot, preferred_element_type=jnp.float32)
    return out + jnp.dot(lo, onehot, preferred_element_type=jnp.float32)


def _rows_kernel(idx_ref, own_ref, recv_ref, out_ref, table_ref):
    own_rows = own_ref.shape[0]
    table_ref[pl.ds(0, own_rows), :] = own_ref[...]
    table_ref[pl.ds(own_rows, recv_ref.shape[0]), :] = recv_ref[...]

    def body(i, carry):
        base = pl.multiple_of(i * 16, 16)
        for j in range(16):
            row = idx_ref[base + j]
            out_ref[pl.ds(base + j, 1), :] = table_ref[pl.ds(row, 1), :]
        return carry

    lax.fori_loop(0, out_ref.shape[0] // 16, body, 0)


def take_rows(own, received, idx):
    rows = own.shape[0] + received.shape[0]
    return pl.pallas_call(
        _rows_kernel,
        out_shape=jax.ShapeDtypeStruct((idx.shape[0], own.shape[1]), own.dtype),
        in_specs=[
            pl.BlockSpec(memory_space=pltpu.SMEM),
            pl.BlockSpec(memory_space=pltpu.VMEM),
            pl.BlockSpec(memory_space=pltpu.VMEM),
        ],
        out_specs=pl.BlockSpec(memory_space=pltpu.VMEM),
        scratch_shapes=[pltpu.VMEM((rows, own.shape[1]), own.dtype)],
        cost_estimate=pl.CostEstimate(
            flops=0, transcendentals=0, bytes_accessed=(2 * idx.shape[0] + rows) * own.shape[1] * 4
        ),
    )(idx, own, received)


def owner_ranks(owners, buckets):
    receptors = owners.shape[0]
    width = 128
    blocks = receptors // width
    member = owners[None, :] == jnp.arange(buckets, dtype=jnp.int32)[:, None]
    member = member.astype(jnp.bfloat16).reshape(buckets * blocks, width)
    upper = jnp.asarray(np.triu(np.ones((width, width))), jnp.bfloat16)
    inside = jnp.dot(member, upper, preferred_element_type=jnp.float32)
    inside = inside.reshape(buckets, blocks, width)
    totals = inside[:, :, width - 1].astype(jnp.bfloat16)
    strict = jnp.asarray(np.triu(np.ones((blocks, blocks)), 1), jnp.bfloat16)
    offsets = jnp.dot(totals, strict, preferred_element_type=jnp.float32)
    counts = (inside + offsets[:, :, None]).reshape(buckets, receptors)
    picked = jnp.sum(jnp.where(member.reshape(buckets, receptors) > 0, counts, 0.0), axis=0)
    return picked.astype(jnp.int32) - 1


def surface_term(table_own, links, received, nvars, elems):
    spread, lifts = lift_mats(nvars)
    width = 16 * nvars
    outer = take_rows(table_own, received, links)
    own_speed = jnp.dot(table_own, spread, precision=lax.Precision.HIGHEST)
    outer_speed = jnp.dot(outer, spread, precision=lax.Precision.HIGHEST)
    values = table_own[:, :width]
    outer_vals = outer[:, :width]
    normal = 0.5 * (own_speed - outer_speed)
    common = 0.5 * normal * (values + outer_vals) + 0.5 * jnp.abs(normal) * (values - outer_vals)
    jump_term = (common - own_speed * values).reshape(6, elems, width)
    lifted = jnp.einsum("fel,fil->ie", jump_term, lifts, precision=lax.Precision.HIGHEST)
    return lifted.reshape(nvars, 64, elems)


def volume_term(solution, velocity, derivative):
    slopes = jnp.einsum("dpq,vqe->dvpe", derivative, solution, precision=lax.Precision.HIGHEST)
    return jnp.sum(velocity[:, None, None, :] * slopes, axis=0)


def receptor_rows(advanced, donors, coords):
    nvars = advanced.shape[0]
    elems = advanced.shape[2]
    basis_x = jnp.stack(lagrange_at(coords[0]))
    basis_y = jnp.stack(lagrange_at(coords[1]))
    basis_z = jnp.stack(lagrange_at(coords[2]))
    weights = (
        jnp.repeat(basis_x, 16, axis=0)
        * jnp.tile(jnp.repeat(basis_y, 4, axis=0), (4, 1))
        * jnp.tile(basis_z, (16, 1))
    )
    onehot = (jnp.arange(elems, dtype=jnp.int32)[:, None] == donors[None, :]).astype(jnp.bfloat16)
    picked = pick_dot(advanced.reshape(nvars * 64, elems), onehot).reshape(nvars, 64, -1)
    return jnp.sum(picked * weights[None], axis=1)


def on_device(
    solution, velocity, inv_jacobian, face_speed, face_link, donor_elem, ref_coords, owner_list
):
    extrapolate, derivative, lifting = tables()
    nvars = solution.shape[0]
    elems = solution.shape[2]
    rim_count = elems // 16
    faces_total = 6 * elems
    links = face_link.reshape(faces_total)
    values, speeds = face_rows(solution, face_speed, extrapolate)
    table_own = jnp.concatenate([values.reshape(faces_total, 16 * nvars), speeds], axis=1)
    outgoing = rim_rows(table_own, links, faces_total, rim_count)
    extended = padded(outgoing, (("valve", 0),), rim_count)
    received = jnp.concatenate([extended[:rim_count], extended[3 * rim_count :]], axis=0)
    surface = surface_term(table_own, links, received, nvars, elems)
    volume = volume_term(solution, velocity, derivative)
    section_rate = -inv_jacobian[None] * (volume + surface)
    advanced = solution + section_step * section_rate
    receptor_vals = receptor_rows(advanced, donor_elem, ref_coords)
    buckets = lax.axis_size("bulk")
    receptors = receptor_vals.shape[1]
    capacity = 2 * receptors // buckets
    owners = owner_list[:, 0]
    ranks = owner_ranks(owners, buckets)
    chosen = owners[:, None] == jnp.arange(buckets, dtype=jnp.int32)[None, :]
    masked = jnp.where(chosen[:, :, None], jnp.transpose(receptor_vals)[:, None, :], 0.0)
    hi, lo = split_bf16(masked.reshape(receptors, buckets * nvars))
    by_rank = (jnp.arange(capacity, dtype=jnp.int32)[:, None] == ranks[None, :]).astype(jnp.bfloat16)
    both = jnp.dot(by_rank, jnp.concatenate([hi, lo], axis=1), preferred_element_type=jnp.float32)
    placed = both[:, : buckets * nvars] + both[:, buckets * nvars :]
    send = jnp.transpose(placed.reshape(capacity, buckets, nvars), (1, 2, 0))
    got = lax.all_to_all(send, "bulk", 0, 0, tiled=True)
    fringe = jnp.transpose(got, (1, 0, 2)).reshape(nvars, buckets * capacity)
    return (section_rate, fringe)


def solution(mesh):
    placed = (
        P(None, None, ("valve", "bulk")),
        P(None, ("valve", "bulk")),
        P(None, ("valve", "bulk")),
        P(None, ("valve", "bulk")),
        P(None, ("valve", "bulk")),
        P(("valve", "bulk")),
        P(None, ("valve", "bulk")),
        P(("valve", "bulk"), None),
    )
    return jax.shard_map(
        on_device,
        mesh=mesh,
        in_specs=placed,
        out_specs=(P(None, None, ("valve", "bulk")), P(None, ("valve", "bulk"))),
        check_vma=False,
    )
```

```python
import jax
import jax.numpy as jnp
import numpy as np
from jax import lax
from jax.sharding import PartitionSpec as P
from jax.experimental import pallas as pl
from jax.experimental.pallas import tpu as pltpu

gauss_nodes = (-0.8611363115940526, -0.3399810435848563, 0.3399810435848563, 0.8611363115940526)
quad_weights = (0.3478548451374538, 0.6521451548625461, 0.6521451548625461, 0.3478548451374538)
section_step = 0.2


def padded(shard, sides, width):
    for axis, dim in sides:
        size, length = (lax.axis_size(axis), shard.shape[dim])
        up = [(i, (i + 1) % size) for i in range(size)]
        down = [(j, i) for i, j in up]
        last = lax.slice_in_dim(shard, length - width, length, axis=dim)
        initial = lax.slice_in_dim(shard, 0, width, axis=dim)
        before = lax.ppermute(last, axis, up)
        after = lax.ppermute(initial, axis, down)
        shard = jnp.concatenate([before, shard, after], axis=dim)
    return shard


def lagrange_at(x):
    values = []
    for j in range(4):
        factor = 1.0
        for m in range(4):
            if m != j:
                factor = factor * (x - gauss_nodes[m]) / (gauss_nodes[j] - gauss_nodes[m])
        values.append(factor)
    return values


def tables_np():
    slopes = np.zeros((4, 4))
    for i in range(4):
        for j in range(4):
            summed = 0.0
            for m in range(4):
                if m != j:
                    product = 1.0 / (gauss_nodes[j] - gauss_nodes[m])
                    for n in range(4):
                        if n != j and n != m:
                            product = (
                                product
                                * (gauss_nodes[i] - gauss_nodes[n])
                                / (gauss_nodes[j] - gauss_nodes[n])
                            )
                    summed = summed + product
            slopes[i, j] = summed
    end_values = [lagrange_at(-1.0), lagrange_at(1.0)]
    extrapolate = np.zeros((96, 64))
    lifting = np.zeros((64, 96))
    derivative = np.zeros((3, 64, 64))
    for p in range(64):
        point_idx = (p // 16, p // 4 % 4, p % 4)
        for f in range(6):
            normal_dir = f // 2
            across = [t for t in range(3) if t != normal_dir]
            q = point_idx[across[0]] * 4 + point_idx[across[1]]
            flux_row = q * 6 + f
            extrapolate[flux_row, p] = end_values[f % 2][point_idx[normal_dir]]
            lifting[p, flux_row] = (
                end_values[f % 2][point_idx[normal_dir]] / quad_weights[point_idx[normal_dir]]
            )
        for s in range(64):
            other_idx = (s // 16, s // 4 % 4, s % 4)
            for normal_dir in range(3):
                if all((point_idx[t] == other_idx[t] for t in range(3) if t != normal_dir)):
                    derivative[normal_dir, p, s] = slopes[
                        point_idx[normal_dir], other_idx[normal_dir]
                    ]
    return (extrapolate, derivative, lifting)


def tables():
    extrapolate, derivative, lifting = tables_np()
    return (
        jnp.asarray(extrapolate, dtype=jnp.float32),
        jnp.asarray(derivative, dtype=jnp.float32),
        jnp.asarray(lifting, dtype=jnp.float32),
    )


def face_mat(nvars, f):
    extrapolate, _, _ = tables_np()
    mat = np.zeros((nvars * 64 + 96, 16 * (nvars + 1)))
    for q in range(16):
        for v in range(nvars):
            mat[v * 64 : (v + 1) * 64, q * nvars + v] = extrapolate[6 * q + f, :]
        mat[nvars * 64 + 6 * q + f, 16 * nvars + q] = 1.0
    return jnp.asarray(mat, jnp.float32)


def face_rows(solution, face_speed):
    nvars, _, elems = solution.shape
    rows = jnp.concatenate([solution.reshape(nvars * 64, elems), face_speed], axis=0)
    faces = [
        jnp.einsum("ie,ij->ej", rows, face_mat(nvars, f), precision=lax.Precision.HIGHEST)
        for f in range(6)
    ]
    table = jnp.concatenate(faces, axis=0)
    values = table[:, : 16 * nvars].reshape(6 * elems, 16, nvars)
    return table, values, table[:, 16 * nvars :]


def rim_rows(table_own, links, faces_total, rim_count):
    wanted = faces_total + jnp.arange(2 * rim_count, dtype=jnp.int32)
    hits = links[None, :] == wanted[:, None]
    faces = jnp.arange(faces_total, dtype=jnp.int32)[None, :]
    senders = jnp.sum(jnp.where(hits, faces, 0), axis=1)
    return jnp.take(table_own, senders, axis=0)


def split_bf16(x):
    hi = lax.reduce_precision(x, exponent_bits=8, mantissa_bits=7)
    return hi.astype(jnp.bfloat16), (x - hi).astype(jnp.bfloat16)


def pick_dot(rows, onehot):
    hi, lo = split_bf16(rows)
    out = jnp.dot(hi, onehot, preferred_element_type=jnp.float32)
    return out + jnp.dot(lo, onehot, preferred_element_type=jnp.float32)


def _rows_kernel(idx_ref, own_ref, recv_ref, out_ref, table_ref):
    own_rows = own_ref.shape[0]
    table_ref[pl.ds(0, own_rows), :] = own_ref[...]
    table_ref[pl.ds(own_rows, recv_ref.shape[0]), :] = recv_ref[...]

    def body(i, carry):
        base = pl.multiple_of(i * 16, 16)
        for j in range(16):
            row = idx_ref[base + j]
            out_ref[pl.ds(base + j, 1), :] = table_ref[pl.ds(row, 1), :]
        return carry

    lax.fori_loop(0, out_ref.shape[0] // 16, body, 0)


def take_rows(own, received, idx):
    rows = own.shape[0] + received.shape[0]
    return pl.pallas_call(
        _rows_kernel,
        out_shape=jax.ShapeDtypeStruct((idx.shape[0], own.shape[1]), own.dtype),
        in_specs=[
            pl.BlockSpec(memory_space=pltpu.SMEM),
            pl.BlockSpec(memory_space=pltpu.VMEM),
            pl.BlockSpec(memory_space=pltpu.VMEM),
        ],
        out_specs=pl.BlockSpec(memory_space=pltpu.VMEM),
        scratch_shapes=[pltpu.VMEM((rows, own.shape[1]), own.dtype)],
        cost_estimate=pl.CostEstimate(
            flops=0, transcendentals=0, bytes_accessed=(2 * idx.shape[0] + rows) * own.shape[1] * 4
        ),
    )(idx, own, received)


def owner_ranks(owners, buckets):
    receptors = owners.shape[0]
    width = 128
    blocks = receptors // width
    member = owners[None, :] == jnp.arange(buckets, dtype=jnp.int32)[:, None]
    member = member.astype(jnp.bfloat16).reshape(buckets * blocks, width)
    upper = jnp.asarray(np.triu(np.ones((width, width))), jnp.bfloat16)
    inside = jnp.dot(member, upper, preferred_element_type=jnp.float32)
    inside = inside.reshape(buckets, blocks, width)
    totals = inside[:, :, width - 1].astype(jnp.bfloat16)
    strict = jnp.asarray(np.triu(np.ones((blocks, blocks)), 1), jnp.bfloat16)
    offsets = jnp.dot(totals, strict, preferred_element_type=jnp.float32)
    counts = (inside + offsets[:, :, None]).reshape(buckets, receptors)
    picked = jnp.sum(jnp.where(member.reshape(buckets, receptors) > 0, counts, 0.0), axis=0)
    return picked.astype(jnp.int32) - 1


def surface_term(values, speeds, table_own, links, received, lifting, elems):
    nvars = values.shape[2]
    outer = take_rows(table_own, received, links)
    outer_vals = outer[:, : 16 * nvars].reshape(6 * elems, 16, nvars)
    outer_speed = outer[:, 16 * nvars :][:, :, None]
    own_speed = speeds[:, :, None]
    normal = 0.5 * (own_speed - outer_speed)
    common = 0.5 * normal * (values + outer_vals) + 0.5 * jnp.abs(normal) * (values - outer_vals)
    jump_term = (common - own_speed * values).reshape(6, elems, 16, nvars)
    lift_faces = lifting.reshape(64, 16, 6)
    return jnp.einsum("pqf,feqv->vpe", lift_faces, jump_term, precision=lax.Precision.HIGHEST)


def volume_term(solution, velocity, derivative):
    slopes = jnp.einsum("dpq,vqe->dvpe", derivative, solution, precision=lax.Precision.HIGHEST)
    return jnp.sum(velocity[:, None, None, :] * slopes, axis=0)


def receptor_rows(advanced, donors, coords):
    nvars = advanced.shape[0]
    elems = advanced.shape[2]
    basis_x = jnp.stack(lagrange_at(coords[0]))
    basis_y = jnp.stack(lagrange_at(coords[1]))
    basis_z = jnp.stack(lagrange_at(coords[2]))
    points = np.arange(64)
    pick = [jnp.asarray(np.equal.outer(idx, np.arange(4)), jnp.float32)
            for idx in (points // 16, points // 4 % 4, points % 4)]
    spread = [jnp.dot(m, b, precision=lax.Precision.HIGHEST)
              for m, b in zip(pick, (basis_x, basis_y, basis_z))]
    weights = spread[0] * spread[1] * spread[2]
    onehot = (jnp.arange(elems, dtype=jnp.int32)[:, None] == donors[None, :]).astype(jnp.bfloat16)
    picked = pick_dot(advanced.reshape(nvars * 64, elems), onehot).reshape(nvars, 64, -1)
    return jnp.sum(picked * weights[None], axis=1)


def on_device(
    solution, velocity, inv_jacobian, face_speed, face_link, donor_elem, ref_coords, owner_list
):
    extrapolate, derivative, lifting = tables()
    nvars = solution.shape[0]
    elems = solution.shape[2]
    rim_count = elems // 16
    faces_total = 6 * elems
    links = face_link.reshape(faces_total)
    table_own, values, speeds = face_rows(solution, face_speed)
    outgoing = rim_rows(table_own, links, faces_total, rim_count)
    extended = padded(outgoing, (("valve", 0),), rim_count)
    received = jnp.concatenate([extended[:rim_count], extended[3 * rim_count :]], axis=0)
    surface = surface_term(values, speeds, table_own, links, received, lifting, elems)
    volume = volume_term(solution, velocity, derivative)
    section_rate = -inv_jacobian[None] * (volume + surface)
    advanced = solution + section_step * section_rate
    receptor_vals = receptor_rows(advanced, donor_elem, ref_coords)
    buckets = lax.axis_size("bulk")
    receptors = receptor_vals.shape[1]
    capacity = 2 * receptors // buckets
    owners = owner_list[:, 0]
    ranks = owner_ranks(owners, buckets)
    chosen = owners[:, None] == jnp.arange(buckets, dtype=jnp.int32)[None, :]
    masked = jnp.where(chosen[:, :, None], jnp.transpose(receptor_vals)[:, None, :], 0.0)
    hi, lo = split_bf16(masked.reshape(receptors, buckets * nvars))
    by_rank = (jnp.arange(capacity, dtype=jnp.int32)[:, None] == ranks[None, :]).astype(jnp.bfloat16)
    both = jnp.dot(by_rank, jnp.concatenate([hi, lo], axis=1), preferred_element_type=jnp.float32)
    placed = both[:, : buckets * nvars] + both[:, buckets * nvars :]
    send = jnp.transpose(placed.reshape(capacity, buckets, nvars), (1, 2, 0))
    got = lax.all_to_all(send, "bulk", 0, 0, tiled=True)
    fringe = jnp.transpose(got, (1, 0, 2)).reshape(nvars, buckets * capacity)
    return (section_rate, fringe)


def solution(mesh):
    placed = (
        P(None, None, ("valve", "bulk")),
        P(None, ("valve", "bulk")),
        P(None, ("valve", "bulk")),
        P(None, ("valve", "bulk")),
        P(None, ("valve", "bulk")),
        P(("valve", "bulk")),
        P(None, ("valve", "bulk")),
        P(("valve", "bulk"), None),
    )
    return jax.shard_map(
        on_device,
        mesh=mesh,
        in_specs=placed,
        out_specs=(P(None, None, ("valve", "bulk")), P(None, ("valve", "bulk"))),
        check_vma=False,
    )
```

```python
import jax
import jax.numpy as jnp
import numpy as np
from jax import lax
from jax.sharding import PartitionSpec as P
from jax.experimental import pallas as pl
from jax.experimental.pallas import tpu as pltpu

gauss_nodes = (-0.8611363115940526, -0.3399810435848563, 0.3399810435848563, 0.8611363115940526)
quad_weights = (0.3478548451374538, 0.6521451548625461, 0.6521451548625461, 0.3478548451374538)
section_step = 0.2


def padded(shard, sides, width):
    for axis, dim in sides:
        size, length = (lax.axis_size(axis), shard.shape[dim])
        up = [(i, (i + 1) % size) for i in range(size)]
        down = [(j, i) for i, j in up]
        last = lax.slice_in_dim(shard, length - width, length, axis=dim)
        initial = lax.slice_in_dim(shard, 0, width, axis=dim)
        before = lax.ppermute(last, axis, up)
        after = lax.ppermute(initial, axis, down)
        shard = jnp.concatenate([before, shard, after], axis=dim)
    return shard


def lagrange_at(x):
    values = []
    for j in range(4):
        factor = 1.0
        for m in range(4):
            if m != j:
                factor = factor * (x - gauss_nodes[m]) / (gauss_nodes[j] - gauss_nodes[m])
        values.append(factor)
    return values


def tables():
    slopes = np.zeros((4, 4))
    for i in range(4):
        for j in range(4):
            summed = 0.0
            for m in range(4):
                if m != j:
                    product = 1.0 / (gauss_nodes[j] - gauss_nodes[m])
                    for n in range(4):
                        if n != j and n != m:
                            product = (
                                product
                                * (gauss_nodes[i] - gauss_nodes[n])
                                / (gauss_nodes[j] - gauss_nodes[n])
                            )
                    summed = summed + product
            slopes[i, j] = summed
    end_values = [lagrange_at(-1.0), lagrange_at(1.0)]
    extrapolate = np.zeros((96, 64))
    lifting = np.zeros((64, 96))
    derivative = np.zeros((3, 64, 64))
    for p in range(64):
        point_idx = (p // 16, p // 4 % 4, p % 4)
        for f in range(6):
            normal_dir = f // 2
            across = [t for t in range(3) if t != normal_dir]
            q = point_idx[across[0]] * 4 + point_idx[across[1]]
            flux_row = q * 6 + f
            extrapolate[flux_row, p] = end_values[f % 2][point_idx[normal_dir]]
            lifting[p, flux_row] = (
                end_values[f % 2][point_idx[normal_dir]] / quad_weights[point_idx[normal_dir]]
            )
        for s in range(64):
            other_idx = (s // 16, s // 4 % 4, s % 4)
            for normal_dir in range(3):
                if all((point_idx[t] == other_idx[t] for t in range(3) if t != normal_dir)):
                    derivative[normal_dir, p, s] = slopes[
                        point_idx[normal_dir], other_idx[normal_dir]
                    ]
    return (
        jnp.asarray(extrapolate, dtype=jnp.float32),
        jnp.asarray(derivative, dtype=jnp.float32),
        jnp.asarray(lifting, dtype=jnp.float32),
    )


def face_rows(solution, face_speed, extrapolate):
    nvars = solution.shape[0]
    elems = solution.shape[2]
    ext_faces = extrapolate.reshape(16, 6, 64)
    values = jnp.einsum("qfp,vpe->feqv", ext_faces, solution, precision=lax.Precision.HIGHEST)
    values = values.reshape(6 * elems, 16, nvars)
    speeds = jnp.transpose(face_speed.reshape(16, 6, elems), (1, 2, 0)).reshape(6 * elems, 16)
    return (values, speeds)


def rim_rows(table_own, links, faces_total, rim_count):
    wanted = faces_total + jnp.arange(2 * rim_count, dtype=jnp.int32)
    hits = links[None, :] == wanted[:, None]
    faces = jnp.arange(faces_total, dtype=jnp.int32)[None, :]
    senders = jnp.sum(jnp.where(hits, faces, 0), axis=1)
    return jnp.take(table_own, senders, axis=0)


def split_bf16(x):
    hi = lax.reduce_precision(x, exponent_bits=8, mantissa_bits=7)
    return hi.astype(jnp.bfloat16), (x - hi).astype(jnp.bfloat16)


def pick_dot(rows, onehot):
    hi, lo = split_bf16(rows)
    both = jnp.dot(jnp.concatenate([hi, lo], axis=0), onehot, preferred_element_type=jnp.float32)
    return both[: rows.shape[0]] + both[rows.shape[0] :]


def _rows_kernel(idx_ref, own_ref, recv_ref, out_ref, table_ref):
    own_rows = own_ref.shape[0]
    table_ref[pl.ds(0, own_rows), :] = own_ref[...]
    table_ref[pl.ds(own_rows, recv_ref.shape[0]), :] = recv_ref[...]

    def body(i, carry):
        base = pl.multiple_of(i * 16, 16)
        for j in range(16):
            row = idx_ref[base + j]
            out_ref[pl.ds(base + j, 1), :] = table_ref[pl.ds(row, 1), :]
        return carry

    lax.fori_loop(0, out_ref.shape[0] // 16, body, 0)


def take_rows(own, received, idx):
    rows = own.shape[0] + received.shape[0]
    return pl.pallas_call(
        _rows_kernel,
        out_shape=jax.ShapeDtypeStruct((idx.shape[0], own.shape[1]), own.dtype),
        in_specs=[
            pl.BlockSpec(memory_space=pltpu.SMEM),
            pl.BlockSpec(memory_space=pltpu.VMEM),
            pl.BlockSpec(memory_space=pltpu.VMEM),
        ],
        out_specs=pl.BlockSpec(memory_space=pltpu.VMEM),
        scratch_shapes=[pltpu.VMEM((rows, own.shape[1]), own.dtype)],
        cost_estimate=pl.CostEstimate(
            flops=0, transcendentals=0, bytes_accessed=(2 * idx.shape[0] + rows) * own.shape[1] * 4
        ),
    )(idx, own, received)


def owner_ranks(owners, buckets):
    receptors = owners.shape[0]
    width = 128
    blocks = receptors // width
    member = owners[None, :] == jnp.arange(buckets, dtype=jnp.int32)[:, None]
    member = member.astype(jnp.bfloat16).reshape(buckets * blocks, width)
    upper = jnp.asarray(np.triu(np.ones((width, width))), jnp.bfloat16)
    inside = jnp.dot(member, upper, preferred_element_type=jnp.float32)
    inside = inside.reshape(buckets, blocks, width)
    totals = inside[:, :, width - 1].astype(jnp.bfloat16)
    strict = jnp.asarray(np.triu(np.ones((blocks, blocks)), 1), jnp.bfloat16)
    offsets = jnp.dot(totals, strict, preferred_element_type=jnp.float32)
    counts = (inside + offsets[:, :, None]).reshape(buckets, receptors)
    picked = jnp.sum(jnp.where(member.reshape(buckets, receptors) > 0, counts, 0.0), axis=0)
    return picked.astype(jnp.int32) - 1


def surface_term(values, speeds, table_own, links, received, lifting, elems):
    nvars = values.shape[2]
    outer = take_rows(table_own, received, links)
    outer_vals = outer[:, : 16 * nvars].reshape(6 * elems, 16, nvars)
    outer_speed = outer[:, 16 * nvars :][:, :, None]
    own_speed = speeds[:, :, None]
    normal = 0.5 * (own_speed - outer_speed)
    common = 0.5 * normal * (values + outer_vals) + 0.5 * jnp.abs(normal) * (values - outer_vals)
    jump_term = (common - own_speed * values).reshape(6, elems, 16, nvars)
    lift_faces = lifting.reshape(64, 16, 6)
    return jnp.einsum("pqf,feqv->vpe", lift_faces, jump_term, precision=lax.Precision.HIGHEST)


def volume_term(solution, velocity, derivative):
    slopes = jnp.einsum("dpq,vqe->dvpe", derivative, solution, precision=lax.Precision.HIGHEST)
    return jnp.sum(velocity[:, None, None, :] * slopes, axis=0)


def receptor_rows(advanced, donors, coords):
    nvars = advanced.shape[0]
    elems = advanced.shape[2]
    basis_x = jnp.stack(lagrange_at(coords[0]))
    basis_y = jnp.stack(lagrange_at(coords[1]))
    basis_z = jnp.stack(lagrange_at(coords[2]))
    weights = (
        jnp.repeat(basis_x, 16, axis=0)
        * jnp.tile(jnp.repeat(basis_y, 4, axis=0), (4, 1))
        * jnp.tile(basis_z, (16, 1))
    )
    onehot = (jnp.arange(elems, dtype=jnp.int32)[:, None] == donors[None, :]).astype(jnp.bfloat16)
    picked = pick_dot(advanced.reshape(nvars * 64, elems), onehot).reshape(nvars, 64, -1)
    return jnp.sum(picked * weights[None], axis=1)


def on_device(
    solution, velocity, inv_jacobian, face_speed, face_link, donor_elem, ref_coords, owner_list
):
    extrapolate, derivative, lifting = tables()
    nvars = solution.shape[0]
    elems = solution.shape[2]
    rim_count = elems // 16
    faces_total = 6 * elems
    links = face_link.reshape(faces_total)
    values, speeds = face_rows(solution, face_speed, extrapolate)
    table_own = jnp.concatenate([values.reshape(faces_total, 16 * nvars), speeds], axis=1)
    outgoing = rim_rows(table_own, links, faces_total, rim_count)
    extended = padded(outgoing, (("valve", 0),), rim_count)
    received = jnp.concatenate([extended[:rim_count], extended[3 * rim_count :]], axis=0)
    surface = surface_term(values, speeds, table_own, links, received, lifting, elems)
    volume = volume_term(solution, velocity, derivative)
    section_rate = -inv_jacobian[None] * (volume + surface)
    advanced = solution + section_step * section_rate
    receptor_vals = receptor_rows(advanced, donor_elem, ref_coords)
    buckets = lax.axis_size("bulk")
    receptors = receptor_vals.shape[1]
    capacity = 2 * receptors // buckets
    owners = owner_list[:, 0]
    ranks = owner_ranks(owners, buckets)
    copies = jnp.asarray(np.tile(np.eye(nvars), (1, buckets)), jnp.float32)
    spread = lax.dot_general(
        receptor_vals, copies, (((0,), (0,)), ((), ())), precision=lax.Precision.HIGHEST
    )
    column_owner = jnp.arange(buckets * nvars, dtype=jnp.int32) // nvars
    masked = jnp.where(owners[:, None] == column_owner[None, :], spread, 0.0)
    hi, lo = split_bf16(masked)
    by_rank = (jnp.arange(capacity, dtype=jnp.int32)[:, None] == ranks[None, :]).astype(jnp.bfloat16)
    both = jnp.dot(by_rank, jnp.concatenate([hi, lo], axis=1), preferred_element_type=jnp.float32)
    placed = both[:, : buckets * nvars] + both[:, buckets * nvars :]
    send = jnp.transpose(placed.reshape(capacity, buckets, nvars), (1, 2, 0))
    got = lax.all_to_all(send, "bulk", 0, 0, tiled=True)
    fringe = jnp.transpose(got, (1, 0, 2)).reshape(nvars, buckets * capacity)
    return (section_rate, fringe)


def solution(mesh):
    placed = (
        P(None, None, ("valve", "bulk")),
        P(None, ("valve", "bulk")),
        P(None, ("valve", "bulk")),
        P(None, ("valve", "bulk")),
        P(None, ("valve", "bulk")),
        P(("valve", "bulk")),
        P(None, ("valve", "bulk")),
        P(("valve", "bulk"), None),
    )
    return jax.shard_map(
        on_device,
        mesh=mesh,
        in_specs=placed,
        out_specs=(P(None, None, ("valve", "bulk")), P(None, ("valve", "bulk"))),
        check_vma=False,
    )
```

```python
import jax
import jax.numpy as jnp
import numpy as np
from jax import lax
from jax.sharding import PartitionSpec as P
from jax.experimental import pallas as pl
from jax.experimental.pallas import tpu as pltpu

gauss_nodes = (-0.8611363115940526, -0.3399810435848563, 0.3399810435848563, 0.8611363115940526)
quad_weights = (0.3478548451374538, 0.6521451548625461, 0.6521451548625461, 0.3478548451374538)
section_step = 0.2


def padded(shard, sides, width):
    for axis, dim in sides:
        size, length = (lax.axis_size(axis), shard.shape[dim])
        up = [(i, (i + 1) % size) for i in range(size)]
        down = [(j, i) for i, j in up]
        last = lax.slice_in_dim(shard, length - width, length, axis=dim)
        initial = lax.slice_in_dim(shard, 0, width, axis=dim)
        before = lax.ppermute(last, axis, up)
        after = lax.ppermute(initial, axis, down)
        shard = jnp.concatenate([before, shard, after], axis=dim)
    return shard


def lagrange_at(x):
    values = []
    for j in range(4):
        factor = 1.0
        for m in range(4):
            if m != j:
                factor = factor * (x - gauss_nodes[m]) / (gauss_nodes[j] - gauss_nodes[m])
        values.append(factor)
    return values


def tables():
    slopes = np.zeros((4, 4))
    for i in range(4):
        for j in range(4):
            summed = 0.0
            for m in range(4):
                if m != j:
                    product = 1.0 / (gauss_nodes[j] - gauss_nodes[m])
                    for n in range(4):
                        if n != j and n != m:
                            product = (
                                product
                                * (gauss_nodes[i] - gauss_nodes[n])
                                / (gauss_nodes[j] - gauss_nodes[n])
                            )
                    summed = summed + product
            slopes[i, j] = summed
    end_values = [lagrange_at(-1.0), lagrange_at(1.0)]
    extrapolate = np.zeros((96, 64))
    lifting = np.zeros((64, 96))
    derivative = np.zeros((3, 64, 64))
    for p in range(64):
        point_idx = (p // 16, p // 4 % 4, p % 4)
        for f in range(6):
            normal_dir = f // 2
            across = [t for t in range(3) if t != normal_dir]
            q = point_idx[across[0]] * 4 + point_idx[across[1]]
            flux_row = q * 6 + f
            extrapolate[flux_row, p] = end_values[f % 2][point_idx[normal_dir]]
            lifting[p, flux_row] = (
                end_values[f % 2][point_idx[normal_dir]] / quad_weights[point_idx[normal_dir]]
            )
        for s in range(64):
            other_idx = (s // 16, s // 4 % 4, s % 4)
            for normal_dir in range(3):
                if all((point_idx[t] == other_idx[t] for t in range(3) if t != normal_dir)):
                    derivative[normal_dir, p, s] = slopes[
                        point_idx[normal_dir], other_idx[normal_dir]
                    ]
    return (
        jnp.asarray(extrapolate, dtype=jnp.float32),
        jnp.asarray(derivative, dtype=jnp.float32),
        jnp.asarray(lifting, dtype=jnp.float32),
    )


def face_rows(solution, face_speed, extrapolate):
    nvars = solution.shape[0]
    elems = solution.shape[2]
    ext_faces = extrapolate.reshape(16, 6, 64)
    values = jnp.einsum("qfp,vpe->feqv", ext_faces, solution, precision=lax.Precision.HIGHEST)
    values = values.reshape(6 * elems, 16, nvars)
    speeds = jnp.transpose(face_speed.reshape(16, 6, elems), (1, 2, 0)).reshape(6 * elems, 16)
    return (values, speeds)


def rim_rows(table_own, links, faces_total, rim_count):
    wanted = faces_total + jnp.arange(2 * rim_count, dtype=jnp.int32)
    hits = links[None, :] == wanted[:, None]
    faces = jnp.arange(faces_total, dtype=jnp.int32)[None, :]
    senders = jnp.sum(jnp.where(hits, faces, 0), axis=1)
    return jnp.take(table_own, senders, axis=0)


def split_bf16(x):
    hi = lax.reduce_precision(x, exponent_bits=8, mantissa_bits=7)
    return hi.astype(jnp.bfloat16), (x - hi).astype(jnp.bfloat16)


def pick_dot(rows, onehot):
    hi, lo = split_bf16(rows)
    both = jnp.dot(jnp.concatenate([hi, lo], axis=0), onehot, preferred_element_type=jnp.float32)
    return both[: rows.shape[0]] + both[rows.shape[0] :]


def _rows_kernel(idx_ref, own_ref, recv_ref, out_ref, table_ref):
    own_rows = own_ref.shape[0]
    table_ref[pl.ds(0, own_rows), :] = own_ref[...]
    table_ref[pl.ds(own_rows, recv_ref.shape[0]), :] = recv_ref[...]

    def body(i, carry):
        base = pl.multiple_of(i * 16, 16)
        for j in range(16):
            row = idx_ref[base + j]
            out_ref[pl.ds(base + j, 1), :] = table_ref[pl.ds(row, 1), :]
        return carry

    lax.fori_loop(0, out_ref.shape[0] // 16, body, 0)


def take_rows(own, received, idx):
    rows = own.shape[0] + received.shape[0]
    return pl.pallas_call(
        _rows_kernel,
        out_shape=jax.ShapeDtypeStruct((idx.shape[0], own.shape[1]), own.dtype),
        in_specs=[
            pl.BlockSpec(memory_space=pltpu.SMEM),
            pl.BlockSpec(memory_space=pltpu.VMEM),
            pl.BlockSpec(memory_space=pltpu.VMEM),
        ],
        out_specs=pl.BlockSpec(memory_space=pltpu.VMEM),
        scratch_shapes=[pltpu.VMEM((rows, own.shape[1]), own.dtype)],
        cost_estimate=pl.CostEstimate(
            flops=0, transcendentals=0, bytes_accessed=(2 * idx.shape[0] + rows) * own.shape[1] * 4
        ),
    )(idx, own, received)


def owner_ranks(owners, buckets):
    receptors = owners.shape[0]
    width = 128
    blocks = receptors // width
    member = owners[None, :] == jnp.arange(buckets, dtype=jnp.int32)[:, None]
    member = member.astype(jnp.bfloat16).reshape(buckets * blocks, width)
    upper = jnp.asarray(np.triu(np.ones((width, width))), jnp.bfloat16)
    inside = jnp.dot(member, upper, preferred_element_type=jnp.float32)
    inside = inside.reshape(buckets, blocks, width)
    totals = inside[:, :, width - 1].astype(jnp.bfloat16)
    strict = jnp.asarray(np.triu(np.ones((blocks, blocks)), 1), jnp.bfloat16)
    offsets = jnp.dot(totals, strict, preferred_element_type=jnp.float32)
    counts = (inside + offsets[:, :, None]).reshape(buckets, receptors)
    picked = jnp.sum(jnp.where(member.reshape(buckets, receptors) > 0, counts, 0.0), axis=0)
    return picked.astype(jnp.int32) - 1


def surface_term(values, speeds, table_own, links, received, lifting, elems):
    nvars = values.shape[2]
    outer = take_rows(table_own, received, links)
    outer_vals = outer[:, : 16 * nvars].reshape(6 * elems, 16, nvars)
    outer_speed = outer[:, 16 * nvars :][:, :, None]
    own_speed = speeds[:, :, None]
    normal = 0.5 * (own_speed - outer_speed)
    common = 0.5 * normal * (values + outer_vals) + 0.5 * jnp.abs(normal) * (values - outer_vals)
    jump_term = (common - own_speed * values).reshape(6, elems, 16, nvars)
    lift_faces = lifting.reshape(64, 16, 6)
    return jnp.einsum("pqf,feqv->vpe", lift_faces, jump_term, precision=lax.Precision.HIGHEST)


def volume_term(solution, velocity, derivative):
    slopes = jnp.einsum("dpq,vqe->dvpe", derivative, solution, precision=lax.Precision.HIGHEST)
    return jnp.sum(velocity[:, None, None, :] * slopes, axis=0)


def _interp_kernel(rows_ref, donors_ref, weights_ref, out_ref):
    elems = rows_ref.shape[1]
    tile = donors_ref.shape[1]
    half = rows_ref.shape[0] // 2
    onehot = lax.broadcasted_iota(jnp.int32, (elems, tile), 0) == donors_ref[...]
    picked = jnp.dot(rows_ref[...], onehot.astype(jnp.bfloat16), preferred_element_type=jnp.float32)
    picked = picked[:half] + picked[half:]
    nvars = out_ref.shape[0]
    picked = picked.reshape(nvars, half // nvars, tile) * weights_ref[...][None]
    out_ref[...] = jnp.sum(picked, axis=1)


def receptor_rows(advanced, donors, coords):
    nvars = advanced.shape[0]
    elems = advanced.shape[2]
    receptors = donors.shape[0]
    basis_x = jnp.stack(lagrange_at(coords[0]))
    basis_y = jnp.stack(lagrange_at(coords[1]))
    basis_z = jnp.stack(lagrange_at(coords[2]))
    weights = (
        jnp.repeat(basis_x, 16, axis=0)
        * jnp.tile(jnp.repeat(basis_y, 4, axis=0), (4, 1))
        * jnp.tile(basis_z, (16, 1))
    )
    hi, lo = split_bf16(advanced.reshape(nvars * 64, elems))
    rows = jnp.concatenate([hi, lo], axis=0)
    tile = 512
    return pl.pallas_call(
        _interp_kernel,
        out_shape=jax.ShapeDtypeStruct((nvars, receptors), jnp.float32),
        grid=(receptors // tile,),
        in_specs=[
            pl.BlockSpec((2 * nvars * 64, elems), lambda i: (0, 0)),
            pl.BlockSpec((1, tile), lambda i: (0, i)),
            pl.BlockSpec((64, tile), lambda i: (0, i)),
        ],
        out_specs=pl.BlockSpec((nvars, tile), lambda i: (0, i)),
        cost_estimate=pl.CostEstimate(
            flops=2 * 2 * nvars * 64 * elems * receptors,
            transcendentals=0,
            bytes_accessed=2 * nvars * 64 * elems * 2 + receptors * (1 + 64 + nvars) * 4,
        ),
    )(rows, donors.reshape(1, receptors), weights)


def on_device(
    solution, velocity, inv_jacobian, face_speed, face_link, donor_elem, ref_coords, owner_list
):
    extrapolate, derivative, lifting = tables()
    nvars = solution.shape[0]
    elems = solution.shape[2]
    rim_count = elems // 16
    faces_total = 6 * elems
    links = face_link.reshape(faces_total)
    values, speeds = face_rows(solution, face_speed, extrapolate)
    table_own = jnp.concatenate([values.reshape(faces_total, 16 * nvars), speeds], axis=1)
    outgoing = rim_rows(table_own, links, faces_total, rim_count)
    extended = padded(outgoing, (("valve", 0),), rim_count)
    received = jnp.concatenate([extended[:rim_count], extended[3 * rim_count :]], axis=0)
    surface = surface_term(values, speeds, table_own, links, received, lifting, elems)
    volume = volume_term(solution, velocity, derivative)
    section_rate = -inv_jacobian[None] * (volume + surface)
    advanced = solution + section_step * section_rate
    receptor_vals = receptor_rows(advanced, donor_elem, ref_coords)
    buckets = lax.axis_size("bulk")
    receptors = receptor_vals.shape[1]
    capacity = 2 * receptors // buckets
    owners = owner_list[:, 0]
    ranks = owner_ranks(owners, buckets)
    copies = jnp.asarray(np.tile(np.eye(nvars), (1, buckets)), jnp.float32)
    spread = lax.dot_general(
        receptor_vals, copies, (((0,), (0,)), ((), ())), precision=lax.Precision.HIGHEST
    )
    column_owner = jnp.arange(buckets * nvars, dtype=jnp.int32) // nvars
    masked = jnp.where(owners[:, None] == column_owner[None, :], spread, 0.0)
    hi, lo = split_bf16(masked)
    by_rank = (jnp.arange(capacity, dtype=jnp.int32)[:, None] == ranks[None, :]).astype(jnp.bfloat16)
    both = jnp.dot(by_rank, jnp.concatenate([hi, lo], axis=1), preferred_element_type=jnp.float32)
    placed = both[:, : buckets * nvars] + both[:, buckets * nvars :]
    send = jnp.transpose(placed.reshape(capacity, buckets, nvars), (1, 2, 0))
    got = lax.all_to_all(send, "bulk", 0, 0, tiled=True)
    fringe = jnp.transpose(got, (1, 0, 2)).reshape(nvars, buckets * capacity)
    return (section_rate, fringe)


def solution(mesh):
    placed = (
        P(None, None, ("valve", "bulk")),
        P(None, ("valve", "bulk")),
        P(None, ("valve", "bulk")),
        P(None, ("valve", "bulk")),
        P(None, ("valve", "bulk")),
        P(("valve", "bulk")),
        P(None, ("valve", "bulk")),
        P(("valve", "bulk"), None),
    )
    return jax.shard_map(
        on_device,
        mesh=mesh,
        in_specs=placed,
        out_specs=(P(None, None, ("valve", "bulk")), P(None, ("valve", "bulk"))),
        check_vma=False,
    )
```

```python
import jax
import jax.numpy as jnp
import numpy as np
from jax import lax
from jax.sharding import PartitionSpec as P
from jax.experimental import pallas as pl
from jax.experimental.pallas import tpu as pltpu

gauss_nodes = (-0.8611363115940526, -0.3399810435848563, 0.3399810435848563, 0.8611363115940526)
quad_weights = (0.3478548451374538, 0.6521451548625461, 0.6521451548625461, 0.3478548451374538)
section_step = 0.2


def padded(shard, sides, width):
    for axis, dim in sides:
        size, length = (lax.axis_size(axis), shard.shape[dim])
        up = [(i, (i + 1) % size) for i in range(size)]
        down = [(j, i) for i, j in up]
        last = lax.slice_in_dim(shard, length - width, length, axis=dim)
        initial = lax.slice_in_dim(shard, 0, width, axis=dim)
        before = lax.ppermute(last, axis, up)
        after = lax.ppermute(initial, axis, down)
        shard = jnp.concatenate([before, shard, after], axis=dim)
    return shard


def lagrange_at(x):
    values = []
    for j in range(4):
        factor = 1.0
        for m in range(4):
            if m != j:
                factor = factor * (x - gauss_nodes[m]) / (gauss_nodes[j] - gauss_nodes[m])
        values.append(factor)
    return values


def tables():
    slopes = np.zeros((4, 4))
    for i in range(4):
        for j in range(4):
            summed = 0.0
            for m in range(4):
                if m != j:
                    product = 1.0 / (gauss_nodes[j] - gauss_nodes[m])
                    for n in range(4):
                        if n != j and n != m:
                            product = (
                                product
                                * (gauss_nodes[i] - gauss_nodes[n])
                                / (gauss_nodes[j] - gauss_nodes[n])
                            )
                    summed = summed + product
            slopes[i, j] = summed
    end_values = [lagrange_at(-1.0), lagrange_at(1.0)]
    extrapolate = np.zeros((96, 64))
    lifting = np.zeros((64, 96))
    derivative = np.zeros((3, 64, 64))
    for p in range(64):
        point_idx = (p // 16, p // 4 % 4, p % 4)
        for f in range(6):
            normal_dir = f // 2
            across = [t for t in range(3) if t != normal_dir]
            q = point_idx[across[0]] * 4 + point_idx[across[1]]
            flux_row = q * 6 + f
            extrapolate[flux_row, p] = end_values[f % 2][point_idx[normal_dir]]
            lifting[p, flux_row] = (
                end_values[f % 2][point_idx[normal_dir]] / quad_weights[point_idx[normal_dir]]
            )
        for s in range(64):
            other_idx = (s // 16, s // 4 % 4, s % 4)
            for normal_dir in range(3):
                if all((point_idx[t] == other_idx[t] for t in range(3) if t != normal_dir)):
                    derivative[normal_dir, p, s] = slopes[
                        point_idx[normal_dir], other_idx[normal_dir]
                    ]
    return (
        jnp.asarray(extrapolate, dtype=jnp.float32),
        jnp.asarray(derivative, dtype=jnp.float32),
        jnp.asarray(lifting, dtype=jnp.float32),
    )


def face_rows(solution, face_speed, extrapolate):
    nvars = solution.shape[0]
    elems = solution.shape[2]
    ext_faces = extrapolate.reshape(16, 6, 64)
    values = jnp.einsum("qfp,vpe->feqv", ext_faces, solution, precision=lax.Precision.HIGHEST)
    values = values.reshape(6 * elems, 16, nvars)
    speeds = jnp.transpose(face_speed.reshape(16, 6, elems), (1, 2, 0)).reshape(6 * elems, 16)
    return (values, speeds)


def rim_rows(values, speeds, links, faces_total, rim_count):
    wanted = faces_total + jnp.arange(2 * rim_count, dtype=jnp.int32)
    hits = links[None, :] == wanted[:, None]
    faces = jnp.arange(faces_total, dtype=jnp.int32)[None, :]
    senders = jnp.sum(jnp.where(hits, faces, 0), axis=1)
    return jnp.concatenate(
        [jnp.take(values, senders, axis=0), jnp.take(speeds, senders, axis=0)], axis=1
    )


def split_bf16(x):
    hi = lax.reduce_precision(x, exponent_bits=8, mantissa_bits=7)
    return hi.astype(jnp.bfloat16), (x - hi).astype(jnp.bfloat16)


def pick_dot(rows, onehot):
    hi, lo = split_bf16(rows)
    both = jnp.dot(jnp.concatenate([hi, lo], axis=0), onehot, preferred_element_type=jnp.float32)
    return both[: rows.shape[0]] + both[rows.shape[0] :]


def _rows_kernel(idx_ref, values_ref, speeds_ref, recv_ref, out_ref, table_ref):
    own_rows, width = values_ref.shape
    table_ref[pl.ds(0, own_rows), pl.ds(0, width)] = values_ref[...]
    table_ref[pl.ds(0, own_rows), pl.ds(width, speeds_ref.shape[1])] = speeds_ref[...]
    table_ref[pl.ds(own_rows, recv_ref.shape[0]), :] = recv_ref[...]

    def body(i, carry):
        base = pl.multiple_of(i * 16, 16)
        for j in range(16):
            row = idx_ref[base + j]
            out_ref[pl.ds(base + j, 1), :] = table_ref[pl.ds(row, 1), :]
        return carry

    lax.fori_loop(0, out_ref.shape[0] // 16, body, 0)


def take_rows(values, speeds, received, idx):
    rows = values.shape[0] + received.shape[0]
    width = received.shape[1]
    return pl.pallas_call(
        _rows_kernel,
        out_shape=jax.ShapeDtypeStruct((idx.shape[0], width), values.dtype),
        in_specs=[
            pl.BlockSpec(memory_space=pltpu.SMEM),
            pl.BlockSpec(memory_space=pltpu.VMEM),
            pl.BlockSpec(memory_space=pltpu.VMEM),
            pl.BlockSpec(memory_space=pltpu.VMEM),
        ],
        out_specs=pl.BlockSpec(memory_space=pltpu.VMEM),
        scratch_shapes=[pltpu.VMEM((rows, width), values.dtype)],
        cost_estimate=pl.CostEstimate(
            flops=0, transcendentals=0, bytes_accessed=(2 * idx.shape[0] + rows) * width * 4
        ),
    )(idx, values, speeds, received)


def owner_ranks(owners, buckets):
    receptors = owners.shape[0]
    width = 128
    blocks = receptors // width
    member = owners[None, :] == jnp.arange(buckets, dtype=jnp.int32)[:, None]
    member = member.astype(jnp.bfloat16).reshape(buckets * blocks, width)
    upper = jnp.asarray(np.triu(np.ones((width, width))), jnp.bfloat16)
    inside = jnp.dot(member, upper, preferred_element_type=jnp.float32)
    inside = inside.reshape(buckets, blocks, width)
    totals = inside[:, :, width - 1].astype(jnp.bfloat16)
    strict = jnp.asarray(np.triu(np.ones((blocks, blocks)), 1), jnp.bfloat16)
    offsets = jnp.dot(totals, strict, preferred_element_type=jnp.float32)
    counts = (inside + offsets[:, :, None]).reshape(buckets, receptors)
    picked = jnp.sum(jnp.where(member.reshape(buckets, receptors) > 0, counts, 0.0), axis=0)
    return picked.astype(jnp.int32) - 1


def surface_term(values, speeds, table_own, links, received, lifting, elems):
    nvars = values.shape[2]
    outer = take_rows(table_own, speeds, received, links)
    outer_vals = outer[:, : 16 * nvars].reshape(6 * elems, 16, nvars)
    outer_speed = outer[:, 16 * nvars :][:, :, None]
    own_speed = speeds[:, :, None]
    normal = 0.5 * (own_speed - outer_speed)
    common = 0.5 * normal * (values + outer_vals) + 0.5 * jnp.abs(normal) * (values - outer_vals)
    jump_term = (common - own_speed * values).reshape(6, elems, 16, nvars)
    lift_faces = lifting.reshape(64, 16, 6)
    return jnp.einsum("pqf,feqv->vpe", lift_faces, jump_term, precision=lax.Precision.HIGHEST)


def volume_term(solution, velocity, derivative):
    slopes = jnp.einsum("dpq,vqe->dvpe", derivative, solution, precision=lax.Precision.HIGHEST)
    return jnp.sum(velocity[:, None, None, :] * slopes, axis=0)


def _interp_kernel(rows_ref, donors_ref, weights_ref, out_ref):
    elems = rows_ref.shape[1]
    tile = donors_ref.shape[1]
    half = rows_ref.shape[0] // 2
    onehot = lax.broadcasted_iota(jnp.int32, (elems, tile), 0) == donors_ref[...]
    picked = jnp.dot(rows_ref[...], onehot.astype(jnp.bfloat16), preferred_element_type=jnp.float32)
    picked = picked[:half] + picked[half:]
    nvars = out_ref.shape[0]
    picked = picked.reshape(nvars, half // nvars, tile) * weights_ref[...][None]
    out_ref[...] = jnp.sum(picked, axis=1)


def receptor_rows(advanced, donors, coords):
    nvars = advanced.shape[0]
    elems = advanced.shape[2]
    receptors = donors.shape[0]
    basis_x = jnp.stack(lagrange_at(coords[0]))
    basis_y = jnp.stack(lagrange_at(coords[1]))
    basis_z = jnp.stack(lagrange_at(coords[2]))
    weights = (
        jnp.repeat(basis_x, 16, axis=0)
        * jnp.tile(jnp.repeat(basis_y, 4, axis=0), (4, 1))
        * jnp.tile(basis_z, (16, 1))
    )
    hi, lo = split_bf16(advanced.reshape(nvars * 64, elems))
    rows = jnp.concatenate([hi, lo], axis=0)
    tile = 512
    return pl.pallas_call(
        _interp_kernel,
        out_shape=jax.ShapeDtypeStruct((nvars, receptors), jnp.float32),
        grid=(receptors // tile,),
        in_specs=[
            pl.BlockSpec((2 * nvars * 64, elems), lambda i: (0, 0)),
            pl.BlockSpec((1, tile), lambda i: (0, i)),
            pl.BlockSpec((64, tile), lambda i: (0, i)),
        ],
        out_specs=pl.BlockSpec((nvars, tile), lambda i: (0, i)),
        cost_estimate=pl.CostEstimate(
            flops=2 * 2 * nvars * 64 * elems * receptors,
            transcendentals=0,
            bytes_accessed=2 * nvars * 64 * elems * 2 + receptors * (1 + 64 + nvars) * 4,
        ),
    )(rows, donors.reshape(1, receptors), weights)


def on_device(
    solution, velocity, inv_jacobian, face_speed, face_link, donor_elem, ref_coords, owner_list
):
    extrapolate, derivative, lifting = tables()
    nvars = solution.shape[0]
    elems = solution.shape[2]
    rim_count = elems // 16
    faces_total = 6 * elems
    links = face_link.reshape(faces_total)
    values, speeds = face_rows(solution, face_speed, extrapolate)
    flat_values = values.reshape(faces_total, 16 * nvars)
    outgoing = rim_rows(flat_values, speeds, links, faces_total, rim_count)
    extended = padded(outgoing, (("valve", 0),), rim_count)
    received = jnp.concatenate([extended[:rim_count], extended[3 * rim_count :]], axis=0)
    surface = surface_term(values, speeds, flat_values, links, received, lifting, elems)
    volume = volume_term(solution, velocity, derivative)
    section_rate = -inv_jacobian[None] * (volume + surface)
    advanced = solution + section_step * section_rate
    receptor_vals = receptor_rows(advanced, donor_elem, ref_coords)
    buckets = lax.axis_size("bulk")
    receptors = receptor_vals.shape[1]
    capacity = 2 * receptors // buckets
    owners = owner_list[:, 0]
    ranks = owner_ranks(owners, buckets)
    copies = jnp.asarray(np.tile(np.eye(nvars), (1, buckets)), jnp.float32)
    spread = lax.dot_general(
        receptor_vals, copies, (((0,), (0,)), ((), ())), precision=lax.Precision.HIGHEST
    )
    column_owner = jnp.arange(buckets * nvars, dtype=jnp.int32) // nvars
    masked = jnp.where(owners[:, None] == column_owner[None, :], spread, 0.0)
    hi, lo = split_bf16(masked)
    by_rank = (jnp.arange(capacity, dtype=jnp.int32)[:, None] == ranks[None, :]).astype(jnp.bfloat16)
    both = jnp.dot(by_rank, jnp.concatenate([hi, lo], axis=1), preferred_element_type=jnp.float32)
    placed = both[:, : buckets * nvars] + both[:, buckets * nvars :]
    send = jnp.transpose(placed.reshape(capacity, buckets, nvars), (1, 2, 0))
    got = lax.all_to_all(send, "bulk", 0, 0, tiled=True)
    fringe = jnp.transpose(got, (1, 0, 2)).reshape(nvars, buckets * capacity)
    return (section_rate, fringe)


def solution(mesh):
    placed = (
        P(None, None, ("valve", "bulk")),
        P(None, ("valve", "bulk")),
        P(None, ("valve", "bulk")),
        P(None, ("valve", "bulk")),
        P(None, ("valve", "bulk")),
        P(("valve", "bulk")),
        P(None, ("valve", "bulk")),
        P(("valve", "bulk"), None),
    )
    return jax.shard_map(
        on_device,
        mesh=mesh,
        in_specs=placed,
        out_specs=(P(None, None, ("valve", "bulk")), P(None, ("valve", "bulk"))),
        check_vma=False,
    )
```

```python
import jax
import jax.numpy as jnp
import numpy as np
from jax import lax
from jax.sharding import PartitionSpec as P
from jax.experimental import pallas as pl
from jax.experimental.pallas import tpu as pltpu

gauss_nodes = (-0.8611363115940526, -0.3399810435848563, 0.3399810435848563, 0.8611363115940526)
quad_weights = (0.3478548451374538, 0.6521451548625461, 0.6521451548625461, 0.3478548451374538)
section_step = 0.2


def padded(shard, sides, width):
    for axis, dim in sides:
        size, length = (lax.axis_size(axis), shard.shape[dim])
        up = [(i, (i + 1) % size) for i in range(size)]
        down = [(j, i) for i, j in up]
        last = lax.slice_in_dim(shard, length - width, length, axis=dim)
        initial = lax.slice_in_dim(shard, 0, width, axis=dim)
        before = lax.ppermute(last, axis, up)
        after = lax.ppermute(initial, axis, down)
        shard = jnp.concatenate([before, shard, after], axis=dim)
    return shard


def lagrange_at(x):
    values = []
    for j in range(4):
        factor = 1.0
        for m in range(4):
            if m != j:
                factor = factor * (x - gauss_nodes[m]) / (gauss_nodes[j] - gauss_nodes[m])
        values.append(factor)
    return values


def tables():
    slopes = np.zeros((4, 4))
    for i in range(4):
        for j in range(4):
            summed = 0.0
            for m in range(4):
                if m != j:
                    product = 1.0 / (gauss_nodes[j] - gauss_nodes[m])
                    for n in range(4):
                        if n != j and n != m:
                            product = (
                                product
                                * (gauss_nodes[i] - gauss_nodes[n])
                                / (gauss_nodes[j] - gauss_nodes[n])
                            )
                    summed = summed + product
            slopes[i, j] = summed
    end_values = [lagrange_at(-1.0), lagrange_at(1.0)]
    extrapolate = np.zeros((96, 64))
    lifting = np.zeros((64, 96))
    derivative = np.zeros((3, 64, 64))
    for p in range(64):
        point_idx = (p // 16, p // 4 % 4, p % 4)
        for f in range(6):
            normal_dir = f // 2
            across = [t for t in range(3) if t != normal_dir]
            q = point_idx[across[0]] * 4 + point_idx[across[1]]
            flux_row = q * 6 + f
            extrapolate[flux_row, p] = end_values[f % 2][point_idx[normal_dir]]
            lifting[p, flux_row] = (
                end_values[f % 2][point_idx[normal_dir]] / quad_weights[point_idx[normal_dir]]
            )
        for s in range(64):
            other_idx = (s // 16, s // 4 % 4, s % 4)
            for normal_dir in range(3):
                if all((point_idx[t] == other_idx[t] for t in range(3) if t != normal_dir)):
                    derivative[normal_dir, p, s] = slopes[
                        point_idx[normal_dir], other_idx[normal_dir]
                    ]
    return (
        jnp.asarray(extrapolate, dtype=jnp.float32),
        jnp.asarray(derivative, dtype=jnp.float32),
        jnp.asarray(lifting, dtype=jnp.float32),
    )


def face_rows(solution, face_speed, extrapolate):
    nvars = solution.shape[0]
    elems = solution.shape[2]
    ext_faces = extrapolate.reshape(16, 6, 64)
    values = jnp.einsum("qfp,vpe->feqv", ext_faces, solution, precision=lax.Precision.HIGHEST)
    values = values.reshape(6 * elems, 16, nvars)
    speeds = jnp.transpose(face_speed.reshape(16, 6, elems), (1, 2, 0)).reshape(6 * elems, 16)
    return (values, speeds)


def rim_rows(values, speeds, links, faces_total, rim_count):
    wanted = faces_total + jnp.arange(2 * rim_count, dtype=jnp.int32)
    hits = links[None, :] == wanted[:, None]
    faces = jnp.arange(faces_total, dtype=jnp.int32)[None, :]
    senders = jnp.sum(jnp.where(hits, faces, 0), axis=1)
    return jnp.concatenate(
        [jnp.take(values, senders, axis=0), jnp.take(speeds, senders, axis=0)], axis=1
    )


def split_bf16(x):
    hi = lax.reduce_precision(x, exponent_bits=8, mantissa_bits=7)
    return hi.astype(jnp.bfloat16), (x - hi).astype(jnp.bfloat16)


def pick_dot(rows, onehot):
    hi, lo = split_bf16(rows)
    both = jnp.dot(jnp.concatenate([hi, lo], axis=0), onehot, preferred_element_type=jnp.float32)
    return both[: rows.shape[0]] + both[rows.shape[0] :]


def _rows_kernel(idx_ref, values_ref, speeds_ref, recv_ref, out_ref, table_ref):
    own_rows, width = values_ref.shape
    table_ref[pl.ds(0, own_rows), pl.ds(0, width)] = values_ref[...]
    table_ref[pl.ds(0, own_rows), pl.ds(width, speeds_ref.shape[1])] = speeds_ref[...]
    table_ref[pl.ds(own_rows, recv_ref.shape[0]), :] = recv_ref[...]

    def body(i, carry):
        base = pl.multiple_of(i * 16, 16)
        for j in range(16):
            row = idx_ref[base + j]
            out_ref[pl.ds(base + j, 1), :] = table_ref[pl.ds(row, 1), :]
        return carry

    lax.fori_loop(0, out_ref.shape[0] // 16, body, 0)


def take_rows(values, speeds, received, idx):
    rows = values.shape[0] + received.shape[0]
    width = received.shape[1]
    return pl.pallas_call(
        _rows_kernel,
        out_shape=jax.ShapeDtypeStruct((idx.shape[0], width), values.dtype),
        in_specs=[
            pl.BlockSpec(memory_space=pltpu.SMEM),
            pl.BlockSpec(memory_space=pltpu.VMEM),
            pl.BlockSpec(memory_space=pltpu.VMEM),
            pl.BlockSpec(memory_space=pltpu.VMEM),
        ],
        out_specs=pl.BlockSpec(memory_space=pltpu.VMEM),
        scratch_shapes=[pltpu.VMEM((rows, width), values.dtype)],
        cost_estimate=pl.CostEstimate(
            flops=0, transcendentals=0, bytes_accessed=(2 * idx.shape[0] + rows) * width * 4
        ),
    )(idx, values, speeds, received)


def owner_ranks(owners, buckets):
    receptors = owners.shape[0]
    width = 128
    blocks = receptors // width
    member = owners[None, :] == jnp.arange(buckets, dtype=jnp.int32)[:, None]
    member = member.astype(jnp.bfloat16).reshape(buckets * blocks, width)
    upper = jnp.asarray(np.triu(np.ones((width, width))), jnp.bfloat16)
    inside = jnp.dot(member, upper, preferred_element_type=jnp.float32)
    inside = inside.reshape(buckets, blocks, width)
    totals = inside[:, :, width - 1].astype(jnp.bfloat16)
    strict = jnp.asarray(np.triu(np.ones((blocks, blocks)), 1), jnp.bfloat16)
    offsets = jnp.dot(totals, strict, preferred_element_type=jnp.float32)
    counts = (inside + offsets[:, :, None]).reshape(buckets, receptors)
    picked = jnp.sum(jnp.where(member.reshape(buckets, receptors) > 0, counts, 0.0), axis=0)
    return picked.astype(jnp.int32) - 1


def surface_term(values, speeds, table_own, links, received, lifting, elems):
    nvars = values.shape[2]
    outer = take_rows(table_own, speeds, received, links)
    outer_vals = outer[:, : 16 * nvars].reshape(6 * elems, 16, nvars)
    outer_speed = outer[:, 16 * nvars :][:, :, None]
    own_speed = speeds[:, :, None]
    normal = 0.5 * (own_speed - outer_speed)
    common = 0.5 * normal * (values + outer_vals) + 0.5 * jnp.abs(normal) * (values - outer_vals)
    jump_term = (common - own_speed * values).reshape(6, elems, 16, nvars)
    lift_faces = lifting.reshape(64, 16, 6)
    return jnp.einsum("pqf,feqv->vpe", lift_faces, jump_term, precision=lax.Precision.HIGHEST)


def volume_term(solution, velocity, derivative):
    slopes = jnp.einsum("dpq,vqe->dvpe", derivative, solution, precision=lax.Precision.HIGHEST)
    return jnp.sum(velocity[:, None, None, :] * slopes, axis=0)


def _pick_row(basis, first, index):
    out = basis[first : first + 1]
    for i in range(1, 4):
        out = jnp.where(index == i, basis[first + i : first + i + 1], out)
    return out


def _interp_kernel(rows_ref, donors_ref, basis_ref, out_ref):
    elems = rows_ref.shape[1]
    tile = donors_ref.shape[1]
    half = rows_ref.shape[0] // 2
    onehot = lax.broadcasted_iota(jnp.int32, (elems, tile), 0) == donors_ref[...]
    picked = jnp.dot(rows_ref[...], onehot.astype(jnp.bfloat16), preferred_element_type=jnp.float32)
    picked = picked[:half] + picked[half:]
    nvars = out_ref.shape[0]
    points = half // nvars
    basis = basis_ref[...]
    point = lax.broadcasted_iota(jnp.int32, (points, tile), 0)
    weights = (
        _pick_row(basis, 0, point // 16)
        * _pick_row(basis, 4, point // 4 % 4)
        * _pick_row(basis, 8, point % 4)
    )
    picked = picked.reshape(nvars, points, tile) * weights[None]
    out_ref[...] = jnp.sum(picked, axis=1)


def receptor_rows(advanced, donors, coords):
    nvars = advanced.shape[0]
    elems = advanced.shape[2]
    receptors = donors.shape[0]
    basis = jnp.concatenate([jnp.stack(lagrange_at(coords[d])) for d in range(3)], axis=0)
    hi, lo = split_bf16(advanced.reshape(nvars * 64, elems))
    rows = jnp.concatenate([hi, lo], axis=0)
    tile = 512
    return pl.pallas_call(
        _interp_kernel,
        out_shape=jax.ShapeDtypeStruct((nvars, receptors), jnp.float32),
        grid=(receptors // tile,),
        in_specs=[
            pl.BlockSpec((2 * nvars * 64, elems), lambda i: (0, 0)),
            pl.BlockSpec((1, tile), lambda i: (0, i)),
            pl.BlockSpec((12, tile), lambda i: (0, i)),
        ],
        out_specs=pl.BlockSpec((nvars, tile), lambda i: (0, i)),
        cost_estimate=pl.CostEstimate(
            flops=2 * 2 * nvars * 64 * elems * receptors,
            transcendentals=0,
            bytes_accessed=2 * nvars * 64 * elems * 2 + receptors * (1 + 12 + nvars) * 4,
        ),
    )(rows, donors.reshape(1, receptors), basis)


def on_device(
    solution, velocity, inv_jacobian, face_speed, face_link, donor_elem, ref_coords, owner_list
):
    extrapolate, derivative, lifting = tables()
    nvars = solution.shape[0]
    elems = solution.shape[2]
    rim_count = elems // 16
    faces_total = 6 * elems
    links = face_link.reshape(faces_total)
    values, speeds = face_rows(solution, face_speed, extrapolate)
    flat_values = values.reshape(faces_total, 16 * nvars)
    outgoing = rim_rows(flat_values, speeds, links, faces_total, rim_count)
    extended = padded(outgoing, (("valve", 0),), rim_count)
    received = jnp.concatenate([extended[:rim_count], extended[3 * rim_count :]], axis=0)
    surface = surface_term(values, speeds, flat_values, links, received, lifting, elems)
    volume = volume_term(solution, velocity, derivative)
    section_rate = -inv_jacobian[None] * (volume + surface)
    advanced = solution + section_step * section_rate
    receptor_vals = receptor_rows(advanced, donor_elem, ref_coords)
    buckets = lax.axis_size("bulk")
    receptors = receptor_vals.shape[1]
    capacity = 2 * receptors // buckets
    owners = owner_list[:, 0]
    ranks = owner_ranks(owners, buckets)
    copies = jnp.asarray(np.tile(np.eye(nvars), (1, buckets)), jnp.float32)
    spread = lax.dot_general(
        receptor_vals, copies, (((0,), (0,)), ((), ())), precision=lax.Precision.HIGHEST
    )
    column_owner = jnp.arange(buckets * nvars, dtype=jnp.int32) // nvars
    masked = jnp.where(owners[:, None] == column_owner[None, :], spread, 0.0)
    hi, lo = split_bf16(masked)
    by_rank = (jnp.arange(capacity, dtype=jnp.int32)[:, None] == ranks[None, :]).astype(jnp.bfloat16)
    both = jnp.dot(by_rank, jnp.concatenate([hi, lo], axis=1), preferred_element_type=jnp.float32)
    placed = both[:, : buckets * nvars] + both[:, buckets * nvars :]
    send = jnp.transpose(placed.reshape(capacity, buckets, nvars), (1, 2, 0))
    got = lax.all_to_all(send, "bulk", 0, 0, tiled=True)
    fringe = jnp.transpose(got, (1, 0, 2)).reshape(nvars, buckets * capacity)
    return (section_rate, fringe)


def solution(mesh):
    placed = (
        P(None, None, ("valve", "bulk")),
        P(None, ("valve", "bulk")),
        P(None, ("valve", "bulk")),
        P(None, ("valve", "bulk")),
        P(None, ("valve", "bulk")),
        P(("valve", "bulk")),
        P(None, ("valve", "bulk")),
        P(("valve", "bulk"), None),
    )
    return jax.shard_map(
        on_device,
        mesh=mesh,
        in_specs=placed,
        out_specs=(P(None, None, ("valve", "bulk")), P(None, ("valve", "bulk"))),
        check_vma=False,
    )
```

```python
import jax
import jax.numpy as jnp
import numpy as np
from jax import lax
from jax.sharding import PartitionSpec as P
from jax.experimental import pallas as pl
from jax.experimental.pallas import tpu as pltpu

gauss_nodes = (-0.8611363115940526, -0.3399810435848563, 0.3399810435848563, 0.8611363115940526)
quad_weights = (0.3478548451374538, 0.6521451548625461, 0.6521451548625461, 0.3478548451374538)
section_step = 0.2


def padded(shard, sides, width):
    for axis, dim in sides:
        size, length = (lax.axis_size(axis), shard.shape[dim])
        up = [(i, (i + 1) % size) for i in range(size)]
        down = [(j, i) for i, j in up]
        last = lax.slice_in_dim(shard, length - width, length, axis=dim)
        initial = lax.slice_in_dim(shard, 0, width, axis=dim)
        before = lax.ppermute(last, axis, up)
        after = lax.ppermute(initial, axis, down)
        shard = jnp.concatenate([before, shard, after], axis=dim)
    return shard


def lagrange_at(x):
    values = []
    for j in range(4):
        factor = 1.0
        for m in range(4):
            if m != j:
                factor = factor * (x - gauss_nodes[m]) / (gauss_nodes[j] - gauss_nodes[m])
        values.append(factor)
    return values


def tables():
    slopes = np.zeros((4, 4))
    for i in range(4):
        for j in range(4):
            summed = 0.0
            for m in range(4):
                if m != j:
                    product = 1.0 / (gauss_nodes[j] - gauss_nodes[m])
                    for n in range(4):
                        if n != j and n != m:
                            product = (
                                product
                                * (gauss_nodes[i] - gauss_nodes[n])
                                / (gauss_nodes[j] - gauss_nodes[n])
                            )
                    summed = summed + product
            slopes[i, j] = summed
    end_values = [lagrange_at(-1.0), lagrange_at(1.0)]
    extrapolate = np.zeros((96, 64))
    lifting = np.zeros((64, 96))
    derivative = np.zeros((3, 64, 64))
    for p in range(64):
        point_idx = (p // 16, p // 4 % 4, p % 4)
        for f in range(6):
            normal_dir = f // 2
            across = [t for t in range(3) if t != normal_dir]
            q = point_idx[across[0]] * 4 + point_idx[across[1]]
            flux_row = q * 6 + f
            extrapolate[flux_row, p] = end_values[f % 2][point_idx[normal_dir]]
            lifting[p, flux_row] = (
                end_values[f % 2][point_idx[normal_dir]] / quad_weights[point_idx[normal_dir]]
            )
        for s in range(64):
            other_idx = (s // 16, s // 4 % 4, s % 4)
            for normal_dir in range(3):
                if all((point_idx[t] == other_idx[t] for t in range(3) if t != normal_dir)):
                    derivative[normal_dir, p, s] = slopes[
                        point_idx[normal_dir], other_idx[normal_dir]
                    ]
    return (
        jnp.asarray(extrapolate, dtype=jnp.float32),
        jnp.asarray(derivative, dtype=jnp.float32),
        jnp.asarray(lifting, dtype=jnp.float32),
    )


def face_rows(solution, face_speed, extrapolate):
    nvars = solution.shape[0]
    elems = solution.shape[2]
    ext_faces = extrapolate.reshape(16, 6, 64)
    values = jnp.einsum("qfp,vpe->feqv", ext_faces, solution, precision=lax.Precision.HIGHEST)
    values = values.reshape(6 * elems, 16, nvars)
    speeds = jnp.transpose(face_speed.reshape(16, 6, elems), (1, 2, 0)).reshape(6 * elems, 16)
    return (values, speeds)


def rim_rows(values, speeds, links, faces_total, rim_count):
    wanted = faces_total + jnp.arange(2 * rim_count, dtype=jnp.int32)
    hits = links[None, :] == wanted[:, None]
    faces = jnp.arange(faces_total, dtype=jnp.int32)[None, :]
    senders = jnp.sum(jnp.where(hits, faces, 0), axis=1)
    return jnp.concatenate(
        [jnp.take(values, senders, axis=0), jnp.take(speeds, senders, axis=0)], axis=1
    )


def split_bf16(x):
    hi = lax.reduce_precision(x, exponent_bits=8, mantissa_bits=7)
    return hi.astype(jnp.bfloat16), (x - hi).astype(jnp.bfloat16)


def pick_dot(rows, onehot):
    hi, lo = split_bf16(rows)
    both = jnp.dot(jnp.concatenate([hi, lo], axis=0), onehot, preferred_element_type=jnp.float32)
    return both[: rows.shape[0]] + both[rows.shape[0] :]


def _exact_spread(x, spread):
    hi = x.astype(jnp.bfloat16)
    rest = x - hi.astype(jnp.float32)
    mid = rest.astype(jnp.bfloat16)
    lo = (rest - mid.astype(jnp.float32)).astype(jnp.bfloat16)
    out = jnp.dot(hi, spread, preferred_element_type=jnp.float32)
    out = out + jnp.dot(mid, spread, preferred_element_type=jnp.float32)
    return out + jnp.dot(lo, spread, preferred_element_type=jnp.float32)


def _jump_kernel(idx_ref, values_ref, speeds_ref, recv_ref, spread_ref, jump_ref, table_ref, outer_ref):
    own_rows, width = values_ref.shape
    table_ref[pl.ds(0, own_rows), pl.ds(0, width)] = values_ref[...]
    table_ref[pl.ds(0, own_rows), pl.ds(width, speeds_ref.shape[1])] = speeds_ref[...]
    table_ref[pl.ds(own_rows, recv_ref.shape[0]), :] = recv_ref[...]

    def body(i, carry):
        base = pl.multiple_of(i * 16, 16)
        for j in range(16):
            row = idx_ref[base + j]
            outer_ref[pl.ds(base + j, 1), :] = table_ref[pl.ds(row, 1), :]
        return carry

    lax.fori_loop(0, own_rows // 16, body, 0)
    chunk = 512
    spread = spread_ref[...]

    def rows(c, carry):
        start = pl.multiple_of(c * chunk, chunk)
        own = table_ref[pl.ds(start, chunk), :]
        other = outer_ref[pl.ds(start, chunk), :]
        own_speed = _exact_spread(own, spread)
        outer_speed = _exact_spread(other, spread)
        own_vals = own[:, :width]
        outer_vals = other[:, :width]
        normal = 0.5 * (own_speed - outer_speed)
        common = 0.5 * normal * (own_vals + outer_vals) + 0.5 * jnp.abs(normal) * (own_vals - outer_vals)
        jump_ref[pl.ds(start, chunk), :] = common - own_speed * own_vals
        return carry

    lax.fori_loop(0, own_rows // chunk, rows, 0)


def jump_rows(values, speeds, received, idx):
    rows = values.shape[0] + received.shape[0]
    full = received.shape[1]
    width = values.shape[1]
    nvars = width // speeds.shape[1]
    spread = np.zeros((full, width))
    for c in range(width):
        spread[width + c // nvars, c] = 1.0
    return pl.pallas_call(
        _jump_kernel,
        out_shape=jax.ShapeDtypeStruct((idx.shape[0], width), values.dtype),
        in_specs=[pl.BlockSpec(memory_space=pltpu.SMEM)]
        + [pl.BlockSpec(memory_space=pltpu.VMEM)] * 4,
        out_specs=pl.BlockSpec(memory_space=pltpu.VMEM),
        scratch_shapes=[
            pltpu.VMEM((rows, full), values.dtype),
            pltpu.VMEM((idx.shape[0], full), values.dtype),
        ],
        cost_estimate=pl.CostEstimate(
            flops=12 * idx.shape[0] * full * width,
            transcendentals=0,
            bytes_accessed=(3 * idx.shape[0] + rows) * full * 4,
        ),
    )(idx, values, speeds, received, jnp.asarray(spread, jnp.bfloat16))


def owner_ranks(owners, buckets):
    receptors = owners.shape[0]
    width = 128
    blocks = receptors // width
    member = owners[None, :] == jnp.arange(buckets, dtype=jnp.int32)[:, None]
    member = member.astype(jnp.bfloat16).reshape(buckets * blocks, width)
    upper = jnp.asarray(np.triu(np.ones((width, width))), jnp.bfloat16)
    inside = jnp.dot(member, upper, preferred_element_type=jnp.float32)
    inside = inside.reshape(buckets, blocks, width)
    totals = inside[:, :, width - 1].astype(jnp.bfloat16)
    strict = jnp.asarray(np.triu(np.ones((blocks, blocks)), 1), jnp.bfloat16)
    offsets = jnp.dot(totals, strict, preferred_element_type=jnp.float32)
    counts = (inside + offsets[:, :, None]).reshape(buckets, receptors)
    picked = jnp.sum(jnp.where(member.reshape(buckets, receptors) > 0, counts, 0.0), axis=0)
    return picked.astype(jnp.int32) - 1


def surface_term(values, speeds, links, received, lifting, elems):
    nvars = received.shape[1] // 16 - 1
    jump_term = jump_rows(values, speeds, received, links).reshape(6, elems, 16, nvars)
    lift_faces = lifting.reshape(64, 16, 6)
    return jnp.einsum("pqf,feqv->vpe", lift_faces, jump_term, precision=lax.Precision.HIGHEST)


def volume_term(solution, velocity, derivative):
    slopes = jnp.einsum("dpq,vqe->dvpe", derivative, solution, precision=lax.Precision.HIGHEST)
    return jnp.sum(velocity[:, None, None, :] * slopes, axis=0)


def _pick_row(basis, first, index):
    out = basis[first : first + 1]
    for i in range(1, 4):
        out = jnp.where(index == i, basis[first + i : first + i + 1], out)
    return out


def _interp_kernel(rows_ref, donors_ref, basis_ref, out_ref):
    elems = rows_ref.shape[1]
    tile = donors_ref.shape[1]
    half = rows_ref.shape[0] // 2
    onehot = lax.broadcasted_iota(jnp.int32, (elems, tile), 0) == donors_ref[...]
    picked = jnp.dot(rows_ref[...], onehot.astype(jnp.bfloat16), preferred_element_type=jnp.float32)
    picked = picked[:half] + picked[half:]
    nvars = out_ref.shape[0]
    points = half // nvars
    basis = basis_ref[...]
    point = lax.broadcasted_iota(jnp.int32, (points, tile), 0)
    weights = (
        _pick_row(basis, 0, point // 16)
        * _pick_row(basis, 4, point // 4 % 4)
        * _pick_row(basis, 8, point % 4)
    )
    picked = picked.reshape(nvars, points, tile) * weights[None]
    out_ref[...] = jnp.sum(picked, axis=1)


def receptor_rows(advanced, donors, coords):
    nvars = advanced.shape[0]
    elems = advanced.shape[2]
    receptors = donors.shape[0]
    basis = jnp.concatenate([jnp.stack(lagrange_at(coords[d])) for d in range(3)], axis=0)
    hi, lo = split_bf16(advanced.reshape(nvars * 64, elems))
    rows = jnp.concatenate([hi, lo], axis=0)
    tile = 512
    return pl.pallas_call(
        _interp_kernel,
        out_shape=jax.ShapeDtypeStruct((nvars, receptors), jnp.float32),
        grid=(receptors // tile,),
        in_specs=[
            pl.BlockSpec((2 * nvars * 64, elems), lambda i: (0, 0)),
            pl.BlockSpec((1, tile), lambda i: (0, i)),
            pl.BlockSpec((12, tile), lambda i: (0, i)),
        ],
        out_specs=pl.BlockSpec((nvars, tile), lambda i: (0, i)),
        cost_estimate=pl.CostEstimate(
            flops=2 * 2 * nvars * 64 * elems * receptors,
            transcendentals=0,
            bytes_accessed=2 * nvars * 64 * elems * 2 + receptors * (1 + 12 + nvars) * 4,
        ),
    )(rows, donors.reshape(1, receptors), basis)


def on_device(
    solution, velocity, inv_jacobian, face_speed, face_link, donor_elem, ref_coords, owner_list
):
    extrapolate, derivative, lifting = tables()
    nvars = solution.shape[0]
    elems = solution.shape[2]
    rim_count = elems // 16
    faces_total = 6 * elems
    links = face_link.reshape(faces_total)
    values, speeds = face_rows(solution, face_speed, extrapolate)
    flat_values = values.reshape(faces_total, 16 * nvars)
    outgoing = rim_rows(flat_values, speeds, links, faces_total, rim_count)
    extended = padded(outgoing, (("valve", 0),), rim_count)
    received = jnp.concatenate([extended[:rim_count], extended[3 * rim_count :]], axis=0)
    surface = surface_term(flat_values, speeds, links, received, lifting, elems)
    volume = volume_term(solution, velocity, derivative)
    section_rate = -inv_jacobian[None] * (volume + surface)
    advanced = solution + section_step * section_rate
    receptor_vals = receptor_rows(advanced, donor_elem, ref_coords)
    buckets = lax.axis_size("bulk")
    receptors = receptor_vals.shape[1]
    capacity = 2 * receptors // buckets
    owners = owner_list[:, 0]
    ranks = owner_ranks(owners, buckets)
    copies = jnp.asarray(np.tile(np.eye(nvars), (1, buckets)), jnp.float32)
    spread = lax.dot_general(
        receptor_vals, copies, (((0,), (0,)), ((), ())), precision=lax.Precision.HIGHEST
    )
    column_owner = jnp.arange(buckets * nvars, dtype=jnp.int32) // nvars
    masked = jnp.where(owners[:, None] == column_owner[None, :], spread, 0.0)
    hi, lo = split_bf16(masked)
    by_rank = (jnp.arange(capacity, dtype=jnp.int32)[:, None] == ranks[None, :]).astype(jnp.bfloat16)
    both = jnp.dot(by_rank, jnp.concatenate([hi, lo], axis=1), preferred_element_type=jnp.float32)
    placed = both[:, : buckets * nvars] + both[:, buckets * nvars :]
    send = jnp.transpose(placed.reshape(capacity, buckets, nvars), (1, 2, 0))
    got = lax.all_to_all(send, "bulk", 0, 0, tiled=True)
    fringe = jnp.transpose(got, (1, 0, 2)).reshape(nvars, buckets * capacity)
    return (section_rate, fringe)


def solution(mesh):
    placed = (
        P(None, None, ("valve", "bulk")),
        P(None, ("valve", "bulk")),
        P(None, ("valve", "bulk")),
        P(None, ("valve", "bulk")),
        P(None, ("valve", "bulk")),
        P(("valve", "bulk")),
        P(None, ("valve", "bulk")),
        P(("valve", "bulk"), None),
    )
    return jax.shard_map(
        on_device,
        mesh=mesh,
        in_specs=placed,
        out_specs=(P(None, None, ("valve", "bulk")), P(None, ("valve", "bulk"))),
        check_vma=False,
    )
```

```python
import jax
import jax.numpy as jnp
import numpy as np
from jax import lax
from jax.sharding import PartitionSpec as P
from jax.experimental import pallas as pl
from jax.experimental.pallas import tpu as pltpu

gauss_nodes = (-0.8611363115940526, -0.3399810435848563, 0.3399810435848563, 0.8611363115940526)
quad_weights = (0.3478548451374538, 0.6521451548625461, 0.6521451548625461, 0.3478548451374538)
section_step = 0.2


def padded(shard, sides, width):
    for axis, dim in sides:
        size, length = (lax.axis_size(axis), shard.shape[dim])
        up = [(i, (i + 1) % size) for i in range(size)]
        down = [(j, i) for i, j in up]
        last = lax.slice_in_dim(shard, length - width, length, axis=dim)
        initial = lax.slice_in_dim(shard, 0, width, axis=dim)
        before = lax.ppermute(last, axis, up)
        after = lax.ppermute(initial, axis, down)
        shard = jnp.concatenate([before, shard, after], axis=dim)
    return shard


def lagrange_at(x):
    values = []
    for j in range(4):
        factor = 1.0
        for m in range(4):
            if m != j:
                factor = factor * (x - gauss_nodes[m]) / (gauss_nodes[j] - gauss_nodes[m])
        values.append(factor)
    return values


def tables():
    slopes = np.zeros((4, 4))
    for i in range(4):
        for j in range(4):
            summed = 0.0
            for m in range(4):
                if m != j:
                    product = 1.0 / (gauss_nodes[j] - gauss_nodes[m])
                    for n in range(4):
                        if n != j and n != m:
                            product = (
                                product
                                * (gauss_nodes[i] - gauss_nodes[n])
                                / (gauss_nodes[j] - gauss_nodes[n])
                            )
                    summed = summed + product
            slopes[i, j] = summed
    end_values = [lagrange_at(-1.0), lagrange_at(1.0)]
    extrapolate = np.zeros((96, 64))
    lifting = np.zeros((64, 96))
    derivative = np.zeros((3, 64, 64))
    for p in range(64):
        point_idx = (p // 16, p // 4 % 4, p % 4)
        for f in range(6):
            normal_dir = f // 2
            across = [t for t in range(3) if t != normal_dir]
            q = point_idx[across[0]] * 4 + point_idx[across[1]]
            flux_row = q * 6 + f
            extrapolate[flux_row, p] = end_values[f % 2][point_idx[normal_dir]]
            lifting[p, flux_row] = (
                end_values[f % 2][point_idx[normal_dir]] / quad_weights[point_idx[normal_dir]]
            )
        for s in range(64):
            other_idx = (s // 16, s // 4 % 4, s % 4)
            for normal_dir in range(3):
                if all((point_idx[t] == other_idx[t] for t in range(3) if t != normal_dir)):
                    derivative[normal_dir, p, s] = slopes[
                        point_idx[normal_dir], other_idx[normal_dir]
                    ]
    return (
        jnp.asarray(extrapolate, dtype=jnp.float32),
        jnp.asarray(derivative, dtype=jnp.float32),
        jnp.asarray(lifting, dtype=jnp.float32),
    )


def face_rows(solution, face_speed, extrapolate):
    nvars = solution.shape[0]
    elems = solution.shape[2]
    ext_faces = extrapolate.reshape(16, 6, 64)
    values = jnp.einsum("qfp,vpe->feqv", ext_faces, solution, precision=lax.Precision.HIGHEST)
    values = values.reshape(6 * elems, 16, nvars)
    speeds = jnp.transpose(face_speed.reshape(16, 6, elems), (1, 2, 0)).reshape(6 * elems, 16)
    return (values, speeds)


def rim_rows(values, speeds, links, faces_total, rim_count):
    wanted = faces_total + jnp.arange(2 * rim_count, dtype=jnp.int32)
    hits = links[None, :] == wanted[:, None]
    faces = jnp.arange(faces_total, dtype=jnp.int32)[None, :]
    senders = jnp.sum(jnp.where(hits, faces, 0), axis=1)
    return jnp.concatenate(
        [jnp.take(values, senders, axis=0), jnp.take(speeds, senders, axis=0)], axis=1
    )


def split_bf16(x):
    hi = lax.reduce_precision(x, exponent_bits=8, mantissa_bits=7)
    return hi.astype(jnp.bfloat16), (x - hi).astype(jnp.bfloat16)


def pick_dot(rows, onehot):
    hi, lo = split_bf16(rows)
    both = jnp.dot(jnp.concatenate([hi, lo], axis=0), onehot, preferred_element_type=jnp.float32)
    return both[: rows.shape[0]] + both[rows.shape[0] :]


def _exact_spread(x, spread):
    hi = x.astype(jnp.bfloat16)
    rest = x - hi.astype(jnp.float32)
    mid = rest.astype(jnp.bfloat16)
    lo = (rest - mid.astype(jnp.float32)).astype(jnp.bfloat16)
    out = jnp.dot(hi, spread, preferred_element_type=jnp.float32)
    out = out + jnp.dot(mid, spread, preferred_element_type=jnp.float32)
    return out + jnp.dot(lo, spread, preferred_element_type=jnp.float32)


def _jump_kernel(idx_ref, values_ref, speeds_ref, recv_ref, spread_ref, jump_ref, table_ref, outer_ref):
    own_rows, width = values_ref.shape
    table_ref[pl.ds(0, own_rows), pl.ds(0, width)] = values_ref[...]
    table_ref[pl.ds(0, own_rows), pl.ds(width, speeds_ref.shape[1])] = speeds_ref[...]
    table_ref[pl.ds(own_rows, recv_ref.shape[0]), :] = recv_ref[...]

    def body(i, carry):
        base = pl.multiple_of(i * 16, 16)
        for j in range(16):
            row = idx_ref[base + j]
            outer_ref[pl.ds(base + j, 1), :] = table_ref[pl.ds(row, 1), :]
        return carry

    lax.fori_loop(0, own_rows // 16, body, 0)
    chunk = 512
    spread = spread_ref[...]

    def rows(c, carry):
        start = pl.multiple_of(c * chunk, chunk)
        own = table_ref[pl.ds(start, chunk), :]
        other = outer_ref[pl.ds(start, chunk), :]
        own_speed = _exact_spread(own, spread)
        outer_speed = _exact_spread(other, spread)
        own_vals = own[:, :width]
        outer_vals = other[:, :width]
        normal = 0.5 * (own_speed - outer_speed)
        common = 0.5 * normal * (own_vals + outer_vals) + 0.5 * jnp.abs(normal) * (own_vals - outer_vals)
        jump_ref[pl.ds(start, chunk), :] = common - own_speed * own_vals
        return carry

    lax.fori_loop(0, own_rows // chunk, rows, 0)


def jump_rows(values, speeds, received, idx):
    rows = values.shape[0] + received.shape[0]
    full = received.shape[1]
    width = values.shape[1]
    nvars = width // speeds.shape[1]
    spread = np.zeros((full, width))
    for c in range(width):
        spread[width + c // nvars, c] = 1.0
    return pl.pallas_call(
        _jump_kernel,
        out_shape=jax.ShapeDtypeStruct((idx.shape[0], width), values.dtype),
        in_specs=[pl.BlockSpec(memory_space=pltpu.SMEM)]
        + [pl.BlockSpec(memory_space=pltpu.VMEM)] * 4,
        out_specs=pl.BlockSpec(memory_space=pltpu.VMEM),
        scratch_shapes=[
            pltpu.VMEM((rows, full), values.dtype),
            pltpu.VMEM((idx.shape[0], full), values.dtype),
        ],
        cost_estimate=pl.CostEstimate(
            flops=12 * idx.shape[0] * full * width,
            transcendentals=0,
            bytes_accessed=(3 * idx.shape[0] + rows) * full * 4,
        ),
    )(idx, values, speeds, received, jnp.asarray(spread, jnp.bfloat16))


def owner_ranks(owners, buckets):
    receptors = owners.shape[0]
    width = 128
    blocks = receptors // width
    member = owners[None, :] == jnp.arange(buckets, dtype=jnp.int32)[:, None]
    member = member.astype(jnp.bfloat16).reshape(buckets * blocks, width)
    upper = jnp.asarray(np.triu(np.ones((width, width))), jnp.bfloat16)
    inside = jnp.dot(member, upper, preferred_element_type=jnp.float32)
    inside = inside.reshape(buckets, blocks, width)
    totals = inside[:, :, width - 1].astype(jnp.bfloat16)
    strict = jnp.asarray(np.triu(np.ones((blocks, blocks)), 1), jnp.bfloat16)
    offsets = jnp.dot(totals, strict, preferred_element_type=jnp.float32)
    counts = (inside + offsets[:, :, None]).reshape(buckets, receptors)
    picked = jnp.sum(jnp.where(member.reshape(buckets, receptors) > 0, counts, 0.0), axis=0)
    return picked.astype(jnp.int32) - 1


def surface_term(values, speeds, links, received, lifting, elems):
    nvars = received.shape[1] // 16 - 1
    jump_term = jump_rows(values, speeds, received, links).reshape(6, elems, 16, nvars)
    lift_faces = lifting.reshape(64, 16, 6)
    return jnp.einsum("pqf,feqv->vpe", lift_faces, jump_term, precision=lax.Precision.HIGHEST)


def volume_term(solution, velocity, derivative):
    slopes = jnp.einsum("dpq,vqe->dvpe", derivative, solution, precision=lax.Precision.HIGHEST)
    return jnp.sum(velocity[:, None, None, :] * slopes, axis=0)


def _pick_row(basis, first, index):
    out = basis[first : first + 1]
    for i in range(1, 4):
        out = jnp.where(index == i, basis[first + i : first + i + 1], out)
    return out


def _interp_kernel(rows_ref, donors_ref, basis_ref, out_ref):
    elems = rows_ref.shape[1]
    tile = donors_ref.shape[1]
    half = rows_ref.shape[0] // 2
    onehot = lax.broadcasted_iota(jnp.int32, (elems, tile), 0) == donors_ref[...]
    picked = jnp.dot(rows_ref[...], onehot.astype(jnp.bfloat16), preferred_element_type=jnp.float32)
    picked = picked[:half] + picked[half:]
    nvars = out_ref.shape[0]
    points = half // nvars
    basis = basis_ref[...]
    point = lax.broadcasted_iota(jnp.int32, (points, tile), 0)
    weights = (
        _pick_row(basis, 0, point // 16)
        * _pick_row(basis, 4, point // 4 % 4)
        * _pick_row(basis, 8, point % 4)
    )
    picked = picked.reshape(nvars, points, tile) * weights[None]
    out_ref[...] = jnp.sum(picked, axis=1)


def receptor_rows(advanced, donors, coords):
    nvars = advanced.shape[0]
    elems = advanced.shape[2]
    receptors = donors.shape[0]
    basis = jnp.concatenate([jnp.stack(lagrange_at(coords[d])) for d in range(3)], axis=0)
    hi, lo = split_bf16(advanced.reshape(nvars * 64, elems))
    rows = jnp.concatenate([hi, lo], axis=0)
    tile = 1024
    return pl.pallas_call(
        _interp_kernel,
        out_shape=jax.ShapeDtypeStruct((nvars, receptors), jnp.float32),
        grid=(receptors // tile,),
        in_specs=[
            pl.BlockSpec((2 * nvars * 64, elems), lambda i: (0, 0)),
            pl.BlockSpec((1, tile), lambda i: (0, i)),
            pl.BlockSpec((12, tile), lambda i: (0, i)),
        ],
        out_specs=pl.BlockSpec((nvars, tile), lambda i: (0, i)),
        cost_estimate=pl.CostEstimate(
            flops=2 * 2 * nvars * 64 * elems * receptors,
            transcendentals=0,
            bytes_accessed=2 * nvars * 64 * elems * 2 + receptors * (1 + 12 + nvars) * 4,
        ),
    )(rows, donors.reshape(1, receptors), basis)


def on_device(
    solution, velocity, inv_jacobian, face_speed, face_link, donor_elem, ref_coords, owner_list
):
    extrapolate, derivative, lifting = tables()
    nvars = solution.shape[0]
    elems = solution.shape[2]
    rim_count = elems // 16
    faces_total = 6 * elems
    links = face_link.reshape(faces_total)
    values, speeds = face_rows(solution, face_speed, extrapolate)
    flat_values = values.reshape(faces_total, 16 * nvars)
    outgoing = rim_rows(flat_values, speeds, links, faces_total, rim_count)
    extended = padded(outgoing, (("valve", 0),), rim_count)
    received = jnp.concatenate([extended[:rim_count], extended[3 * rim_count :]], axis=0)
    surface = surface_term(flat_values, speeds, links, received, lifting, elems)
    volume = volume_term(solution, velocity, derivative)
    section_rate = -inv_jacobian[None] * (volume + surface)
    advanced = solution + section_step * section_rate
    receptor_vals = receptor_rows(advanced, donor_elem, ref_coords)
    buckets = lax.axis_size("bulk")
    receptors = receptor_vals.shape[1]
    capacity = 2 * receptors // buckets
    owners = owner_list[:, 0]
    ranks = owner_ranks(owners, buckets)
    copies = jnp.asarray(np.tile(np.eye(nvars), (1, buckets)), jnp.float32)
    spread = lax.dot_general(
        receptor_vals, copies, (((0,), (0,)), ((), ())), precision=lax.Precision.HIGHEST
    )
    column_owner = jnp.arange(buckets * nvars, dtype=jnp.int32) // nvars
    masked = jnp.where(owners[:, None] == column_owner[None, :], spread, 0.0)
    hi, lo = split_bf16(masked)
    by_rank = (jnp.arange(capacity, dtype=jnp.int32)[:, None] == ranks[None, :]).astype(jnp.bfloat16)
    both = jnp.dot(by_rank, jnp.concatenate([hi, lo], axis=1), preferred_element_type=jnp.float32)
    placed = both[:, : buckets * nvars] + both[:, buckets * nvars :]
    send = jnp.transpose(placed.reshape(capacity, buckets, nvars), (1, 2, 0))
    got = lax.all_to_all(send, "bulk", 0, 0, tiled=True)
    fringe = jnp.transpose(got, (1, 0, 2)).reshape(nvars, buckets * capacity)
    return (section_rate, fringe)


def solution(mesh):
    placed = (
        P(None, None, ("valve", "bulk")),
        P(None, ("valve", "bulk")),
        P(None, ("valve", "bulk")),
        P(None, ("valve", "bulk")),
        P(None, ("valve", "bulk")),
        P(("valve", "bulk")),
        P(None, ("valve", "bulk")),
        P(("valve", "bulk"), None),
    )
    return jax.shard_map(
        on_device,
        mesh=mesh,
        in_specs=placed,
        out_specs=(P(None, None, ("valve", "bulk")), P(None, ("valve", "bulk"))),
        check_vma=False,
    )
```

```python
import jax
import jax.numpy as jnp
import numpy as np
from jax import lax
from jax.sharding import PartitionSpec as P
from jax.experimental import pallas as pl
from jax.experimental.pallas import tpu as pltpu

gauss_nodes = (-0.8611363115940526, -0.3399810435848563, 0.3399810435848563, 0.8611363115940526)
quad_weights = (0.3478548451374538, 0.6521451548625461, 0.6521451548625461, 0.3478548451374538)
section_step = 0.2


def padded(shard, sides, width):
    for axis, dim in sides:
        size, length = (lax.axis_size(axis), shard.shape[dim])
        up = [(i, (i + 1) % size) for i in range(size)]
        down = [(j, i) for i, j in up]
        last = lax.slice_in_dim(shard, length - width, length, axis=dim)
        initial = lax.slice_in_dim(shard, 0, width, axis=dim)
        before = lax.ppermute(last, axis, up)
        after = lax.ppermute(initial, axis, down)
        shard = jnp.concatenate([before, shard, after], axis=dim)
    return shard


def lagrange_at(x):
    values = []
    for j in range(4):
        factor = 1.0
        for m in range(4):
            if m != j:
                factor = factor * (x - gauss_nodes[m]) / (gauss_nodes[j] - gauss_nodes[m])
        values.append(factor)
    return values


def tables():
    slopes = np.zeros((4, 4))
    for i in range(4):
        for j in range(4):
            summed = 0.0
            for m in range(4):
                if m != j:
                    product = 1.0 / (gauss_nodes[j] - gauss_nodes[m])
                    for n in range(4):
                        if n != j and n != m:
                            product = (
                                product
                                * (gauss_nodes[i] - gauss_nodes[n])
                                / (gauss_nodes[j] - gauss_nodes[n])
                            )
                    summed = summed + product
            slopes[i, j] = summed
    end_values = [lagrange_at(-1.0), lagrange_at(1.0)]
    extrapolate = np.zeros((96, 64))
    lifting = np.zeros((64, 96))
    derivative = np.zeros((3, 64, 64))
    for p in range(64):
        point_idx = (p // 16, p // 4 % 4, p % 4)
        for f in range(6):
            normal_dir = f // 2
            across = [t for t in range(3) if t != normal_dir]
            q = point_idx[across[0]] * 4 + point_idx[across[1]]
            flux_row = q * 6 + f
            extrapolate[flux_row, p] = end_values[f % 2][point_idx[normal_dir]]
            lifting[p, flux_row] = (
                end_values[f % 2][point_idx[normal_dir]] / quad_weights[point_idx[normal_dir]]
            )
        for s in range(64):
            other_idx = (s // 16, s // 4 % 4, s % 4)
            for normal_dir in range(3):
                if all((point_idx[t] == other_idx[t] for t in range(3) if t != normal_dir)):
                    derivative[normal_dir, p, s] = slopes[
                        point_idx[normal_dir], other_idx[normal_dir]
                    ]
    return (
        jnp.asarray(extrapolate, dtype=jnp.float32),
        jnp.asarray(derivative, dtype=jnp.float32),
        jnp.asarray(lifting, dtype=jnp.float32),
    )


def face_rows(solution, face_speed, extrapolate):
    nvars = solution.shape[0]
    elems = solution.shape[2]
    ext_faces = extrapolate.reshape(16, 6, 64)
    values = jnp.einsum("qfp,vpe->feqv", ext_faces, solution, precision=lax.Precision.HIGHEST)
    values = values.reshape(6 * elems, 16, nvars)
    speeds = jnp.transpose(face_speed.reshape(16, 6, elems), (1, 2, 0)).reshape(6 * elems, 16)
    return (values, speeds)


def rim_rows(values, speeds, links, faces_total, rim_count):
    wanted = faces_total + jnp.arange(2 * rim_count, dtype=jnp.int32)
    hits = links[None, :] == wanted[:, None]
    faces = jnp.arange(faces_total, dtype=jnp.int32)[None, :]
    senders = jnp.sum(jnp.where(hits, faces, 0), axis=1)
    return jnp.concatenate(
        [jnp.take(values, senders, axis=0), jnp.take(speeds, senders, axis=0)], axis=1
    )


def split_bf16(x):
    hi = lax.reduce_precision(x, exponent_bits=8, mantissa_bits=7)
    return hi.astype(jnp.bfloat16), (x - hi).astype(jnp.bfloat16)


def pick_dot(rows, onehot):
    hi, lo = split_bf16(rows)
    both = jnp.dot(jnp.concatenate([hi, lo], axis=0), onehot, preferred_element_type=jnp.float32)
    return both[: rows.shape[0]] + both[rows.shape[0] :]


def _exact_spread(x, spread):
    hi = x.astype(jnp.bfloat16)
    rest = x - hi.astype(jnp.float32)
    mid = rest.astype(jnp.bfloat16)
    lo = (rest - mid.astype(jnp.float32)).astype(jnp.bfloat16)
    out = jnp.dot(hi, spread, preferred_element_type=jnp.float32)
    out = out + jnp.dot(mid, spread, preferred_element_type=jnp.float32)
    return out + jnp.dot(lo, spread, preferred_element_type=jnp.float32)


def _jump_kernel(idx_ref, values_ref, speeds_ref, recv_ref, spread_ref, jump_ref, table_ref, outer_ref):
    own_rows, width = values_ref.shape
    table_ref[pl.ds(0, own_rows), pl.ds(0, width)] = values_ref[...]
    table_ref[pl.ds(0, own_rows), pl.ds(width, speeds_ref.shape[1])] = speeds_ref[...]
    table_ref[pl.ds(own_rows, recv_ref.shape[0]), :] = recv_ref[...]

    def body(i, carry):
        base = pl.multiple_of(i * 16, 16)
        for j in range(16):
            row = idx_ref[base + j]
            outer_ref[pl.ds(base + j, 1), :] = table_ref[pl.ds(row, 1), :]
        return carry

    lax.fori_loop(0, own_rows // 16, body, 0)
    chunk = 512
    spread = spread_ref[...]

    def rows(c, carry):
        start = pl.multiple_of(c * chunk, chunk)
        own = table_ref[pl.ds(start, chunk), :]
        other = outer_ref[pl.ds(start, chunk), :]
        own_speed = _exact_spread(own, spread)
        outer_speed = _exact_spread(other, spread)
        own_vals = own[:, :width]
        outer_vals = other[:, :width]
        normal = 0.5 * (own_speed - outer_speed)
        common = 0.5 * normal * (own_vals + outer_vals) + 0.5 * jnp.abs(normal) * (own_vals - outer_vals)
        jump_ref[pl.ds(start, chunk), :] = common - own_speed * own_vals
        return carry

    lax.fori_loop(0, own_rows // chunk, rows, 0)


def jump_rows(values, speeds, received, idx):
    rows = values.shape[0] + received.shape[0]
    full = received.shape[1]
    width = values.shape[1]
    nvars = width // speeds.shape[1]
    spread = np.zeros((full, width))
    for c in range(width):
        spread[width + c // nvars, c] = 1.0
    return pl.pallas_call(
        _jump_kernel,
        out_shape=jax.ShapeDtypeStruct((idx.shape[0], width), values.dtype),
        in_specs=[pl.BlockSpec(memory_space=pltpu.SMEM)]
        + [pl.BlockSpec(memory_space=pltpu.VMEM)] * 4,
        out_specs=pl.BlockSpec(memory_space=pltpu.VMEM),
        scratch_shapes=[
            pltpu.VMEM((rows, full), values.dtype),
            pltpu.VMEM((idx.shape[0], full), values.dtype),
        ],
        cost_estimate=pl.CostEstimate(
            flops=12 * idx.shape[0] * full * width,
            transcendentals=0,
            bytes_accessed=(3 * idx.shape[0] + rows) * full * 4,
        ),
    )(idx, values, speeds, received, jnp.asarray(spread, jnp.bfloat16))


def owner_ranks(owners, buckets):
    receptors = owners.shape[0]
    width = 128
    blocks = receptors // width
    member = owners[None, :] == jnp.arange(buckets, dtype=jnp.int32)[:, None]
    member = member.astype(jnp.bfloat16).reshape(buckets * blocks, width)
    upper = jnp.asarray(np.triu(np.ones((width, width))), jnp.bfloat16)
    inside = jnp.dot(member, upper, preferred_element_type=jnp.float32)
    inside = inside.reshape(buckets, blocks, width)
    totals = inside[:, :, width - 1].astype(jnp.bfloat16)
    strict = jnp.asarray(np.triu(np.ones((blocks, blocks)), 1), jnp.bfloat16)
    offsets = jnp.dot(totals, strict, preferred_element_type=jnp.float32)
    counts = (inside + offsets[:, :, None]).reshape(buckets, receptors)
    picked = jnp.sum(jnp.where(member.reshape(buckets, receptors) > 0, counts, 0.0), axis=0)
    return picked.astype(jnp.int32) - 1


def surface_term(values, speeds, links, received, lifting, elems):
    nvars = received.shape[1] // 16 - 1
    jump_term = jump_rows(values, speeds, received, links).reshape(6, elems, 16, nvars)
    lift_faces = lifting.reshape(64, 16, 6)
    return jnp.einsum("pqf,feqv->vpe", lift_faces, jump_term, precision=lax.Precision.HIGHEST)


def volume_term(solution, velocity, derivative):
    slopes = jnp.einsum("dpq,vqe->dvpe", derivative, solution, precision=lax.Precision.HIGHEST)
    return jnp.sum(velocity[:, None, None, :] * slopes, axis=0)


def _pick_row(basis, first, index):
    out = basis[first : first + 1]
    for i in range(1, 4):
        out = jnp.where(index == i, basis[first + i : first + i + 1], out)
    return out


def _interp_kernel(rows_ref, donors_ref, basis_ref, out_ref):
    elems = rows_ref.shape[1]
    tile = donors_ref.shape[1]
    half = rows_ref.shape[0] // 2
    onehot = lax.broadcasted_iota(jnp.int32, (elems, tile), 0) == donors_ref[...]
    picked = jnp.dot(rows_ref[...], onehot.astype(jnp.bfloat16), preferred_element_type=jnp.float32)
    picked = picked[:half] + picked[half:]
    nvars = out_ref.shape[0]
    points = half // nvars
    basis = basis_ref[...]
    point = lax.broadcasted_iota(jnp.int32, (points, tile), 0)
    weights = (
        _pick_row(basis, 0, point // 16)
        * _pick_row(basis, 4, point // 4 % 4)
        * _pick_row(basis, 8, point % 4)
    )
    picked = picked.reshape(nvars, points, tile) * weights[None]
    out_ref[...] = jnp.sum(picked, axis=1)


def receptor_rows(advanced, donors, coords):
    nvars = advanced.shape[0]
    elems = advanced.shape[2]
    receptors = donors.shape[0]
    basis = jnp.concatenate([jnp.stack(lagrange_at(coords[d])) for d in range(3)], axis=0)
    hi, lo = split_bf16(advanced.reshape(nvars * 64, elems))
    rows = jnp.concatenate([hi, lo], axis=0)
    tile = 2048
    return pl.pallas_call(
        _interp_kernel,
        out_shape=jax.ShapeDtypeStruct((nvars, receptors), jnp.float32),
        grid=(receptors // tile,),
        in_specs=[
            pl.BlockSpec((2 * nvars * 64, elems), lambda i: (0, 0)),
            pl.BlockSpec((1, tile), lambda i: (0, i)),
            pl.BlockSpec((12, tile), lambda i: (0, i)),
        ],
        out_specs=pl.BlockSpec((nvars, tile), lambda i: (0, i)),
        cost_estimate=pl.CostEstimate(
            flops=2 * 2 * nvars * 64 * elems * receptors,
            transcendentals=0,
            bytes_accessed=2 * nvars * 64 * elems * 2 + receptors * (1 + 12 + nvars) * 4,
        ),
    )(rows, donors.reshape(1, receptors), basis)


def on_device(
    solution, velocity, inv_jacobian, face_speed, face_link, donor_elem, ref_coords, owner_list
):
    extrapolate, derivative, lifting = tables()
    nvars = solution.shape[0]
    elems = solution.shape[2]
    rim_count = elems // 16
    faces_total = 6 * elems
    links = face_link.reshape(faces_total)
    values, speeds = face_rows(solution, face_speed, extrapolate)
    flat_values = values.reshape(faces_total, 16 * nvars)
    outgoing = rim_rows(flat_values, speeds, links, faces_total, rim_count)
    extended = padded(outgoing, (("valve", 0),), rim_count)
    received = jnp.concatenate([extended[:rim_count], extended[3 * rim_count :]], axis=0)
    surface = surface_term(flat_values, speeds, links, received, lifting, elems)
    volume = volume_term(solution, velocity, derivative)
    section_rate = -inv_jacobian[None] * (volume + surface)
    advanced = solution + section_step * section_rate
    receptor_vals = receptor_rows(advanced, donor_elem, ref_coords)
    buckets = lax.axis_size("bulk")
    receptors = receptor_vals.shape[1]
    capacity = 2 * receptors // buckets
    owners = owner_list[:, 0]
    ranks = owner_ranks(owners, buckets)
    copies = jnp.asarray(np.tile(np.eye(nvars), (1, buckets)), jnp.float32)
    spread = lax.dot_general(
        receptor_vals, copies, (((0,), (0,)), ((), ())), precision=lax.Precision.HIGHEST
    )
    column_owner = jnp.arange(buckets * nvars, dtype=jnp.int32) // nvars
    masked = jnp.where(owners[:, None] == column_owner[None, :], spread, 0.0)
    hi, lo = split_bf16(masked)
    by_rank = (jnp.arange(capacity, dtype=jnp.int32)[:, None] == ranks[None, :]).astype(jnp.bfloat16)
    both = jnp.dot(by_rank, jnp.concatenate([hi, lo], axis=1), preferred_element_type=jnp.float32)
    placed = both[:, : buckets * nvars] + both[:, buckets * nvars :]
    send = jnp.transpose(placed.reshape(capacity, buckets, nvars), (1, 2, 0))
    got = lax.all_to_all(send, "bulk", 0, 0, tiled=True)
    fringe = jnp.transpose(got, (1, 0, 2)).reshape(nvars, buckets * capacity)
    return (section_rate, fringe)


def solution(mesh):
    placed = (
        P(None, None, ("valve", "bulk")),
        P(None, ("valve", "bulk")),
        P(None, ("valve", "bulk")),
        P(None, ("valve", "bulk")),
        P(None, ("valve", "bulk")),
        P(("valve", "bulk")),
        P(None, ("valve", "bulk")),
        P(("valve", "bulk"), None),
    )
    return jax.shard_map(
        on_device,
        mesh=mesh,
        in_specs=placed,
        out_specs=(P(None, None, ("valve", "bulk")), P(None, ("valve", "bulk"))),
        check_vma=False,
    )
```

```python
import jax
import jax.numpy as jnp
import numpy as np
from jax import lax
from jax.sharding import PartitionSpec as P
from jax.experimental import pallas as pl
from jax.experimental.pallas import tpu as pltpu

gauss_nodes = (-0.8611363115940526, -0.3399810435848563, 0.3399810435848563, 0.8611363115940526)
quad_weights = (0.3478548451374538, 0.6521451548625461, 0.6521451548625461, 0.3478548451374538)
section_step = 0.2


def padded(shard, sides, width):
    for axis, dim in sides:
        size, length = (lax.axis_size(axis), shard.shape[dim])
        up = [(i, (i + 1) % size) for i in range(size)]
        down = [(j, i) for i, j in up]
        last = lax.slice_in_dim(shard, length - width, length, axis=dim)
        initial = lax.slice_in_dim(shard, 0, width, axis=dim)
        before = lax.ppermute(last, axis, up)
        after = lax.ppermute(initial, axis, down)
        shard = jnp.concatenate([before, shard, after], axis=dim)
    return shard


def lagrange_at(x):
    values = []
    for j in range(4):
        factor = 1.0
        for m in range(4):
            if m != j:
                factor = factor * (x - gauss_nodes[m]) / (gauss_nodes[j] - gauss_nodes[m])
        values.append(factor)
    return values


def tables():
    slopes = np.zeros((4, 4))
    for i in range(4):
        for j in range(4):
            summed = 0.0
            for m in range(4):
                if m != j:
                    product = 1.0 / (gauss_nodes[j] - gauss_nodes[m])
                    for n in range(4):
                        if n != j and n != m:
                            product = (
                                product
                                * (gauss_nodes[i] - gauss_nodes[n])
                                / (gauss_nodes[j] - gauss_nodes[n])
                            )
                    summed = summed + product
            slopes[i, j] = summed
    end_values = [lagrange_at(-1.0), lagrange_at(1.0)]
    extrapolate = np.zeros((96, 64))
    lifting = np.zeros((64, 96))
    derivative = np.zeros((3, 64, 64))
    for p in range(64):
        point_idx = (p // 16, p // 4 % 4, p % 4)
        for f in range(6):
            normal_dir = f // 2
            across = [t for t in range(3) if t != normal_dir]
            q = point_idx[across[0]] * 4 + point_idx[across[1]]
            flux_row = q * 6 + f
            extrapolate[flux_row, p] = end_values[f % 2][point_idx[normal_dir]]
            lifting[p, flux_row] = (
                end_values[f % 2][point_idx[normal_dir]] / quad_weights[point_idx[normal_dir]]
            )
        for s in range(64):
            other_idx = (s // 16, s // 4 % 4, s % 4)
            for normal_dir in range(3):
                if all((point_idx[t] == other_idx[t] for t in range(3) if t != normal_dir)):
                    derivative[normal_dir, p, s] = slopes[
                        point_idx[normal_dir], other_idx[normal_dir]
                    ]
    return (
        jnp.asarray(extrapolate, dtype=jnp.float32),
        jnp.asarray(derivative, dtype=jnp.float32),
        jnp.asarray(lifting, dtype=jnp.float32),
    )


def face_rows(solution, face_speed, extrapolate):
    nvars = solution.shape[0]
    elems = solution.shape[2]
    ext_faces = extrapolate.reshape(16, 6, 64)
    values = jnp.einsum("qfp,vpe->feqv", ext_faces, solution, precision=lax.Precision.HIGHEST)
    values = values.reshape(6 * elems, 16, nvars)
    speeds = jnp.transpose(face_speed.reshape(16, 6, elems), (1, 2, 0)).reshape(6 * elems, 16)
    return (values, speeds)


def rim_rows(values, speeds, links, faces_total, rim_count):
    wanted = faces_total + jnp.arange(2 * rim_count, dtype=jnp.int32)
    hits = links[None, :] == wanted[:, None]
    faces = jnp.arange(faces_total, dtype=jnp.int32)[None, :]
    senders = jnp.sum(jnp.where(hits, faces, 0), axis=1)
    return jnp.concatenate(
        [jnp.take(values, senders, axis=0), jnp.take(speeds, senders, axis=0)], axis=1
    )


def split_bf16(x):
    hi = lax.reduce_precision(x, exponent_bits=8, mantissa_bits=7)
    return hi.astype(jnp.bfloat16), (x - hi).astype(jnp.bfloat16)


def pick_dot(rows, onehot):
    hi, lo = split_bf16(rows)
    both = jnp.dot(jnp.concatenate([hi, lo], axis=0), onehot, preferred_element_type=jnp.float32)
    return both[: rows.shape[0]] + both[rows.shape[0] :]


def _exact_spread(x, spread):
    hi = x.astype(jnp.bfloat16)
    rest = x - hi.astype(jnp.float32)
    mid = rest.astype(jnp.bfloat16)
    lo = (rest - mid.astype(jnp.float32)).astype(jnp.bfloat16)
    out = jnp.dot(hi, spread, preferred_element_type=jnp.float32)
    out = out + jnp.dot(mid, spread, preferred_element_type=jnp.float32)
    return out + jnp.dot(lo, spread, preferred_element_type=jnp.float32)


def _jump_kernel(idx_ref, values_ref, speeds_ref, recv_ref, spread_ref, jump_ref, table_ref, outer_ref):
    own_rows, width = values_ref.shape
    table_ref[pl.ds(0, own_rows), pl.ds(0, width)] = values_ref[...]
    table_ref[pl.ds(0, own_rows), pl.ds(width, speeds_ref.shape[1])] = speeds_ref[...]
    table_ref[pl.ds(own_rows, recv_ref.shape[0]), :] = recv_ref[...]

    def body(i, carry):
        base = pl.multiple_of(i * 32, 32)
        for j in range(32):
            row = idx_ref[base + j]
            outer_ref[pl.ds(base + j, 1), :] = table_ref[pl.ds(row, 1), :]
        return carry

    lax.fori_loop(0, own_rows // 32, body, 0)
    chunk = 1024
    spread = spread_ref[...]

    def rows(c, carry):
        start = pl.multiple_of(c * chunk, chunk)
        own = table_ref[pl.ds(start, chunk), :]
        other = outer_ref[pl.ds(start, chunk), :]
        own_speed = _exact_spread(own, spread)
        outer_speed = _exact_spread(other, spread)
        own_vals = own[:, :width]
        outer_vals = other[:, :width]
        normal = 0.5 * (own_speed - outer_speed)
        common = 0.5 * normal * (own_vals + outer_vals) + 0.5 * jnp.abs(normal) * (own_vals - outer_vals)
        jump_ref[pl.ds(start, chunk), :] = common - own_speed * own_vals
        return carry

    lax.fori_loop(0, own_rows // chunk, rows, 0)


def jump_rows(values, speeds, received, idx):
    rows = values.shape[0] + received.shape[0]
    full = received.shape[1]
    width = values.shape[1]
    nvars = width // speeds.shape[1]
    spread = np.zeros((full, width))
    for c in range(width):
        spread[width + c // nvars, c] = 1.0
    return pl.pallas_call(
        _jump_kernel,
        out_shape=jax.ShapeDtypeStruct((idx.shape[0], width), values.dtype),
        in_specs=[pl.BlockSpec(memory_space=pltpu.SMEM)]
        + [pl.BlockSpec(memory_space=pltpu.VMEM)] * 4,
        out_specs=pl.BlockSpec(memory_space=pltpu.VMEM),
        scratch_shapes=[
            pltpu.VMEM((rows, full), values.dtype),
            pltpu.VMEM((idx.shape[0], full), values.dtype),
        ],
        cost_estimate=pl.CostEstimate(
            flops=12 * idx.shape[0] * full * width,
            transcendentals=0,
            bytes_accessed=(3 * idx.shape[0] + rows) * full * 4,
        ),
    )(idx, values, speeds, received, jnp.asarray(spread, jnp.bfloat16))


def owner_ranks(owners, buckets):
    receptors = owners.shape[0]
    width = 128
    blocks = receptors // width
    member = owners[None, :] == jnp.arange(buckets, dtype=jnp.int32)[:, None]
    member = member.astype(jnp.bfloat16).reshape(buckets * blocks, width)
    upper = jnp.asarray(np.triu(np.ones((width, width))), jnp.bfloat16)
    inside = jnp.dot(member, upper, preferred_element_type=jnp.float32)
    inside = inside.reshape(buckets, blocks, width)
    totals = inside[:, :, width - 1].astype(jnp.bfloat16)
    strict = jnp.asarray(np.triu(np.ones((blocks, blocks)), 1), jnp.bfloat16)
    offsets = jnp.dot(totals, strict, preferred_element_type=jnp.float32)
    counts = (inside + offsets[:, :, None]).reshape(buckets, receptors)
    picked = jnp.sum(jnp.where(member.reshape(buckets, receptors) > 0, counts, 0.0), axis=0)
    return picked.astype(jnp.int32) - 1


def surface_term(values, speeds, links, received, lifting, elems):
    nvars = received.shape[1] // 16 - 1
    jump_term = jump_rows(values, speeds, received, links).reshape(6, elems, 16, nvars)
    lift_faces = lifting.reshape(64, 16, 6)
    return jnp.einsum("pqf,feqv->vpe", lift_faces, jump_term, precision=lax.Precision.HIGHEST)


def volume_term(solution, velocity, derivative):
    slopes = jnp.einsum("dpq,vqe->dvpe", derivative, solution, precision=lax.Precision.HIGHEST)
    return jnp.sum(velocity[:, None, None, :] * slopes, axis=0)


def _pick_row(basis, first, index):
    out = basis[first : first + 1]
    for i in range(1, 4):
        out = jnp.where(index == i, basis[first + i : first + i + 1], out)
    return out


def _interp_kernel(rows_ref, donors_ref, basis_ref, out_ref):
    elems = rows_ref.shape[1]
    tile = donors_ref.shape[1]
    half = rows_ref.shape[0] // 2
    onehot = lax.broadcasted_iota(jnp.int32, (elems, tile), 0) == donors_ref[...]
    picked = jnp.dot(rows_ref[...], onehot.astype(jnp.bfloat16), preferred_element_type=jnp.float32)
    picked = picked[:half] + picked[half:]
    nvars = out_ref.shape[0]
    points = half // nvars
    basis = basis_ref[...]
    point = lax.broadcasted_iota(jnp.int32, (points, tile), 0)
    weights = (
        _pick_row(basis, 0, point // 16)
        * _pick_row(basis, 4, point // 4 % 4)
        * _pick_row(basis, 8, point % 4)
    )
    picked = picked.reshape(nvars, points, tile) * weights[None]
    out_ref[...] = jnp.sum(picked, axis=1)


def receptor_rows(advanced, donors, coords):
    nvars = advanced.shape[0]
    elems = advanced.shape[2]
    receptors = donors.shape[0]
    basis = jnp.concatenate([jnp.stack(lagrange_at(coords[d])) for d in range(3)], axis=0)
    hi, lo = split_bf16(advanced.reshape(nvars * 64, elems))
    rows = jnp.concatenate([hi, lo], axis=0)
    tile = 2048
    return pl.pallas_call(
        _interp_kernel,
        out_shape=jax.ShapeDtypeStruct((nvars, receptors), jnp.float32),
        grid=(receptors // tile,),
        in_specs=[
            pl.BlockSpec((2 * nvars * 64, elems), lambda i: (0, 0)),
            pl.BlockSpec((1, tile), lambda i: (0, i)),
            pl.BlockSpec((12, tile), lambda i: (0, i)),
        ],
        out_specs=pl.BlockSpec((nvars, tile), lambda i: (0, i)),
        cost_estimate=pl.CostEstimate(
            flops=2 * 2 * nvars * 64 * elems * receptors,
            transcendentals=0,
            bytes_accessed=2 * nvars * 64 * elems * 2 + receptors * (1 + 12 + nvars) * 4,
        ),
    )(rows, donors.reshape(1, receptors), basis)


def on_device(
    solution, velocity, inv_jacobian, face_speed, face_link, donor_elem, ref_coords, owner_list
):
    extrapolate, derivative, lifting = tables()
    nvars = solution.shape[0]
    elems = solution.shape[2]
    rim_count = elems // 16
    faces_total = 6 * elems
    links = face_link.reshape(faces_total)
    values, speeds = face_rows(solution, face_speed, extrapolate)
    flat_values = values.reshape(faces_total, 16 * nvars)
    outgoing = rim_rows(flat_values, speeds, links, faces_total, rim_count)
    extended = padded(outgoing, (("valve", 0),), rim_count)
    received = jnp.concatenate([extended[:rim_count], extended[3 * rim_count :]], axis=0)
    surface = surface_term(flat_values, speeds, links, received, lifting, elems)
    volume = volume_term(solution, velocity, derivative)
    section_rate = -inv_jacobian[None] * (volume + surface)
    advanced = solution + section_step * section_rate
    receptor_vals = receptor_rows(advanced, donor_elem, ref_coords)
    buckets = lax.axis_size("bulk")
    receptors = receptor_vals.shape[1]
    capacity = 2 * receptors // buckets
    owners = owner_list[:, 0]
    ranks = owner_ranks(owners, buckets)
    copies = jnp.asarray(np.tile(np.eye(nvars), (1, buckets)), jnp.float32)
    spread = lax.dot_general(
        receptor_vals, copies, (((0,), (0,)), ((), ())), precision=lax.Precision.HIGHEST
    )
    column_owner = jnp.arange(buckets * nvars, dtype=jnp.int32) // nvars
    masked = jnp.where(owners[:, None] == column_owner[None, :], spread, 0.0)
    hi, lo = split_bf16(masked)
    by_rank = (jnp.arange(capacity, dtype=jnp.int32)[:, None] == ranks[None, :]).astype(jnp.bfloat16)
    both = jnp.dot(by_rank, jnp.concatenate([hi, lo], axis=1), preferred_element_type=jnp.float32)
    placed = both[:, : buckets * nvars] + both[:, buckets * nvars :]
    send = jnp.transpose(placed.reshape(capacity, buckets, nvars), (1, 2, 0))
    got = lax.all_to_all(send, "bulk", 0, 0, tiled=True)
    fringe = jnp.transpose(got, (1, 0, 2)).reshape(nvars, buckets * capacity)
    return (section_rate, fringe)


def solution(mesh):
    placed = (
        P(None, None, ("valve", "bulk")),
        P(None, ("valve", "bulk")),
        P(None, ("valve", "bulk")),
        P(None, ("valve", "bulk")),
        P(None, ("valve", "bulk")),
        P(("valve", "bulk")),
        P(None, ("valve", "bulk")),
        P(("valve", "bulk"), None),
    )
    return jax.shard_map(
        on_device,
        mesh=mesh,
        in_specs=placed,
        out_specs=(P(None, None, ("valve", "bulk")), P(None, ("valve", "bulk"))),
        check_vma=False,
    )
```

```python
import jax
import jax.numpy as jnp
import numpy as np
from jax import lax
from jax.sharding import PartitionSpec as P
from jax.experimental import pallas as pl
from jax.experimental.pallas import tpu as pltpu

gauss_nodes = (-0.8611363115940526, -0.3399810435848563, 0.3399810435848563, 0.8611363115940526)
quad_weights = (0.3478548451374538, 0.6521451548625461, 0.6521451548625461, 0.3478548451374538)
section_step = 0.2


def padded(shard, sides, width):
    for axis, dim in sides:
        size, length = (lax.axis_size(axis), shard.shape[dim])
        up = [(i, (i + 1) % size) for i in range(size)]
        down = [(j, i) for i, j in up]
        last = lax.slice_in_dim(shard, length - width, length, axis=dim)
        initial = lax.slice_in_dim(shard, 0, width, axis=dim)
        before = lax.ppermute(last, axis, up)
        after = lax.ppermute(initial, axis, down)
        shard = jnp.concatenate([before, shard, after], axis=dim)
    return shard


def lagrange_at(x):
    values = []
    for j in range(4):
        factor = 1.0
        for m in range(4):
            if m != j:
                factor = factor * (x - gauss_nodes[m]) / (gauss_nodes[j] - gauss_nodes[m])
        values.append(factor)
    return values


def tables():
    slopes = np.zeros((4, 4))
    for i in range(4):
        for j in range(4):
            summed = 0.0
            for m in range(4):
                if m != j:
                    product = 1.0 / (gauss_nodes[j] - gauss_nodes[m])
                    for n in range(4):
                        if n != j and n != m:
                            product = (
                                product
                                * (gauss_nodes[i] - gauss_nodes[n])
                                / (gauss_nodes[j] - gauss_nodes[n])
                            )
                    summed = summed + product
            slopes[i, j] = summed
    end_values = [lagrange_at(-1.0), lagrange_at(1.0)]
    extrapolate = np.zeros((96, 64))
    lifting = np.zeros((64, 96))
    derivative = np.zeros((3, 64, 64))
    for p in range(64):
        point_idx = (p // 16, p // 4 % 4, p % 4)
        for f in range(6):
            normal_dir = f // 2
            across = [t for t in range(3) if t != normal_dir]
            q = point_idx[across[0]] * 4 + point_idx[across[1]]
            flux_row = q * 6 + f
            extrapolate[flux_row, p] = end_values[f % 2][point_idx[normal_dir]]
            lifting[p, flux_row] = (
                end_values[f % 2][point_idx[normal_dir]] / quad_weights[point_idx[normal_dir]]
            )
        for s in range(64):
            other_idx = (s // 16, s // 4 % 4, s % 4)
            for normal_dir in range(3):
                if all((point_idx[t] == other_idx[t] for t in range(3) if t != normal_dir)):
                    derivative[normal_dir, p, s] = slopes[
                        point_idx[normal_dir], other_idx[normal_dir]
                    ]
    return (
        jnp.asarray(extrapolate, dtype=jnp.float32),
        jnp.asarray(derivative, dtype=jnp.float32),
        jnp.asarray(lifting, dtype=jnp.float32),
    )


def face_rows(solution, face_speed, extrapolate):
    nvars = solution.shape[0]
    elems = solution.shape[2]
    ext_faces = extrapolate.reshape(16, 6, 64)
    values = jnp.einsum("qfp,vpe->feqv", ext_faces, solution, precision=lax.Precision.HIGHEST)
    values = values.reshape(6 * elems, 16, nvars)
    speeds = jnp.transpose(face_speed.reshape(16, 6, elems), (1, 2, 0)).reshape(6 * elems, 16)
    return (values, speeds)


def rim_rows(values, speeds, links, faces_total, rim_count):
    wanted = faces_total + jnp.arange(2 * rim_count, dtype=jnp.int32)
    hits = links[None, :] == wanted[:, None]
    faces = jnp.arange(faces_total, dtype=jnp.int32)[None, :]
    senders = jnp.sum(jnp.where(hits, faces, 0), axis=1)
    return jnp.concatenate(
        [jnp.take(values, senders, axis=0), jnp.take(speeds, senders, axis=0)], axis=1
    )


def split_bf16(x):
    hi = lax.reduce_precision(x, exponent_bits=8, mantissa_bits=7)
    return hi.astype(jnp.bfloat16), (x - hi).astype(jnp.bfloat16)


def pick_dot(rows, onehot):
    hi, lo = split_bf16(rows)
    both = jnp.dot(jnp.concatenate([hi, lo], axis=0), onehot, preferred_element_type=jnp.float32)
    return both[: rows.shape[0]] + both[rows.shape[0] :]


def _exact_spread(x, spread):
    hi = x.astype(jnp.bfloat16)
    rest = x - hi.astype(jnp.float32)
    mid = rest.astype(jnp.bfloat16)
    lo = (rest - mid.astype(jnp.float32)).astype(jnp.bfloat16)
    out = jnp.dot(hi, spread, preferred_element_type=jnp.float32)
    out = out + jnp.dot(mid, spread, preferred_element_type=jnp.float32)
    return out + jnp.dot(lo, spread, preferred_element_type=jnp.float32)


def _jump_kernel(idx_ref, values_ref, speeds_ref, recv_ref, spread_ref, jump_ref, table_ref, outer_ref):
    own_rows, width = values_ref.shape
    table_ref[pl.ds(0, own_rows), pl.ds(0, width)] = values_ref[...]
    table_ref[pl.ds(0, own_rows), pl.ds(width, speeds_ref.shape[1])] = speeds_ref[...]
    table_ref[pl.ds(own_rows, recv_ref.shape[0]), :] = recv_ref[...]

    def body(i, carry):
        base = pl.multiple_of(i * 64, 64)
        for j in range(64):
            row = idx_ref[base + j]
            outer_ref[pl.ds(base + j, 1), :] = table_ref[pl.ds(row, 1), :]
        return carry

    lax.fori_loop(0, own_rows // 64, body, 0)
    chunk = 2048
    spread = spread_ref[...]

    def rows(c, carry):
        start = pl.multiple_of(c * chunk, chunk)
        own = table_ref[pl.ds(start, chunk), :]
        other = outer_ref[pl.ds(start, chunk), :]
        own_speed = _exact_spread(own, spread)
        outer_speed = _exact_spread(other, spread)
        own_vals = own[:, :width]
        outer_vals = other[:, :width]
        normal = 0.5 * (own_speed - outer_speed)
        common = 0.5 * normal * (own_vals + outer_vals) + 0.5 * jnp.abs(normal) * (own_vals - outer_vals)
        jump_ref[pl.ds(start, chunk), :] = common - own_speed * own_vals
        return carry

    lax.fori_loop(0, own_rows // chunk, rows, 0)


def jump_rows(values, speeds, received, idx):
    rows = values.shape[0] + received.shape[0]
    full = received.shape[1]
    width = values.shape[1]
    nvars = width // speeds.shape[1]
    spread = np.zeros((full, width))
    for c in range(width):
        spread[width + c // nvars, c] = 1.0
    return pl.pallas_call(
        _jump_kernel,
        out_shape=jax.ShapeDtypeStruct((idx.shape[0], width), values.dtype),
        in_specs=[pl.BlockSpec(memory_space=pltpu.SMEM)]
        + [pl.BlockSpec(memory_space=pltpu.VMEM)] * 4,
        out_specs=pl.BlockSpec(memory_space=pltpu.VMEM),
        scratch_shapes=[
            pltpu.VMEM((rows, full), values.dtype),
            pltpu.VMEM((idx.shape[0], full), values.dtype),
        ],
        cost_estimate=pl.CostEstimate(
            flops=12 * idx.shape[0] * full * width,
            transcendentals=0,
            bytes_accessed=(3 * idx.shape[0] + rows) * full * 4,
        ),
    )(idx, values, speeds, received, jnp.asarray(spread, jnp.bfloat16))


def owner_ranks(owners, buckets):
    receptors = owners.shape[0]
    width = 128
    blocks = receptors // width
    member = owners[None, :] == jnp.arange(buckets, dtype=jnp.int32)[:, None]
    member = member.astype(jnp.bfloat16).reshape(buckets * blocks, width)
    upper = jnp.asarray(np.triu(np.ones((width, width))), jnp.bfloat16)
    inside = jnp.dot(member, upper, preferred_element_type=jnp.float32)
    inside = inside.reshape(buckets, blocks, width)
    totals = inside[:, :, width - 1].astype(jnp.bfloat16)
    strict = jnp.asarray(np.triu(np.ones((blocks, blocks)), 1), jnp.bfloat16)
    offsets = jnp.dot(totals, strict, preferred_element_type=jnp.float32)
    counts = (inside + offsets[:, :, None]).reshape(buckets, receptors)
    picked = jnp.sum(jnp.where(member.reshape(buckets, receptors) > 0, counts, 0.0), axis=0)
    return picked.astype(jnp.int32) - 1


def surface_term(values, speeds, links, received, lifting, elems):
    nvars = received.shape[1] // 16 - 1
    jump_term = jump_rows(values, speeds, received, links).reshape(6, elems, 16, nvars)
    lift_faces = lifting.reshape(64, 16, 6)
    return jnp.einsum("pqf,feqv->vpe", lift_faces, jump_term, precision=lax.Precision.HIGHEST)


def volume_term(solution, velocity, derivative):
    slopes = jnp.einsum("dpq,vqe->dvpe", derivative, solution, precision=lax.Precision.HIGHEST)
    return jnp.sum(velocity[:, None, None, :] * slopes, axis=0)


def _pick_row(basis, first, index):
    out = basis[first : first + 1]
    for i in range(1, 4):
        out = jnp.where(index == i, basis[first + i : first + i + 1], out)
    return out


def _interp_kernel(rows_ref, donors_ref, basis_ref, out_ref):
    elems = rows_ref.shape[1]
    tile = donors_ref.shape[1]
    half = rows_ref.shape[0] // 2
    onehot = lax.broadcasted_iota(jnp.int32, (elems, tile), 0) == donors_ref[...]
    picked = jnp.dot(rows_ref[...], onehot.astype(jnp.bfloat16), preferred_element_type=jnp.float32)
    picked = picked[:half] + picked[half:]
    nvars = out_ref.shape[0]
    points = half // nvars
    basis = basis_ref[...]
    point = lax.broadcasted_iota(jnp.int32, (points, tile), 0)
    weights = (
        _pick_row(basis, 0, point // 16)
        * _pick_row(basis, 4, point // 4 % 4)
        * _pick_row(basis, 8, point % 4)
    )
    picked = picked.reshape(nvars, points, tile) * weights[None]
    out_ref[...] = jnp.sum(picked, axis=1)


def receptor_rows(advanced, donors, coords):
    nvars = advanced.shape[0]
    elems = advanced.shape[2]
    receptors = donors.shape[0]
    basis = jnp.concatenate([jnp.stack(lagrange_at(coords[d])) for d in range(3)], axis=0)
    hi, lo = split_bf16(advanced.reshape(nvars * 64, elems))
    rows = jnp.concatenate([hi, lo], axis=0)
    tile = 2048
    return pl.pallas_call(
        _interp_kernel,
        out_shape=jax.ShapeDtypeStruct((nvars, receptors), jnp.float32),
        grid=(receptors // tile,),
        in_specs=[
            pl.BlockSpec((2 * nvars * 64, elems), lambda i: (0, 0)),
            pl.BlockSpec((1, tile), lambda i: (0, i)),
            pl.BlockSpec((12, tile), lambda i: (0, i)),
        ],
        out_specs=pl.BlockSpec((nvars, tile), lambda i: (0, i)),
        cost_estimate=pl.CostEstimate(
            flops=2 * 2 * nvars * 64 * elems * receptors,
            transcendentals=0,
            bytes_accessed=2 * nvars * 64 * elems * 2 + receptors * (1 + 12 + nvars) * 4,
        ),
    )(rows, donors.reshape(1, receptors), basis)


def on_device(
    solution, velocity, inv_jacobian, face_speed, face_link, donor_elem, ref_coords, owner_list
):
    extrapolate, derivative, lifting = tables()
    nvars = solution.shape[0]
    elems = solution.shape[2]
    rim_count = elems // 16
    faces_total = 6 * elems
    links = face_link.reshape(faces_total)
    values, speeds = face_rows(solution, face_speed, extrapolate)
    flat_values = values.reshape(faces_total, 16 * nvars)
    outgoing = rim_rows(flat_values, speeds, links, faces_total, rim_count)
    extended = padded(outgoing, (("valve", 0),), rim_count)
    received = jnp.concatenate([extended[:rim_count], extended[3 * rim_count :]], axis=0)
    surface = surface_term(flat_values, speeds, links, received, lifting, elems)
    volume = volume_term(solution, velocity, derivative)
    section_rate = -inv_jacobian[None] * (volume + surface)
    advanced = solution + section_step * section_rate
    receptor_vals = receptor_rows(advanced, donor_elem, ref_coords)
    buckets = lax.axis_size("bulk")
    receptors = receptor_vals.shape[1]
    capacity = 2 * receptors // buckets
    owners = owner_list[:, 0]
    ranks = owner_ranks(owners, buckets)
    copies = jnp.asarray(np.tile(np.eye(nvars), (1, buckets)), jnp.float32)
    spread = lax.dot_general(
        receptor_vals, copies, (((0,), (0,)), ((), ())), precision=lax.Precision.HIGHEST
    )
    column_owner = jnp.arange(buckets * nvars, dtype=jnp.int32) // nvars
    masked = jnp.where(owners[:, None] == column_owner[None, :], spread, 0.0)
    hi, lo = split_bf16(masked)
    by_rank = (jnp.arange(capacity, dtype=jnp.int32)[:, None] == ranks[None, :]).astype(jnp.bfloat16)
    both = jnp.dot(by_rank, jnp.concatenate([hi, lo], axis=1), preferred_element_type=jnp.float32)
    placed = both[:, : buckets * nvars] + both[:, buckets * nvars :]
    send = jnp.transpose(placed.reshape(capacity, buckets, nvars), (1, 2, 0))
    got = lax.all_to_all(send, "bulk", 0, 0, tiled=True)
    fringe = jnp.transpose(got, (1, 0, 2)).reshape(nvars, buckets * capacity)
    return (section_rate, fringe)


def solution(mesh):
    placed = (
        P(None, None, ("valve", "bulk")),
        P(None, ("valve", "bulk")),
        P(None, ("valve", "bulk")),
        P(None, ("valve", "bulk")),
        P(None, ("valve", "bulk")),
        P(("valve", "bulk")),
        P(None, ("valve", "bulk")),
        P(("valve", "bulk"), None),
    )
    return jax.shard_map(
        on_device,
        mesh=mesh,
        in_specs=placed,
        out_specs=(P(None, None, ("valve", "bulk")), P(None, ("valve", "bulk"))),
        check_vma=False,
    )
```

```python
import jax
import jax.numpy as jnp
import numpy as np
from jax import lax
from jax.sharding import PartitionSpec as P
from jax.experimental import pallas as pl
from jax.experimental.pallas import tpu as pltpu

gauss_nodes = (-0.8611363115940526, -0.3399810435848563, 0.3399810435848563, 0.8611363115940526)
quad_weights = (0.3478548451374538, 0.6521451548625461, 0.6521451548625461, 0.3478548451374538)
section_step = 0.2


def padded(shard, sides, width):
    for axis, dim in sides:
        size, length = (lax.axis_size(axis), shard.shape[dim])
        up = [(i, (i + 1) % size) for i in range(size)]
        down = [(j, i) for i, j in up]
        last = lax.slice_in_dim(shard, length - width, length, axis=dim)
        initial = lax.slice_in_dim(shard, 0, width, axis=dim)
        before = lax.ppermute(last, axis, up)
        after = lax.ppermute(initial, axis, down)
        shard = jnp.concatenate([before, shard, after], axis=dim)
    return shard


def lagrange_at(x):
    values = []
    for j in range(4):
        factor = 1.0
        for m in range(4):
            if m != j:
                factor = factor * (x - gauss_nodes[m]) / (gauss_nodes[j] - gauss_nodes[m])
        values.append(factor)
    return values


def tables():
    slopes = np.zeros((4, 4))
    for i in range(4):
        for j in range(4):
            summed = 0.0
            for m in range(4):
                if m != j:
                    product = 1.0 / (gauss_nodes[j] - gauss_nodes[m])
                    for n in range(4):
                        if n != j and n != m:
                            product = (
                                product
                                * (gauss_nodes[i] - gauss_nodes[n])
                                / (gauss_nodes[j] - gauss_nodes[n])
                            )
                    summed = summed + product
            slopes[i, j] = summed
    end_values = [lagrange_at(-1.0), lagrange_at(1.0)]
    extrapolate = np.zeros((96, 64))
    lifting = np.zeros((64, 96))
    derivative = np.zeros((3, 64, 64))
    for p in range(64):
        point_idx = (p // 16, p // 4 % 4, p % 4)
        for f in range(6):
            normal_dir = f // 2
            across = [t for t in range(3) if t != normal_dir]
            q = point_idx[across[0]] * 4 + point_idx[across[1]]
            flux_row = q * 6 + f
            extrapolate[flux_row, p] = end_values[f % 2][point_idx[normal_dir]]
            lifting[p, flux_row] = (
                end_values[f % 2][point_idx[normal_dir]] / quad_weights[point_idx[normal_dir]]
            )
        for s in range(64):
            other_idx = (s // 16, s // 4 % 4, s % 4)
            for normal_dir in range(3):
                if all((point_idx[t] == other_idx[t] for t in range(3) if t != normal_dir)):
                    derivative[normal_dir, p, s] = slopes[
                        point_idx[normal_dir], other_idx[normal_dir]
                    ]
    return (
        jnp.asarray(extrapolate, dtype=jnp.float32),
        jnp.asarray(derivative, dtype=jnp.float32),
        jnp.asarray(lifting, dtype=jnp.float32),
    )


def face_rows(solution, face_speed, extrapolate):
    nvars = solution.shape[0]
    elems = solution.shape[2]
    ext_faces = extrapolate.reshape(16, 6, 64)
    values = jnp.einsum("qfp,vpe->feqv", ext_faces, solution, precision=lax.Precision.HIGHEST)
    values = values.reshape(6 * elems, 16, nvars)
    speeds = jnp.transpose(face_speed.reshape(16, 6, elems), (1, 2, 0)).reshape(6 * elems, 16)
    return (values, speeds)


def rim_rows(values, speeds, links, faces_total, rim_count):
    wanted = faces_total + jnp.arange(2 * rim_count, dtype=jnp.int32)
    hits = links[None, :] == wanted[:, None]
    faces = jnp.arange(faces_total, dtype=jnp.int32)[None, :]
    senders = jnp.sum(jnp.where(hits, faces, 0), axis=1)
    return jnp.concatenate(
        [jnp.take(values, senders, axis=0), jnp.take(speeds, senders, axis=0)], axis=1
    )


def split_bf16(x):
    hi = lax.reduce_precision(x, exponent_bits=8, mantissa_bits=7)
    return hi.astype(jnp.bfloat16), (x - hi).astype(jnp.bfloat16)


def pick_dot(rows, onehot):
    hi, lo = split_bf16(rows)
    both = jnp.dot(jnp.concatenate([hi, lo], axis=0), onehot, preferred_element_type=jnp.float32)
    return both[: rows.shape[0]] + both[rows.shape[0] :]


def _exact_spread(x, spread):
    hi = x.astype(jnp.bfloat16)
    rest = x - hi.astype(jnp.float32)
    mid = rest.astype(jnp.bfloat16)
    lo = (rest - mid.astype(jnp.float32)).astype(jnp.bfloat16)
    out = jnp.dot(hi, spread, preferred_element_type=jnp.float32)
    out = out + jnp.dot(mid, spread, preferred_element_type=jnp.float32)
    return out + jnp.dot(lo, spread, preferred_element_type=jnp.float32)


def _jump_kernel(idx_ref, values_ref, speeds_ref, recv_ref, spread_ref, jump_ref, table_ref, outer_ref):
    own_rows, width = values_ref.shape
    table_ref[pl.ds(0, own_rows), pl.ds(0, width)] = values_ref[...]
    table_ref[pl.ds(0, own_rows), pl.ds(width, speeds_ref.shape[1])] = speeds_ref[...]
    table_ref[pl.ds(own_rows, recv_ref.shape[0]), :] = recv_ref[...]

    def body(i, carry):
        base = pl.multiple_of(i * 128, 128)
        for j in range(128):
            row = idx_ref[base + j]
            outer_ref[pl.ds(base + j, 1), :] = table_ref[pl.ds(row, 1), :]
        return carry

    lax.fori_loop(0, own_rows // 128, body, 0)
    chunk = 3072
    spread = spread_ref[...]

    def rows(c, carry):
        start = pl.multiple_of(c * chunk, chunk)
        own = table_ref[pl.ds(start, chunk), :]
        other = outer_ref[pl.ds(start, chunk), :]
        own_speed = _exact_spread(own, spread)
        outer_speed = _exact_spread(other, spread)
        own_vals = own[:, :width]
        outer_vals = other[:, :width]
        normal = 0.5 * (own_speed - outer_speed)
        common = 0.5 * normal * (own_vals + outer_vals) + 0.5 * jnp.abs(normal) * (own_vals - outer_vals)
        jump_ref[pl.ds(start, chunk), :] = common - own_speed * own_vals
        return carry

    lax.fori_loop(0, own_rows // chunk, rows, 0)


def jump_rows(values, speeds, received, idx):
    rows = values.shape[0] + received.shape[0]
    full = received.shape[1]
    width = values.shape[1]
    nvars = width // speeds.shape[1]
    spread = np.zeros((full, width))
    for c in range(width):
        spread[width + c // nvars, c] = 1.0
    return pl.pallas_call(
        _jump_kernel,
        out_shape=jax.ShapeDtypeStruct((idx.shape[0], width), values.dtype),
        in_specs=[pl.BlockSpec(memory_space=pltpu.SMEM)]
        + [pl.BlockSpec(memory_space=pltpu.VMEM)] * 4,
        out_specs=pl.BlockSpec(memory_space=pltpu.VMEM),
        scratch_shapes=[
            pltpu.VMEM((rows, full), values.dtype),
            pltpu.VMEM((idx.shape[0], full), values.dtype),
        ],
        cost_estimate=pl.CostEstimate(
            flops=12 * idx.shape[0] * full * width,
            transcendentals=0,
            bytes_accessed=(3 * idx.shape[0] + rows) * full * 4,
        ),
    )(idx, values, speeds, received, jnp.asarray(spread, jnp.bfloat16))


def owner_ranks(owners, buckets):
    receptors = owners.shape[0]
    width = 128
    blocks = receptors // width
    member = owners[None, :] == jnp.arange(buckets, dtype=jnp.int32)[:, None]
    member = member.astype(jnp.bfloat16).reshape(buckets * blocks, width)
    upper = jnp.asarray(np.triu(np.ones((width, width))), jnp.bfloat16)
    inside = jnp.dot(member, upper, preferred_element_type=jnp.float32)
    inside = inside.reshape(buckets, blocks, width)
    totals = inside[:, :, width - 1].astype(jnp.bfloat16)
    strict = jnp.asarray(np.triu(np.ones((blocks, blocks)), 1), jnp.bfloat16)
    offsets = jnp.dot(totals, strict, preferred_element_type=jnp.float32)
    counts = (inside + offsets[:, :, None]).reshape(buckets, receptors)
    picked = jnp.sum(jnp.where(member.reshape(buckets, receptors) > 0, counts, 0.0), axis=0)
    return picked.astype(jnp.int32) - 1


def surface_term(values, speeds, links, received, lifting, elems):
    nvars = received.shape[1] // 16 - 1
    jump_term = jump_rows(values, speeds, received, links).reshape(6, elems, 16, nvars)
    lift_faces = lifting.reshape(64, 16, 6)
    return jnp.einsum("pqf,feqv->vpe", lift_faces, jump_term, precision=lax.Precision.HIGHEST)


def volume_term(solution, velocity, derivative):
    slopes = jnp.einsum("dpq,vqe->dvpe", derivative, solution, precision=lax.Precision.HIGHEST)
    return jnp.sum(velocity[:, None, None, :] * slopes, axis=0)


def _pick_row(basis, first, index):
    out = basis[first : first + 1]
    for i in range(1, 4):
        out = jnp.where(index == i, basis[first + i : first + i + 1], out)
    return out


def _interp_kernel(rows_ref, donors_ref, basis_ref, out_ref):
    elems = rows_ref.shape[1]
    tile = donors_ref.shape[1]
    half = rows_ref.shape[0] // 2
    onehot = lax.broadcasted_iota(jnp.int32, (elems, tile), 0) == donors_ref[...]
    picked = jnp.dot(rows_ref[...], onehot.astype(jnp.bfloat16), preferred_element_type=jnp.float32)
    picked = picked[:half] + picked[half:]
    nvars = out_ref.shape[0]
    points = half // nvars
    basis = basis_ref[...]
    point = lax.broadcasted_iota(jnp.int32, (points, tile), 0)
    weights = (
        _pick_row(basis, 0, point // 16)
        * _pick_row(basis, 4, point // 4 % 4)
        * _pick_row(basis, 8, point % 4)
    )
    picked = picked.reshape(nvars, points, tile) * weights[None]
    out_ref[...] = jnp.sum(picked, axis=1)


def receptor_rows(advanced, donors, coords):
    nvars = advanced.shape[0]
    elems = advanced.shape[2]
    receptors = donors.shape[0]
    basis = jnp.concatenate([jnp.stack(lagrange_at(coords[d])) for d in range(3)], axis=0)
    hi, lo = split_bf16(advanced.reshape(nvars * 64, elems))
    rows = jnp.concatenate([hi, lo], axis=0)
    tile = 2048
    return pl.pallas_call(
        _interp_kernel,
        out_shape=jax.ShapeDtypeStruct((nvars, receptors), jnp.float32),
        grid=(receptors // tile,),
        in_specs=[
            pl.BlockSpec((2 * nvars * 64, elems), lambda i: (0, 0)),
            pl.BlockSpec((1, tile), lambda i: (0, i)),
            pl.BlockSpec((12, tile), lambda i: (0, i)),
        ],
        out_specs=pl.BlockSpec((nvars, tile), lambda i: (0, i)),
        cost_estimate=pl.CostEstimate(
            flops=2 * 2 * nvars * 64 * elems * receptors,
            transcendentals=0,
            bytes_accessed=2 * nvars * 64 * elems * 2 + receptors * (1 + 12 + nvars) * 4,
        ),
    )(rows, donors.reshape(1, receptors), basis)


def on_device(
    solution, velocity, inv_jacobian, face_speed, face_link, donor_elem, ref_coords, owner_list
):
    extrapolate, derivative, lifting = tables()
    nvars = solution.shape[0]
    elems = solution.shape[2]
    rim_count = elems // 16
    faces_total = 6 * elems
    links = face_link.reshape(faces_total)
    values, speeds = face_rows(solution, face_speed, extrapolate)
    flat_values = values.reshape(faces_total, 16 * nvars)
    outgoing = rim_rows(flat_values, speeds, links, faces_total, rim_count)
    extended = padded(outgoing, (("valve", 0),), rim_count)
    received = jnp.concatenate([extended[:rim_count], extended[3 * rim_count :]], axis=0)
    surface = surface_term(flat_values, speeds, links, received, lifting, elems)
    volume = volume_term(solution, velocity, derivative)
    section_rate = -inv_jacobian[None] * (volume + surface)
    advanced = solution + section_step * section_rate
    receptor_vals = receptor_rows(advanced, donor_elem, ref_coords)
    buckets = lax.axis_size("bulk")
    receptors = receptor_vals.shape[1]
    capacity = 2 * receptors // buckets
    owners = owner_list[:, 0]
    ranks = owner_ranks(owners, buckets)
    copies = jnp.asarray(np.tile(np.eye(nvars), (1, buckets)), jnp.float32)
    spread = lax.dot_general(
        receptor_vals, copies, (((0,), (0,)), ((), ())), precision=lax.Precision.HIGHEST
    )
    column_owner = jnp.arange(buckets * nvars, dtype=jnp.int32) // nvars
    masked = jnp.where(owners[:, None] == column_owner[None, :], spread, 0.0)
    hi, lo = split_bf16(masked)
    by_rank = (jnp.arange(capacity, dtype=jnp.int32)[:, None] == ranks[None, :]).astype(jnp.bfloat16)
    both = jnp.dot(by_rank, jnp.concatenate([hi, lo], axis=1), preferred_element_type=jnp.float32)
    placed = both[:, : buckets * nvars] + both[:, buckets * nvars :]
    send = jnp.transpose(placed.reshape(capacity, buckets, nvars), (1, 2, 0))
    got = lax.all_to_all(send, "bulk", 0, 0, tiled=True)
    fringe = jnp.transpose(got, (1, 0, 2)).reshape(nvars, buckets * capacity)
    return (section_rate, fringe)


def solution(mesh):
    placed = (
        P(None, None, ("valve", "bulk")),
        P(None, ("valve", "bulk")),
        P(None, ("valve", "bulk")),
        P(None, ("valve", "bulk")),
        P(None, ("valve", "bulk")),
        P(("valve", "bulk")),
        P(None, ("valve", "bulk")),
        P(("valve", "bulk"), None),
    )
    return jax.shard_map(
        on_device,
        mesh=mesh,
        in_specs=placed,
        out_specs=(P(None, None, ("valve", "bulk")), P(None, ("valve", "bulk"))),
        check_vma=False,
    )
```
